256 devices in a mesh: row: 4 (over z_lo), col: 64 (over y, x, z_hi, core).
Axes of the slice: x: 4, y: 4, z: 8 (z_hi: 2, z_lo: 4; z = z_hi * 4 + z_lo), core: 2. Of those that a mesh axis runs over, the one named last changes fastest.
Arguments:
- iterate: float32 [256, 131072], P('row', 'col'), may hold values from -6 to 6
- residual: float32 [256, 131072], P('row', 'col'), may hold values from -24 to 24
- direction: float32 [256, 131072], P('row', 'col'), may hold values from -24 to 24
- window_weight: float32 [16, 8192], P('row', 'col'), may hold values from 0.2 to 5
- freq_weight: float32 [32, 32], replicated, may hold values from 0.2 to 5
Outputs:
- new_iterate: float32 [256, 131072], P('row', 'col')
- new_residual: float32 [256, 131072], P('row', 'col')
- new_direction: float32 [256, 131072], P('row', 'col')
The draws below stay inside these ranges and needn't reach their ends.
All inputs are finite; a program needn't handle non-finite values.
Results may differ from the reference program's by a relative error of at most 0.0003.
Values sent between devices are 32-bit elements; how exact they have to be, the bound alone decides.
No kernel may reach another device: no remote copies, remote signals or barrier semaphores. Data moves between devices by JAX's collectives and lax.ppermute only.
A program may use at most 64 MiB of HBM per device.

```python
import math
import jax
import jax.numpy as jnp
from jax import lax

CD = 2048
NR = 256
NC = 131072
N_COL = 64


def rising_field(key):
    column_pos = jnp.arange(NC, dtype=jnp.float32)
    column_ramp = 1.0 + 2.0 * column_pos / NC
    first_key = jax.random.fold_in(key, 0)
    entries = jnp.clip(jax.random.normal(first_key, (NR, NC), jnp.float32), -4.0, 4.0)
    return entries * column_ramp[None, :]


def draw_residual(key, part):
    return rising_field(jax.random.fold_in(key, 11))


def draw_direction(key, part):
    return rising_field(jax.random.fold_in(key, 23))


def level_of(key, dims, shards, smallest, largest):
    gain = 1.0
    for position, blocks in shards:
        steps = jax.random.uniform(jax.random.fold_in(jax.random.fold_in(key, 6), position), (blocks,), jnp.float32, smallest / len(shards), largest / len(shards))
        gain = gain * jnp.repeat(jnp.exp(steps), dims[position] // blocks).reshape((-1,) + (1,) * (len(dims) - 1 - position))
    return gain


def noise(stream_key, dims, scale, reach, shards=(), kind=jnp.bfloat16):
    drawn = jax.random.normal(stream_key, dims, jnp.float32) * scale
    if len(shards) > 0:
        drawn = level_of(stream_key, dims, shards, -0.22, 0.18) * drawn
    return jnp.clip(drawn, min=-reach, max=reach).astype(kind)


def setup_inputs(seed: int = 0) -> dict:
    keys = jax.random.split(jax.random.key(seed), 6)
    iterate = noise(keys[0], (NR, NC), 1.0, 6.0, ((0, 4), (1, 64)), jnp.float32)
    residual = draw_residual(jax.random.fold_in(keys[5], 71), 0)
    direction = draw_direction(jax.random.fold_in(keys[5], 71), 0)
    window_weight = jnp.clip(jnp.exp(math.log(5.0) - 3.218876 * jax.random.uniform(keys[3], (NR // 16, NC // 16), jnp.float32) ** level_of(keys[3], (NR // 16, NC // 16), ((0, 4), (1, 64)), -0.2, 0.2)), 0.2, 5.0)
    freq_weight = jnp.clip(jnp.exp(jax.random.uniform(keys[4], (32, 32), jnp.float32, math.log(0.2), math.log(5.0))), 0.2, 5.0)
    return {"iterate": iterate, "residual": residual, "direction": direction, "window_weight": window_weight, "freq_weight": freq_weight}


precise = lax.Precision.HIGHEST
damping = 0.5

def tables():
    positions = jnp.arange(32, dtype=jnp.float32)
    window = jnp.exp(-0.5 * ((positions - 15.5) / 8.0) ** 2)
    phases = 2.0 * jnp.pi * jnp.outer(positions, positions) / 32.0
    cos_part = jnp.cos(phases) * window[None, :] / jnp.sqrt(32.0)
    sin_part = -jnp.sin(phases) * window[None, :] / jnp.sqrt(32.0)
    column_table = jnp.concatenate([cos_part.T, sin_part.T], axis=1)
    cos_split = cos_part.reshape(32, 2, 16)
    sin_split = sin_part.reshape(32, 2, 16)
    upper = jnp.stack([cos_split, -sin_split], axis=-1)
    lower = jnp.stack([sin_split, cos_split], axis=-1)
    row_table = jnp.concatenate([upper, lower], axis=0).reshape(64, 64)
    return (column_table, row_table)

def analyze(region, column_table, row_table):
    win_rows = region.shape[0] // 16 - 1
    win_cols = region.shape[1] // 16 - 1
    blocks = region.reshape(win_rows + 1, 16, win_cols + 1, 16)
    section_one = jnp.einsum('akbl,lp->akpb', blocks[:, :, :win_cols], column_table[:16], precision=precise)
    section_one = section_one + jnp.einsum('akbl,lp->akpb', blocks[:, :, 1:], column_table[16:], precision=precise)
    section_one = section_one.reshape(win_rows + 1, 16, 2, 32, win_cols)
    paired = jnp.stack([section_one[:-1], section_one[1:]], axis=1).reshape(win_rows, 64, 32, win_cols)
    return jnp.einsum('tm,amvb->atvb', row_table, paired, precision=precise)

def weigh(coefficients, window_weight, freq_weight):
    doubled = jnp.concatenate([freq_weight, freq_weight], axis=0)
    return coefficients * doubled[None, :, :, None] * window_weight[:, None, None, :]

def synthesize(coefficients, column_table, row_table):
    win_rows = coefficients.shape[0]
    win_cols = coefficients.shape[3]
    spread = jnp.einsum('tm,atvb->amvb', row_table, coefficients, precision=precise)
    spread = spread.reshape(win_rows, 2, 16, 64, win_cols)
    stacked = jnp.pad(spread[:, 0], ((0, 1), (0, 0), (0, 0), (0, 0))) + jnp.pad(spread[:, 1], ((1, 0), (0, 0), (0, 0), (0, 0)))
    lower_piece = jnp.einsum('akpb,lp->akbl', stacked, column_table[:16], precision=precise)
    upper_piece = jnp.einsum('akpb,lp->akbl', stacked, column_table[16:], precision=precise)
    blocks = jnp.pad(lower_piece, ((0, 0), (0, 0), (0, 1), (0, 0))) + jnp.pad(upper_piece, ((0, 0), (0, 0), (1, 0), (0, 0)))
    return blocks.reshape(16 * (win_rows + 1), 16 * (win_cols + 1))

def apply_normal(vector, window_weight, freq_weight):
    column_table, row_table = tables()
    padded = jnp.pad(vector, ((0, 16), (0, 16)))

    def one_block(block_index):
        start = (block_index * CD).astype(jnp.int32)
        region = lax.dynamic_slice(padded, (jnp.int32(0), start), (NR + 16, CD + 16))
        weight_start = (block_index * (CD // 16)).astype(jnp.int32)
        weights_here = lax.dynamic_slice(window_weight, (jnp.int32(0), weight_start), (NR // 16, CD // 16))
        coefficients = weigh(analyze(region, column_table, row_table), weights_here, freq_weight)
        return synthesize(coefficients, column_table, row_table)
    pieces = lax.map(one_block, jnp.arange(N_COL, dtype=jnp.int32))
    main_part = pieces[:, :, :CD].transpose(1, 0, 2).reshape(NR + 16, NC)
    tail_rows = jnp.pad(pieces[:-1, :, CD:].transpose(1, 0, 2), ((0, 0), (1, 0), (0, CD - 16))).reshape(NR + 16, NC)
    return (main_part + tail_rows)[:NR] + damping * vector

def reference(iterate, residual, direction, window_weight, freq_weight):
    norm_now = jnp.sum(residual * residual)
    applied = apply_normal(direction, window_weight, freq_weight)
    curvature = jnp.sum(direction * applied)
    step_length = norm_now / curvature
    new_iterate = iterate + step_length * direction
    new_residual = residual - step_length * applied
    norm_next = jnp.sum(new_residual * new_residual)
    new_direction = new_residual + norm_next / norm_now * direction
    return (new_iterate, new_residual, new_direction)
```

```python
import jax
import jax.numpy as jnp
from jax import lax
from jax.sharding import Mesh
from jax.sharding import PartitionSpec as P

COL = ("col_0", "col_1", "col_2", "col_3")
DOUBLING = (
    ("col_3", 1),
    ("row", 1),
    ("row", 2),
    ("col_0", 1),
    ("col_0", 2),
    ("col_1", 1),
    ("col_1", 2),
    ("col_2", 1),
)


precise = lax.Precision.HIGHEST
damping = 0.5


def passed_along(value, axis, steps):
    count = lax.axis_size(axis)
    leading, last = (max(0, -steps), min(count, count - steps))
    return lax.ppermute(value, axis, [(source, source + steps) for source in range(leading, last)])


def summed_everywhere(x, steps):
    for axis, mask in steps:
        count = lax.axis_size(axis)
        x = x + lax.ppermute(x, axis, [(i, i ^ mask) for i in range(count)])
    return x


def tables():
    positions = jnp.arange(32, dtype=jnp.float32)
    window = jnp.exp(-0.5 * ((positions - 15.5) / 8.0) ** 2)
    phases = 2.0 * jnp.pi * jnp.outer(positions, positions) / 32.0
    cos_part = jnp.cos(phases) * window[None, :] / jnp.sqrt(32.0)
    sin_part = -jnp.sin(phases) * window[None, :] / jnp.sqrt(32.0)
    column_table = jnp.concatenate([cos_part.T, sin_part.T], axis=1)
    cos_split = cos_part.reshape(32, 2, 16)
    sin_split = sin_part.reshape(32, 2, 16)
    upper = jnp.stack([cos_split, -sin_split], axis=-1)
    lower = jnp.stack([sin_split, cos_split], axis=-1)
    row_table = jnp.concatenate([upper, lower], axis=0).reshape(64, 64)
    return (column_table, row_table)


def analyze(region, column_table, row_table):
    win_rows = region.shape[0] // 16 - 1
    win_cols = region.shape[1] // 16 - 1
    blocks = region.reshape(win_rows + 1, 16, win_cols + 1, 16)
    section_one = jnp.einsum(
        "akbl,lp->akpb", blocks[:, :, :win_cols], column_table[:16], precision=precise
    )
    section_one = section_one + jnp.einsum(
        "akbl,lp->akpb", blocks[:, :, 1:], column_table[16:], precision=precise
    )
    section_one = section_one.reshape(win_rows + 1, 16, 2, 32, win_cols)
    paired = jnp.stack([section_one[:-1], section_one[1:]], axis=1).reshape(
        win_rows, 64, 32, win_cols
    )
    return jnp.einsum("tm,amvb->atvb", row_table, paired, precision=precise)


def weigh(coefficients, window_weight, freq_weight):
    doubled = jnp.concatenate([freq_weight, freq_weight], axis=0)
    return coefficients * doubled[None, :, :, None] * window_weight[:, None, None, :]


def synthesize(coefficients, column_table, row_table):
    win_rows = coefficients.shape[0]
    win_cols = coefficients.shape[3]
    spread = jnp.einsum("tm,atvb->amvb", row_table, coefficients, precision=precise)
    spread = spread.reshape(win_rows, 2, 16, 64, win_cols)
    stacked = jnp.pad(spread[:, 0], ((0, 1), (0, 0), (0, 0), (0, 0))) + jnp.pad(
        spread[:, 1], ((1, 0), (0, 0), (0, 0), (0, 0))
    )
    lower_piece = jnp.einsum("akpb,lp->akbl", stacked, column_table[:16], precision=precise)
    upper_piece = jnp.einsum("akpb,lp->akbl", stacked, column_table[16:], precision=precise)
    blocks = jnp.pad(lower_piece, ((0, 0), (0, 0), (0, 1), (0, 0))) + jnp.pad(
        upper_piece, ((0, 0), (0, 0), (1, 0), (0, 0))
    )
    return blocks.reshape(16 * (win_rows + 1), 16 * (win_cols + 1))


def per_device(iterate, residual, direction, window_weight, freq_weight):
    column_table, row_table = tables()
    height, breadth = direction.shape
    beside = passed_along(direction[:, :16], COL, -1)
    widened = jnp.concatenate([direction, beside], axis=1)
    below = passed_along(widened[:16], "row", -1)
    region = jnp.concatenate([widened, below], axis=0)
    coefficients = weigh(analyze(region, column_table, row_table), window_weight, freq_weight)
    spread = synthesize(coefficients, column_table, row_table)
    arrived_rows = passed_along(spread[height:], "row", 1)
    upper_rows = jnp.concatenate([spread[:16] + arrived_rows, spread[16:height]], axis=0)
    arrived_cols = passed_along(upper_rows[:, breadth:], COL, 1)
    synthesized = jnp.concatenate(
        [upper_rows[:, :16] + arrived_cols, upper_rows[:, 16:breadth]], axis=1
    )
    applied = synthesized + damping * direction
    sums = summed_everywhere(
        jnp.stack(
            [
                jnp.sum(residual * residual),
                jnp.sum(direction * applied),
                jnp.sum(residual * applied),
                jnp.sum(applied * applied),
            ]
        ),
        DOUBLING,
    )
    norm_now, curvature, cross_term, image_norm = sums[0], sums[1], sums[2], sums[3]
    step_length = norm_now / curvature
    new_iterate = iterate + step_length * direction
    new_residual = residual - step_length * applied
    norm_next = norm_now - 2.0 * step_length * cross_term + step_length * step_length * image_norm
    new_direction = new_residual + norm_next / norm_now * direction
    return (new_iterate, new_residual, new_direction)


def solution(mesh):
    finer = Mesh(
        mesh.devices.reshape(mesh.shape["row"], 4, 4, 2, 2),
        ("row", "col_0", "col_1", "col_2", "col_3"),
    )
    return jax.shard_map(
        per_device,
        mesh=finer,
        in_specs=(P("row", COL), P("row", COL), P("row", COL), P("row", COL), P()),
        out_specs=(P("row", COL), P("row", COL), P("row", COL)),
        check_vma=False,
    )
```

```python
import jax
import jax.numpy as jnp
from jax import lax
from jax.sharding import Mesh
from jax.sharding import PartitionSpec as P

COL = ("col_0", "col_1", "col_2", "col_3")
DOUBLING = (
    ("col_3", 1),
    ("row", 1),
    ("row", 2),
    ("col_0", 1),
    ("col_0", 2),
    ("col_1", 1),
    ("col_1", 2),
    ("col_2", 1),
)


precise = lax.Precision.HIGHEST
damping = 0.5


def passed_along(value, axis, steps):
    count = lax.axis_size(axis)
    leading, last = (max(0, -steps), min(count, count - steps))
    return lax.ppermute(value, axis, [(source, source + steps) for source in range(leading, last)])


def passed_diagonally(value, steps):
    rows, cols = lax.axis_size("row"), lax.axis_size(COL)
    pairs = [
        (r * cols + c, (r + steps) * cols + (c + steps))
        for r in range(max(0, -steps), min(rows, rows - steps))
        for c in range(max(0, -steps), min(cols, cols - steps))
    ]
    return lax.ppermute(value, ("row",) + COL, pairs)


def summed_everywhere(x, steps):
    for axis, mask in steps:
        count = lax.axis_size(axis)
        x = x + lax.ppermute(x, axis, [(i, i ^ mask) for i in range(count)])
    return x


def tables():
    positions = jnp.arange(32, dtype=jnp.float32)
    window = jnp.exp(-0.5 * ((positions - 15.5) / 8.0) ** 2)
    phases = 2.0 * jnp.pi * jnp.outer(positions, positions) / 32.0
    cos_part = jnp.cos(phases) * window[None, :] / jnp.sqrt(32.0)
    sin_part = -jnp.sin(phases) * window[None, :] / jnp.sqrt(32.0)
    column_table = jnp.concatenate([cos_part.T, sin_part.T], axis=1)
    cos_split = cos_part.reshape(32, 2, 16)
    sin_split = sin_part.reshape(32, 2, 16)
    upper = jnp.stack([cos_split, -sin_split], axis=-1)
    lower = jnp.stack([sin_split, cos_split], axis=-1)
    row_table = jnp.concatenate([upper, lower], axis=0).reshape(64, 64)
    return (column_table, row_table)


def analyze(region, column_table, row_table):
    win_rows = region.shape[0] // 16 - 1
    win_cols = region.shape[1] // 16 - 1
    blocks = region.reshape(win_rows + 1, 16, win_cols + 1, 16)
    section_one = jnp.einsum(
        "akbl,lp->akpb", blocks[:, :, :win_cols], column_table[:16], precision=precise
    )
    section_one = section_one + jnp.einsum(
        "akbl,lp->akpb", blocks[:, :, 1:], column_table[16:], precision=precise
    )
    section_one = section_one.reshape(win_rows + 1, 16, 2, 32, win_cols)
    paired = jnp.stack([section_one[:-1], section_one[1:]], axis=1).reshape(
        win_rows, 64, 32, win_cols
    )
    return jnp.einsum("tm,amvb->atvb", row_table, paired, precision=precise)


def weigh(coefficients, window_weight, freq_weight):
    doubled = jnp.concatenate([freq_weight, freq_weight], axis=0)
    return coefficients * doubled[None, :, :, None] * window_weight[:, None, None, :]


def synthesize(coefficients, column_table, row_table):
    win_rows = coefficients.shape[0]
    win_cols = coefficients.shape[3]
    spread = jnp.einsum("tm,atvb->amvb", row_table, coefficients, precision=precise)
    spread = spread.reshape(win_rows, 2, 16, 64, win_cols)
    stacked = jnp.pad(spread[:, 0], ((0, 1), (0, 0), (0, 0), (0, 0))) + jnp.pad(
        spread[:, 1], ((1, 0), (0, 0), (0, 0), (0, 0))
    )
    lower_piece = jnp.einsum("akpb,lp->akbl", stacked, column_table[:16], precision=precise)
    upper_piece = jnp.einsum("akpb,lp->akbl", stacked, column_table[16:], precision=precise)
    blocks = jnp.pad(lower_piece, ((0, 0), (0, 0), (0, 1), (0, 0))) + jnp.pad(
        upper_piece, ((0, 0), (0, 0), (1, 0), (0, 0))
    )
    return blocks.reshape(16 * (win_rows + 1), 16 * (win_cols + 1))


def per_device(iterate, residual, direction, window_weight, freq_weight):
    column_table, row_table = tables()
    height, breadth = direction.shape
    beside = passed_along(direction[:, :16], COL, -1)
    below = passed_along(direction[:16], "row", -1)
    corner = passed_diagonally(direction[:16, :16], -1)
    region = jnp.concatenate(
        [
            jnp.concatenate([direction, beside], axis=1),
            jnp.concatenate([below, corner], axis=1),
        ],
        axis=0,
    )
    coefficients = weigh(analyze(region, column_table, row_table), window_weight, freq_weight)
    spread = synthesize(coefficients, column_table, row_table)
    arrived_rows = passed_along(spread[height:, :breadth], "row", 1)
    arrived_cols = passed_along(spread[:height, breadth:], COL, 1)
    arrived_corner = passed_diagonally(spread[height:, breadth:], 1)
    synthesized = (
        spread[:height, :breadth]
        + jnp.pad(arrived_rows, ((0, height - 16), (0, 0)))
        + jnp.pad(
            arrived_cols
            + jnp.pad(arrived_corner, ((0, height - 16), (0, 0))),
            ((0, 0), (0, breadth - 16)),
        )
    )
    applied = synthesized + damping * direction
    products = jnp.stack(
        [residual * residual, direction * applied, residual * applied, applied * applied]
    )
    sums = summed_everywhere(jnp.sum(products, axis=(1, 2)), DOUBLING)
    norm_now, curvature, cross_term, image_norm = sums[0], sums[1], sums[2], sums[3]
    step_length = norm_now / curvature
    new_iterate = iterate + step_length * direction
    new_residual = residual - step_length * applied
    norm_next = norm_now - 2.0 * step_length * cross_term + step_length * step_length * image_norm
    new_direction = new_residual + norm_next / norm_now * direction
    return (new_iterate, new_residual, new_direction)


def solution(mesh):
    finer = Mesh(
        mesh.devices.reshape(mesh.shape["row"], 4, 4, 2, 2),
        ("row", "col_0", "col_1", "col_2", "col_3"),
    )
    return jax.shard_map(
        per_device,
        mesh=finer,
        in_specs=(P("row", COL), P("row", COL), P("row", COL), P("row", COL), P()),
        out_specs=(P("row", COL), P("row", COL), P("row", COL)),
        check_vma=False,
    )
```

```python
import jax
import jax.numpy as jnp
from jax import lax
from jax.sharding import Mesh
from jax.sharding import PartitionSpec as P
from jax.experimental import pallas as pl
from jax.experimental.pallas import tpu as pltpu

COL = ("col_0", "col_1", "col_2", "col_3")
DOUBLING = (
    ("col_3", 1),
    ("row", 1),
    ("row", 2),
    ("col_0", 1),
    ("col_0", 2),
    ("col_1", 1),
    ("col_1", 2),
    ("col_2", 1),
)


precise = lax.Precision.HIGHEST
damping = 0.5


def passed_along(value, axis, steps):
    count = lax.axis_size(axis)
    leading, last = (max(0, -steps), min(count, count - steps))
    return lax.ppermute(value, axis, [(source, source + steps) for source in range(leading, last)])


def passed_diagonally(value, steps):
    rows, cols = lax.axis_size("row"), lax.axis_size(COL)
    pairs = [
        (r * cols + c, (r + steps) * cols + (c + steps))
        for r in range(max(0, -steps), min(rows, rows - steps))
        for c in range(max(0, -steps), min(cols, cols - steps))
    ]
    return lax.ppermute(value, ("row",) + COL, pairs)


def summed_everywhere(x, steps):
    for axis, mask in steps:
        count = lax.axis_size(axis)
        x = x + lax.ppermute(x, axis, [(i, i ^ mask) for i in range(count)])
    return x


def tables():
    positions = jnp.arange(32, dtype=jnp.float32)
    window = jnp.exp(-0.5 * ((positions - 15.5) / 8.0) ** 2)
    phases = 2.0 * jnp.pi * jnp.outer(positions, positions) / 32.0
    cos_part = jnp.cos(phases) * window[None, :] / jnp.sqrt(32.0)
    sin_part = -jnp.sin(phases) * window[None, :] / jnp.sqrt(32.0)
    column_table = jnp.concatenate([cos_part.T, sin_part.T], axis=1)
    cos_split = cos_part.reshape(32, 2, 16)
    sin_split = sin_part.reshape(32, 2, 16)
    upper = jnp.stack([cos_split, -sin_split], axis=-1)
    lower = jnp.stack([sin_split, cos_split], axis=-1)
    row_table = jnp.concatenate([upper, lower], axis=0).reshape(64, 64)
    return (column_table, row_table)


def analyze(region, column_table, row_table):
    win_rows = region.shape[0] // 16 - 1
    win_cols = region.shape[1] // 16 - 1
    blocks = region.reshape(win_rows + 1, 16, win_cols + 1, 16)
    section_one = jnp.einsum(
        "akbl,lp->akpb", blocks[:, :, :win_cols], column_table[:16], precision=precise
    )
    section_one = section_one + jnp.einsum(
        "akbl,lp->akpb", blocks[:, :, 1:], column_table[16:], precision=precise
    )
    section_one = section_one.reshape(win_rows + 1, 16, 2, 32, win_cols)
    paired = jnp.stack([section_one[:-1], section_one[1:]], axis=1).reshape(
        win_rows, 64, 32, win_cols
    )
    return jnp.einsum("tm,amvb->atvb", row_table, paired, precision=precise)


def weigh(coefficients, window_weight, freq_weight):
    doubled = jnp.concatenate([freq_weight, freq_weight], axis=0)
    return coefficients * doubled[None, :, :, None] * window_weight[:, None, None, :]


def synthesize(coefficients, column_table, row_table):
    win_rows = coefficients.shape[0]
    win_cols = coefficients.shape[3]
    spread = jnp.einsum("tm,atvb->amvb", row_table, coefficients, precision=precise)
    spread = spread.reshape(win_rows, 2, 16, 64, win_cols)
    stacked = jnp.pad(spread[:, 0], ((0, 1), (0, 0), (0, 0), (0, 0))) + jnp.pad(
        spread[:, 1], ((1, 0), (0, 0), (0, 0), (0, 0))
    )
    lower_piece = jnp.einsum("akpb,lp->akbl", stacked, column_table[:16], precision=precise)
    upper_piece = jnp.einsum("akpb,lp->akbl", stacked, column_table[16:], precision=precise)
    blocks = jnp.pad(lower_piece, ((0, 0), (0, 0), (0, 1), (0, 0))) + jnp.pad(
        upper_piece, ((0, 0), (0, 0), (1, 0), (0, 0))
    )
    return blocks.reshape(16 * (win_rows + 1), 16 * (win_cols + 1))


LANES = 128
WINDOWS_PER_TILE = LANES // 16
HALF = WINDOWS_PER_TILE * 32


def transform_tables(column_table, row_table):
    first = column_table[:16].reshape(16, 2, 32)
    second = column_table[16:].reshape(16, 2, 32)
    same = jnp.eye(2 * WINDOWS_PER_TILE, WINDOWS_PER_TILE, dtype=jnp.float32)
    shifted = jnp.eye(2 * WINDOWS_PER_TILE, WINDOWS_PER_TILE, k=-1, dtype=jnp.float32)
    columns = jnp.einsum("Kk,lcw->Klckw", same, first) + jnp.einsum(
        "Kk,lcw->Klckw", shifted, second
    )
    columns = columns.reshape(2 * LANES, 2 * HALF)
    real = row_table[:32].reshape(32, 2, 16, 2)[..., 0].reshape(32, 32)
    imag = row_table[32:].reshape(32, 2, 16, 2)[..., 0].reshape(32, 32)
    forward = jnp.concatenate([real, imag], axis=1)
    backward = jnp.concatenate([real.T, imag.T], axis=1)
    return columns, columns.T, forward, backward


def transform_kernel(x_ref, m_ref, n_ref, f_ref, g_ref, fw_ref, ww_ref, out_ref):
    rows = x_ref.shape[0]
    win_rows = rows // 16 - 1
    tiles = (x_ref.shape[1] - LANES) // LANES
    out_ref[...] = jnp.zeros_like(out_ref)
    forward = f_ref[...]
    backward = g_ref[...]
    freq = fw_ref[...]

    def one_tile(t, carry):
        start = pl.multiple_of(t * LANES, LANES)
        y = jnp.dot(
            x_ref[:, pl.ds(start, 2 * LANES)],
            m_ref[...],
            precision=lax.Precision.HIGHEST,
            preferred_element_type=jnp.float32,
        )
        weights = ww_ref[:, pl.ds(pl.multiple_of(t * 2 * HALF, 2 * HALF), 2 * HALF)]
        pieces = []
        for a in range(win_rows):
            ya = y[16 * a : 16 * a + 32]
            turned = jnp.concatenate([-ya[:, HALF:], ya[:, :HALF]], axis=1)
            z = jnp.dot(
                forward,
                jnp.concatenate([ya, turned], axis=0),
                precision=lax.Precision.HIGHEST,
                preferred_element_type=jnp.float32,
            )
            z = z * freq * weights[a : a + 1]
            turned = jnp.concatenate([z[:, HALF:], -z[:, :HALF]], axis=1)
            pieces.append(
                jnp.dot(
                    backward,
                    jnp.concatenate([z, turned], axis=0),
                    precision=lax.Precision.HIGHEST,
                    preferred_element_type=jnp.float32,
                )
            )
        blocks = [pieces[0][:16]]
        for a in range(1, win_rows):
            blocks.append(pieces[a][:16] + pieces[a - 1][16:])
        blocks.append(pieces[win_rows - 1][16:])
        stacked = jnp.concatenate(blocks, axis=0)
        out_ref[:, pl.ds(start, 2 * LANES)] += jnp.dot(
            stacked,
            n_ref[...],
            precision=lax.Precision.HIGHEST,
            preferred_element_type=jnp.float32,
        )
        return carry

    lax.fori_loop(0, tiles, one_tile, 0)


def analyze_weigh_synthesize(region, window_weight, freq_weight, column_table, row_table):
    rows, cols = region.shape
    tiles = (cols - 16) // LANES
    wide = (tiles + 1) * LANES
    padded = jnp.pad(region, ((0, 0), (0, wide - cols)))
    columns, columns_t, forward, backward = transform_tables(column_table, row_table)
    freq = jnp.tile(freq_weight, (1, 2 * WINDOWS_PER_TILE))
    weights = jnp.repeat(window_weight, 32, axis=1).reshape(
        window_weight.shape[0], tiles, WINDOWS_PER_TILE, 32
    )
    weights = jnp.concatenate([weights, weights], axis=2).reshape(window_weight.shape[0], -1)
    vmem = pl.BlockSpec(memory_space=pltpu.VMEM)
    out = pl.pallas_call(
        transform_kernel,
        out_shape=jax.ShapeDtypeStruct((rows, wide), jnp.float32),
        in_specs=[vmem] * 7,
        out_specs=vmem,
    )(padded, columns, columns_t, forward, backward, freq, weights)
    return out[:, :cols]

def per_device(iterate, residual, direction, window_weight, freq_weight):
    column_table, row_table = tables()
    height, breadth = direction.shape
    beside = passed_along(direction[:, :16], COL, -1)
    below = passed_along(direction[:16], "row", -1)
    corner = passed_diagonally(direction[:16, :16], -1)
    region = jnp.concatenate(
        [
            jnp.concatenate([direction, beside], axis=1),
            jnp.concatenate([below, corner], axis=1),
        ],
        axis=0,
    )
    spread = analyze_weigh_synthesize(region, window_weight, freq_weight, column_table, row_table)
    arrived_rows = passed_along(spread[height:, :breadth], "row", 1)
    arrived_cols = passed_along(spread[:height, breadth:], COL, 1)
    arrived_corner = passed_diagonally(spread[height:, breadth:], 1)
    synthesized = (
        spread[:height, :breadth]
        + jnp.pad(arrived_rows, ((0, height - 16), (0, 0)))
        + jnp.pad(
            arrived_cols
            + jnp.pad(arrived_corner, ((0, height - 16), (0, 0))),
            ((0, 0), (0, breadth - 16)),
        )
    )
    applied = synthesized + damping * direction
    products = jnp.stack(
        [residual * residual, direction * applied, residual * applied, applied * applied]
    )
    sums = summed_everywhere(jnp.sum(products, axis=(1, 2)), DOUBLING)
    norm_now, curvature, cross_term, image_norm = sums[0], sums[1], sums[2], sums[3]
    step_length = norm_now / curvature
    new_iterate = iterate + step_length * direction
    new_residual = residual - step_length * applied
    norm_next = norm_now - 2.0 * step_length * cross_term + step_length * step_length * image_norm
    new_direction = new_residual + norm_next / norm_now * direction
    return (new_iterate, new_residual, new_direction)


def solution(mesh):
    finer = Mesh(
        mesh.devices.reshape(mesh.shape["row"], 4, 4, 2, 2),
        ("row", "col_0", "col_1", "col_2", "col_3"),
    )
    return jax.shard_map(
        per_device,
        mesh=finer,
        in_specs=(P("row", COL), P("row", COL), P("row", COL), P("row", COL), P()),
        out_specs=(P("row", COL), P("row", COL), P("row", COL)),
        check_vma=False,
    )
```

```python
import jax
import numpy as np
import jax.numpy as jnp
from jax import lax
from jax.sharding import Mesh
from jax.sharding import PartitionSpec as P
from jax.experimental import pallas as pl
from jax.experimental.pallas import tpu as pltpu

COL = ("col_0", "col_1", "col_2", "col_3")
DOUBLING = (
    ("col_3", 1),
    ("row", 1),
    ("row", 2),
    ("col_0", 1),
    ("col_0", 2),
    ("col_1", 1),
    ("col_1", 2),
    ("col_2", 1),
)


precise = lax.Precision.HIGHEST
damping = 0.5


def passed_along(value, axis, steps):
    count = lax.axis_size(axis)
    leading, last = (max(0, -steps), min(count, count - steps))
    return lax.ppermute(value, axis, [(source, source + steps) for source in range(leading, last)])


def passed_diagonally(value, steps):
    rows, cols = lax.axis_size("row"), lax.axis_size(COL)
    pairs = [
        (r * cols + c, (r + steps) * cols + (c + steps))
        for r in range(max(0, -steps), min(rows, rows - steps))
        for c in range(max(0, -steps), min(cols, cols - steps))
    ]
    return lax.ppermute(value, ("row",) + COL, pairs)


def summed_everywhere(x, steps):
    for axis, mask in steps:
        count = lax.axis_size(axis)
        x = x + lax.ppermute(x, axis, [(i, i ^ mask) for i in range(count)])
    return x


def tables():
    positions = jnp.arange(32, dtype=jnp.float32)
    window = jnp.exp(-0.5 * ((positions - 15.5) / 8.0) ** 2)
    phases = 2.0 * jnp.pi * jnp.outer(positions, positions) / 32.0
    cos_part = jnp.cos(phases) * window[None, :] / jnp.sqrt(32.0)
    sin_part = -jnp.sin(phases) * window[None, :] / jnp.sqrt(32.0)
    column_table = jnp.concatenate([cos_part.T, sin_part.T], axis=1)
    cos_split = cos_part.reshape(32, 2, 16)
    sin_split = sin_part.reshape(32, 2, 16)
    upper = jnp.stack([cos_split, -sin_split], axis=-1)
    lower = jnp.stack([sin_split, cos_split], axis=-1)
    row_table = jnp.concatenate([upper, lower], axis=0).reshape(64, 64)
    return (column_table, row_table)


def analyze(region, column_table, row_table):
    win_rows = region.shape[0] // 16 - 1
    win_cols = region.shape[1] // 16 - 1
    blocks = region.reshape(win_rows + 1, 16, win_cols + 1, 16)
    section_one = jnp.einsum(
        "akbl,lp->akpb", blocks[:, :, :win_cols], column_table[:16], precision=precise
    )
    section_one = section_one + jnp.einsum(
        "akbl,lp->akpb", blocks[:, :, 1:], column_table[16:], precision=precise
    )
    section_one = section_one.reshape(win_rows + 1, 16, 2, 32, win_cols)
    paired = jnp.stack([section_one[:-1], section_one[1:]], axis=1).reshape(
        win_rows, 64, 32, win_cols
    )
    return jnp.einsum("tm,amvb->atvb", row_table, paired, precision=precise)


def weigh(coefficients, window_weight, freq_weight):
    doubled = jnp.concatenate([freq_weight, freq_weight], axis=0)
    return coefficients * doubled[None, :, :, None] * window_weight[:, None, None, :]


def synthesize(coefficients, column_table, row_table):
    win_rows = coefficients.shape[0]
    win_cols = coefficients.shape[3]
    spread = jnp.einsum("tm,atvb->amvb", row_table, coefficients, precision=precise)
    spread = spread.reshape(win_rows, 2, 16, 64, win_cols)
    stacked = jnp.pad(spread[:, 0], ((0, 1), (0, 0), (0, 0), (0, 0))) + jnp.pad(
        spread[:, 1], ((1, 0), (0, 0), (0, 0), (0, 0))
    )
    lower_piece = jnp.einsum("akpb,lp->akbl", stacked, column_table[:16], precision=precise)
    upper_piece = jnp.einsum("akpb,lp->akbl", stacked, column_table[16:], precision=precise)
    blocks = jnp.pad(lower_piece, ((0, 0), (0, 0), (0, 1), (0, 0))) + jnp.pad(
        upper_piece, ((0, 0), (0, 0), (1, 0), (0, 0))
    )
    return blocks.reshape(16 * (win_rows + 1), 16 * (win_cols + 1))


LANES = 128
WINDOWS_PER_TILE = LANES // 16
HALF = WINDOWS_PER_TILE * 32


def numpy_tables():
    positions = np.arange(32, dtype=np.float32)
    window = np.exp(np.float32(-0.5) * ((positions - np.float32(15.5)) / np.float32(8.0)) ** 2)
    phases = np.float32(2.0 * np.pi) * np.outer(positions, positions) / np.float32(32.0)
    scale = np.sqrt(np.float32(32.0))
    cos_part = np.cos(phases) * window[None, :] / scale
    sin_part = -np.sin(phases) * window[None, :] / scale
    return cos_part.astype(np.float32), sin_part.astype(np.float32)


def transform_tables(win_rows):
    cos_part, sin_part = numpy_tables()
    column_table = np.stack([cos_part.T, sin_part.T], axis=1)
    columns = np.zeros((2 * WINDOWS_PER_TILE, 16, 2, WINDOWS_PER_TILE, 32), np.float32)
    for k in range(WINDOWS_PER_TILE):
        columns[k, :, :, k] = column_table[:16]
        columns[k + 1, :, :, k] = column_table[16:]
    columns = columns.reshape(2 * LANES, 2 * HALF)
    blocks = win_rows + 1
    real = np.zeros((win_rows, 32, blocks * 16), np.float32)
    imag = np.zeros((win_rows, 32, blocks * 16), np.float32)
    for a in range(win_rows):
        real[a, :, 16 * a : 16 * a + 32] = cos_part
        imag[a, :, 16 * a : 16 * a + 32] = sin_part
    real = real.reshape(win_rows * 32, blocks * 16)
    imag = imag.reshape(win_rows * 32, blocks * 16)
    forward = np.concatenate([real, imag], axis=1)
    backward = np.concatenate([real.T, imag.T], axis=1)
    return [columns, np.ascontiguousarray(columns.T), forward, backward]


def split_constant(table):
    high = table.astype(jnp.bfloat16)
    low = (table - high.astype(np.float32)).astype(jnp.bfloat16)
    return [jnp.asarray(high), jnp.asarray(low)]


def split_value(value):
    high = value.astype(jnp.bfloat16)
    return high, (value - high.astype(jnp.float32)).astype(jnp.bfloat16)


def three_pass_dot(a, b):
    total = jnp.dot(a[0], b[1], preferred_element_type=jnp.float32)
    total += jnp.dot(a[1], b[0], preferred_element_type=jnp.float32)
    return total + jnp.dot(a[0], b[0], preferred_element_type=jnp.float32)


def transform_kernel(
    x_ref, mh_ref, ml_ref, nh_ref, nl_ref, fh_ref, fl_ref, gh_ref, gl_ref, fw_ref, ww_ref,
    out_ref, y_ref, e_ref,
):
    rows = x_ref.shape[0]
    win_rows = rows // 16 - 1
    tiles = (x_ref.shape[1] - LANES) // LANES
    stacked_x = jnp.concatenate(
        [x_ref[:, t * LANES : (t + 2) * LANES] for t in range(tiles)], axis=0
    )
    y_ref[...] = three_pass_dot(split_value(stacked_x), (mh_ref[...], ml_ref[...]))
    forward = (fh_ref[...], fl_ref[...])
    backward = (gh_ref[...], gl_ref[...])
    freq = fw_ref[...]

    def one_tile(t, carry):
        here = pl.ds(pl.multiple_of(t * rows, 8), rows)
        y = y_ref[here, :]
        weights = ww_ref[:, pl.ds(pl.multiple_of(t * 2 * HALF, 2 * HALF), 2 * HALF)]
        turned = jnp.concatenate([-y[:, HALF:], y[:, :HALF]], axis=1)
        z = three_pass_dot(forward, split_value(jnp.concatenate([y, turned], axis=0)))
        spread = jnp.concatenate(
            [jnp.broadcast_to(weights[a : a + 1], (32, 2 * HALF)) for a in range(win_rows)],
            axis=0,
        )
        z = z * freq * spread
        turned = jnp.concatenate([z[:, HALF:], -z[:, :HALF]], axis=1)
        e_ref[here, :] = three_pass_dot(backward, split_value(jnp.concatenate([z, turned], axis=0)))
        return carry

    lax.fori_loop(0, tiles, one_tile, 0)
    pieces = three_pass_dot(split_value(e_ref[...]), (nh_ref[...], nl_ref[...]))
    out_ref[...] = jnp.zeros_like(out_ref)
    for t in range(tiles):
        out_ref[:, t * LANES : (t + 2) * LANES] += pieces[t * rows : (t + 1) * rows]


def analyze_weigh_synthesize(region, window_weight, freq_weight):
    rows, cols = region.shape
    tiles = (cols - 16) // LANES
    wide = (tiles + 1) * LANES
    padded = jnp.pad(region, ((0, 0), (0, wide - cols)))
    win_rows = rows // 16 - 1
    constants = []
    for table in transform_tables(win_rows):
        constants += split_constant(table)
    freq = jnp.broadcast_to(
        freq_weight.reshape(1, 32, 1, 1, 32), (win_rows, 32, 2, WINDOWS_PER_TILE, 32)
    ).reshape(win_rows * 32, 2 * HALF)
    weights = jnp.broadcast_to(
        window_weight.reshape(win_rows, tiles, 1, WINDOWS_PER_TILE, 1),
        (win_rows, tiles, 2, WINDOWS_PER_TILE, 32),
    ).reshape(win_rows, tiles * 2 * HALF)
    vmem = pl.BlockSpec(memory_space=pltpu.VMEM)
    out = pl.pallas_call(
        transform_kernel,
        out_shape=jax.ShapeDtypeStruct((rows, wide), jnp.float32),
        in_specs=[vmem] * 11,
        out_specs=vmem,
        scratch_shapes=[
            pltpu.VMEM((tiles * rows, 2 * HALF), jnp.float32),
            pltpu.VMEM((tiles * rows, 2 * HALF), jnp.float32),
        ],
    )(padded, *constants, freq, weights)
    return out[:, :cols]


def per_device(iterate, residual, direction, window_weight, freq_weight):
    height, breadth = direction.shape
    beside = passed_along(direction[:, :16], COL, -1)
    below = passed_along(direction[:16], "row", -1)
    corner = passed_diagonally(direction[:16, :16], -1)
    region = jnp.concatenate(
        [
            jnp.concatenate([direction, beside], axis=1),
            jnp.concatenate([below, corner], axis=1),
        ],
        axis=0,
    )
    spread = analyze_weigh_synthesize(region, window_weight, freq_weight)
    arrived_rows = passed_along(spread[height:, :breadth], "row", 1)
    arrived_cols = passed_along(spread[:height, breadth:], COL, 1)
    arrived_corner = passed_diagonally(spread[height:, breadth:], 1)
    synthesized = (
        spread[:height, :breadth]
        + jnp.pad(arrived_rows, ((0, height - 16), (0, 0)))
        + jnp.pad(
            arrived_cols
            + jnp.pad(arrived_corner, ((0, height - 16), (0, 0))),
            ((0, 0), (0, breadth - 16)),
        )
    )
    applied = synthesized + damping * direction
    products = jnp.stack(
        [residual * residual, direction * applied, residual * applied, applied * applied]
    )
    sums = summed_everywhere(jnp.sum(products, axis=(1, 2)), DOUBLING)
    norm_now, curvature, cross_term, image_norm = sums[0], sums[1], sums[2], sums[3]
    step_length = norm_now / curvature
    new_iterate = iterate + step_length * direction
    new_residual = residual - step_length * applied
    norm_next = norm_now - 2.0 * step_length * cross_term + step_length * step_length * image_norm
    new_direction = new_residual + norm_next / norm_now * direction
    return (new_iterate, new_residual, new_direction)


def solution(mesh):
    finer = Mesh(
        mesh.devices.reshape(mesh.shape["row"], 4, 4, 2, 2),
        ("row", "col_0", "col_1", "col_2", "col_3"),
    )
    return jax.shard_map(
        per_device,
        mesh=finer,
        in_specs=(P("row", COL), P("row", COL), P("row", COL), P("row", COL), P()),
        out_specs=(P("row", COL), P("row", COL), P("row", COL)),
        check_vma=False,
    )
```

```python
import jax
import numpy as np
import jax.numpy as jnp
from jax import lax
from jax.sharding import Mesh
from jax.sharding import PartitionSpec as P
from jax.experimental import pallas as pl
from jax.experimental.pallas import tpu as pltpu

COL = ("col_0", "col_1", "col_2", "col_3")
DOUBLING = (
    ("col_3", 1),
    ("row", 1),
    ("row", 2),
    ("col_0", 1),
    ("col_0", 2),
    ("col_1", 1),
    ("col_1", 2),
    ("col_2", 1),
)


precise = lax.Precision.HIGHEST
damping = 0.5


def passed_along(value, axis, steps):
    count = lax.axis_size(axis)
    leading, last = (max(0, -steps), min(count, count - steps))
    return lax.ppermute(value, axis, [(source, source + steps) for source in range(leading, last)])


def passed_diagonally(value, steps):
    rows, cols = lax.axis_size("row"), lax.axis_size(COL)
    pairs = [
        (r * cols + c, (r + steps) * cols + (c + steps))
        for r in range(max(0, -steps), min(rows, rows - steps))
        for c in range(max(0, -steps), min(cols, cols - steps))
    ]
    return lax.ppermute(value, ("row",) + COL, pairs)


def summed_everywhere(x, steps):
    for axis, mask in steps:
        count = lax.axis_size(axis)
        x = x + lax.ppermute(x, axis, [(i, i ^ mask) for i in range(count)])
    return x


def tables():
    positions = jnp.arange(32, dtype=jnp.float32)
    window = jnp.exp(-0.5 * ((positions - 15.5) / 8.0) ** 2)
    phases = 2.0 * jnp.pi * jnp.outer(positions, positions) / 32.0
    cos_part = jnp.cos(phases) * window[None, :] / jnp.sqrt(32.0)
    sin_part = -jnp.sin(phases) * window[None, :] / jnp.sqrt(32.0)
    column_table = jnp.concatenate([cos_part.T, sin_part.T], axis=1)
    cos_split = cos_part.reshape(32, 2, 16)
    sin_split = sin_part.reshape(32, 2, 16)
    upper = jnp.stack([cos_split, -sin_split], axis=-1)
    lower = jnp.stack([sin_split, cos_split], axis=-1)
    row_table = jnp.concatenate([upper, lower], axis=0).reshape(64, 64)
    return (column_table, row_table)


def analyze(region, column_table, row_table):
    win_rows = region.shape[0] // 16 - 1
    win_cols = region.shape[1] // 16 - 1
    blocks = region.reshape(win_rows + 1, 16, win_cols + 1, 16)
    section_one = jnp.einsum(
        "akbl,lp->akpb", blocks[:, :, :win_cols], column_table[:16], precision=precise
    )
    section_one = section_one + jnp.einsum(
        "akbl,lp->akpb", blocks[:, :, 1:], column_table[16:], precision=precise
    )
    section_one = section_one.reshape(win_rows + 1, 16, 2, 32, win_cols)
    paired = jnp.stack([section_one[:-1], section_one[1:]], axis=1).reshape(
        win_rows, 64, 32, win_cols
    )
    return jnp.einsum("tm,amvb->atvb", row_table, paired, precision=precise)


def weigh(coefficients, window_weight, freq_weight):
    doubled = jnp.concatenate([freq_weight, freq_weight], axis=0)
    return coefficients * doubled[None, :, :, None] * window_weight[:, None, None, :]


def synthesize(coefficients, column_table, row_table):
    win_rows = coefficients.shape[0]
    win_cols = coefficients.shape[3]
    spread = jnp.einsum("tm,atvb->amvb", row_table, coefficients, precision=precise)
    spread = spread.reshape(win_rows, 2, 16, 64, win_cols)
    stacked = jnp.pad(spread[:, 0], ((0, 1), (0, 0), (0, 0), (0, 0))) + jnp.pad(
        spread[:, 1], ((1, 0), (0, 0), (0, 0), (0, 0))
    )
    lower_piece = jnp.einsum("akpb,lp->akbl", stacked, column_table[:16], precision=precise)
    upper_piece = jnp.einsum("akpb,lp->akbl", stacked, column_table[16:], precision=precise)
    blocks = jnp.pad(lower_piece, ((0, 0), (0, 0), (0, 1), (0, 0))) + jnp.pad(
        upper_piece, ((0, 0), (0, 0), (1, 0), (0, 0))
    )
    return blocks.reshape(16 * (win_rows + 1), 16 * (win_cols + 1))


LANES = 128
WINDOWS_PER_TILE = LANES // 16
HALF = WINDOWS_PER_TILE * 32


def numpy_tables():
    positions = np.arange(32, dtype=np.float32)
    window = np.exp(np.float32(-0.5) * ((positions - np.float32(15.5)) / np.float32(8.0)) ** 2)
    phases = np.float32(2.0 * np.pi) * np.outer(positions, positions) / np.float32(32.0)
    scale = np.sqrt(np.float32(32.0))
    cos_part = np.cos(phases) * window[None, :] / scale
    sin_part = -np.sin(phases) * window[None, :] / scale
    return cos_part.astype(np.float32), sin_part.astype(np.float32)


def transform_tables(win_rows):
    cos_part, sin_part = numpy_tables()
    column_table = np.stack([cos_part.T, sin_part.T], axis=1)
    columns = np.zeros((2 * WINDOWS_PER_TILE, 16, 2, WINDOWS_PER_TILE, 32), np.float32)
    for k in range(WINDOWS_PER_TILE):
        columns[k, :, :, k] = column_table[:16]
        columns[k + 1, :, :, k] = column_table[16:]
    columns = columns.reshape(2 * LANES, 2 * HALF)
    blocks = win_rows + 1
    real = np.zeros((win_rows, 32, blocks * 16), np.float32)
    imag = np.zeros((win_rows, 32, blocks * 16), np.float32)
    for a in range(win_rows):
        real[a, :, 16 * a : 16 * a + 32] = cos_part
        imag[a, :, 16 * a : 16 * a + 32] = sin_part
    real = real.reshape(win_rows * 32, blocks * 16)
    imag = imag.reshape(win_rows * 32, blocks * 16)
    forward = np.concatenate([real, imag], axis=1)
    backward = np.concatenate([real.T, imag.T], axis=1)
    return [columns, np.ascontiguousarray(columns.T), forward, backward]


def split_constant(table):
    high = table.astype(jnp.bfloat16)
    low = (table - high.astype(np.float32)).astype(jnp.bfloat16)
    return [jnp.asarray(high), jnp.asarray(low)]


def split_value(value):
    high = value.astype(jnp.bfloat16)
    return high, (value - high.astype(jnp.float32)).astype(jnp.bfloat16)


def three_pass_dot(a, b):
    total = jnp.dot(a[0], b[1], preferred_element_type=jnp.float32)
    total += jnp.dot(a[1], b[0], preferred_element_type=jnp.float32)
    return total + jnp.dot(a[0], b[0], preferred_element_type=jnp.float32)


def transform_kernel(
    x_ref, mh_ref, ml_ref, nh_ref, nl_ref, fh_ref, fl_ref, gh_ref, gl_ref, fw_ref, ww_ref,
    out_ref, y_ref, e_ref,
):
    rows = x_ref.shape[0]
    win_rows = rows // 16 - 1
    tiles = (x_ref.shape[1] - LANES) // LANES
    stacked_x = jnp.concatenate(
        [x_ref[:, t * LANES : (t + 2) * LANES] for t in range(tiles)], axis=0
    )
    y_ref[...] = three_pass_dot(split_value(stacked_x), (mh_ref[...], ml_ref[...]))
    forward = (fh_ref[...], fl_ref[...])
    backward = (gh_ref[...], gl_ref[...])
    freq = fw_ref[...]

    def one_tile(t, carry):
        here = pl.ds(pl.multiple_of(t * rows, 8), rows)
        y = y_ref[here, :]
        weights = ww_ref[:, pl.ds(pl.multiple_of(t * 2 * HALF, 2 * HALF), 2 * HALF)]
        turned = jnp.concatenate([-y[:, HALF:], y[:, :HALF]], axis=1)
        z = three_pass_dot(forward, split_value(jnp.concatenate([y, turned], axis=0)))
        spread = jnp.concatenate(
            [jnp.broadcast_to(weights[a : a + 1], (32, 2 * HALF)) for a in range(win_rows)],
            axis=0,
        )
        z = z * freq * spread
        turned = jnp.concatenate([z[:, HALF:], -z[:, :HALF]], axis=1)
        e_ref[here, :] = three_pass_dot(backward, split_value(jnp.concatenate([z, turned], axis=0)))
        return carry

    lax.fori_loop(0, tiles, one_tile, 0)
    pieces = three_pass_dot(split_value(e_ref[...]), (nh_ref[...], nl_ref[...]))
    out_ref[...] = jnp.zeros_like(out_ref)
    for t in range(tiles):
        out_ref[:, t * LANES : (t + 2) * LANES] += pieces[t * rows : (t + 1) * rows]


def analyze_weigh_synthesize(region, window_weight, freq_weight):
    rows, cols = region.shape
    windows = (cols - 16) // 16
    tiles = -(-windows // WINDOWS_PER_TILE)
    wide = (tiles + 1) * LANES
    window_weight = jnp.pad(window_weight, ((0, 0), (0, tiles * WINDOWS_PER_TILE - windows)))
    padded = jnp.pad(region, ((0, 0), (0, wide - cols)))
    win_rows = rows // 16 - 1
    constants = []
    for table in transform_tables(win_rows):
        constants += split_constant(table)
    freq = jnp.broadcast_to(
        freq_weight.reshape(1, 32, 1, 1, 32), (win_rows, 32, 2, WINDOWS_PER_TILE, 32)
    ).reshape(win_rows * 32, 2 * HALF)
    weights = jnp.broadcast_to(
        window_weight.reshape(win_rows, tiles, 1, WINDOWS_PER_TILE, 1),
        (win_rows, tiles, 2, WINDOWS_PER_TILE, 32),
    ).reshape(win_rows, tiles * 2 * HALF)
    vmem = pl.BlockSpec(memory_space=pltpu.VMEM)
    out = pl.pallas_call(
        transform_kernel,
        out_shape=jax.ShapeDtypeStruct((rows, wide), jnp.float32),
        in_specs=[vmem] * 11,
        out_specs=vmem,
        scratch_shapes=[
            pltpu.VMEM((tiles * rows, 2 * HALF), jnp.float32),
            pltpu.VMEM((tiles * rows, 2 * HALF), jnp.float32),
        ],
    )(padded, *constants, freq, weights)
    return out[:, :cols]


def per_device(iterate, residual, direction, window_weight, freq_weight):
    height, breadth = direction.shape
    rim_weight = jnp.pad(window_weight[:, -1:], ((0, 0), (0, 15)))
    from_left = passed_along(
        jnp.concatenate([direction[:, -16:], rim_weight], axis=0), COL, 1
    )
    from_right = passed_along(direction[:, :16], COL, -1)
    widened = jnp.concatenate([from_left[:height], direction, from_right], axis=1)
    weights_wide = jnp.concatenate([from_left[height:, :1], window_weight], axis=1)
    top_weight = jnp.pad(weights_wide[-1:], ((0, 0), (0, widened.shape[1] - weights_wide.shape[1])))
    from_above = passed_along(
        jnp.concatenate([widened[-16:], top_weight], axis=0), "row", 1
    )
    from_below = passed_along(widened[:16], "row", -1)
    region = jnp.concatenate([from_above[:16], widened, from_below], axis=0)
    weights_all = jnp.concatenate(
        [from_above[16:, : weights_wide.shape[1]], weights_wide], axis=0
    )
    spread = analyze_weigh_synthesize(region, weights_all, freq_weight)
    synthesized = spread[16 : 16 + height, 16 : 16 + breadth]
    applied = synthesized + damping * direction
    products = jnp.stack(
        [residual * residual, direction * applied, residual * applied, applied * applied]
    )
    sums = summed_everywhere(jnp.sum(products, axis=(1, 2)), DOUBLING)
    norm_now, curvature, cross_term, image_norm = sums[0], sums[1], sums[2], sums[3]
    step_length = norm_now / curvature
    new_iterate = iterate + step_length * direction
    new_residual = residual - step_length * applied
    norm_next = norm_now - 2.0 * step_length * cross_term + step_length * step_length * image_norm
    new_direction = new_residual + norm_next / norm_now * direction
    return (new_iterate, new_residual, new_direction)


def solution(mesh):
    finer = Mesh(
        mesh.devices.reshape(mesh.shape["row"], 4, 4, 2, 2),
        ("row", "col_0", "col_1", "col_2", "col_3"),
    )
    return jax.shard_map(
        per_device,
        mesh=finer,
        in_specs=(P("row", COL), P("row", COL), P("row", COL), P("row", COL), P()),
        out_specs=(P("row", COL), P("row", COL), P("row", COL)),
        check_vma=False,
    )
```

```python
import jax
import numpy as np
import jax.numpy as jnp
from jax import lax
from jax.sharding import Mesh
from jax.sharding import PartitionSpec as P
from jax.experimental import pallas as pl
from jax.experimental.pallas import tpu as pltpu

COL = ("col_0", "col_1", "col_2", "col_3")
DOUBLING = (
    ("col_3", 1),
    ("row", 1),
    ("row", 2),
    ("col_0", 1),
    ("col_0", 2),
    ("col_1", 1),
    ("col_1", 2),
    ("col_2", 1),
)


precise = lax.Precision.HIGHEST
damping = 0.5


def passed_along(value, axis, steps):
    count = lax.axis_size(axis)
    leading, last = (max(0, -steps), min(count, count - steps))
    return lax.ppermute(value, axis, [(source, source + steps) for source in range(leading, last)])


def passed_diagonally(value, steps):
    rows, cols = lax.axis_size("row"), lax.axis_size(COL)
    pairs = [
        (r * cols + c, (r + steps) * cols + (c + steps))
        for r in range(max(0, -steps), min(rows, rows - steps))
        for c in range(max(0, -steps), min(cols, cols - steps))
    ]
    return lax.ppermute(value, ("row",) + COL, pairs)


def summed_everywhere(x, steps):
    for axis, mask in steps:
        count = lax.axis_size(axis)
        x = x + lax.ppermute(x, axis, [(i, i ^ mask) for i in range(count)])
    return x


def tables():
    positions = jnp.arange(32, dtype=jnp.float32)
    window = jnp.exp(-0.5 * ((positions - 15.5) / 8.0) ** 2)
    phases = 2.0 * jnp.pi * jnp.outer(positions, positions) / 32.0
    cos_part = jnp.cos(phases) * window[None, :] / jnp.sqrt(32.0)
    sin_part = -jnp.sin(phases) * window[None, :] / jnp.sqrt(32.0)
    column_table = jnp.concatenate([cos_part.T, sin_part.T], axis=1)
    cos_split = cos_part.reshape(32, 2, 16)
    sin_split = sin_part.reshape(32, 2, 16)
    upper = jnp.stack([cos_split, -sin_split], axis=-1)
    lower = jnp.stack([sin_split, cos_split], axis=-1)
    row_table = jnp.concatenate([upper, lower], axis=0).reshape(64, 64)
    return (column_table, row_table)


def analyze(region, column_table, row_table):
    win_rows = region.shape[0] // 16 - 1
    win_cols = region.shape[1] // 16 - 1
    blocks = region.reshape(win_rows + 1, 16, win_cols + 1, 16)
    section_one = jnp.einsum(
        "akbl,lp->akpb", blocks[:, :, :win_cols], column_table[:16], precision=precise
    )
    section_one = section_one + jnp.einsum(
        "akbl,lp->akpb", blocks[:, :, 1:], column_table[16:], precision=precise
    )
    section_one = section_one.reshape(win_rows + 1, 16, 2, 32, win_cols)
    paired = jnp.stack([section_one[:-1], section_one[1:]], axis=1).reshape(
        win_rows, 64, 32, win_cols
    )
    return jnp.einsum("tm,amvb->atvb", row_table, paired, precision=precise)


def weigh(coefficients, window_weight, freq_weight):
    doubled = jnp.concatenate([freq_weight, freq_weight], axis=0)
    return coefficients * doubled[None, :, :, None] * window_weight[:, None, None, :]


def synthesize(coefficients, column_table, row_table):
    win_rows = coefficients.shape[0]
    win_cols = coefficients.shape[3]
    spread = jnp.einsum("tm,atvb->amvb", row_table, coefficients, precision=precise)
    spread = spread.reshape(win_rows, 2, 16, 64, win_cols)
    stacked = jnp.pad(spread[:, 0], ((0, 1), (0, 0), (0, 0), (0, 0))) + jnp.pad(
        spread[:, 1], ((1, 0), (0, 0), (0, 0), (0, 0))
    )
    lower_piece = jnp.einsum("akpb,lp->akbl", stacked, column_table[:16], precision=precise)
    upper_piece = jnp.einsum("akpb,lp->akbl", stacked, column_table[16:], precision=precise)
    blocks = jnp.pad(lower_piece, ((0, 0), (0, 0), (0, 1), (0, 0))) + jnp.pad(
        upper_piece, ((0, 0), (0, 0), (1, 0), (0, 0))
    )
    return blocks.reshape(16 * (win_rows + 1), 16 * (win_cols + 1))


LANES = 128
WINDOWS_PER_TILE = LANES // 16
HALF = WINDOWS_PER_TILE * 32


def numpy_tables():
    positions = np.arange(32, dtype=np.float32)
    window = np.exp(np.float32(-0.5) * ((positions - np.float32(15.5)) / np.float32(8.0)) ** 2)
    phases = np.float32(2.0 * np.pi) * np.outer(positions, positions) / np.float32(32.0)
    scale = np.sqrt(np.float32(32.0))
    cos_part = np.cos(phases) * window[None, :] / scale
    sin_part = -np.sin(phases) * window[None, :] / scale
    return cos_part.astype(np.float32), sin_part.astype(np.float32)


def transform_tables(win_rows):
    cos_part, sin_part = numpy_tables()
    column_table = np.stack([cos_part.T, sin_part.T], axis=1)
    columns = np.zeros((2 * WINDOWS_PER_TILE, 16, 2, WINDOWS_PER_TILE, 32), np.float32)
    for k in range(WINDOWS_PER_TILE):
        columns[k, :, :, k] = column_table[:16]
        columns[k + 1, :, :, k] = column_table[16:]
    columns = columns.reshape(2 * LANES, 2 * HALF)
    blocks = win_rows + 1
    real = np.zeros((win_rows, 32, blocks * 16), np.float32)
    imag = np.zeros((win_rows, 32, blocks * 16), np.float32)
    for a in range(win_rows):
        real[a, :, 16 * a : 16 * a + 32] = cos_part
        imag[a, :, 16 * a : 16 * a + 32] = sin_part
    real = real.reshape(win_rows * 32, blocks * 16)
    imag = imag.reshape(win_rows * 32, blocks * 16)
    forward = np.concatenate([real, imag], axis=1)
    backward = np.concatenate([real.T, imag.T], axis=1)
    return [columns, np.ascontiguousarray(columns.T), forward, backward]


def split_constant(table):
    high = table.astype(jnp.bfloat16)
    low = (table - high.astype(np.float32)).astype(jnp.bfloat16)
    return [jnp.asarray(high), jnp.asarray(low)]


def split_value(value):
    high = value.astype(jnp.bfloat16)
    return high, (value - high.astype(jnp.float32)).astype(jnp.bfloat16)


def three_pass_dot(a, b):
    total = jnp.dot(a[0], b[1], preferred_element_type=jnp.float32)
    total += jnp.dot(a[1], b[0], preferred_element_type=jnp.float32)
    return total + jnp.dot(a[0], b[0], preferred_element_type=jnp.float32)


def transform_kernel(
    x_ref, mh_ref, ml_ref, nh_ref, nl_ref, fh_ref, fl_ref, gh_ref, gl_ref, fw_ref, ww_ref,
    out_ref, y_ref, e_ref,
):
    rows = x_ref.shape[0]
    win_rows = rows // 16 - 1
    tiles = (x_ref.shape[1] - LANES) // LANES
    stacked_x = jnp.concatenate(
        [x_ref[:, t * LANES : (t + 2) * LANES] for t in range(tiles)], axis=0
    )
    y_ref[...] = three_pass_dot(split_value(stacked_x), (mh_ref[...], ml_ref[...]))
    forward = (fh_ref[...], fl_ref[...])
    backward = (gh_ref[...], gl_ref[...])
    freq = fw_ref[...]

    def one_tile(t, carry):
        here = pl.ds(pl.multiple_of(t * rows, 8), rows)
        y = y_ref[here, :]
        weights = ww_ref[:, pl.ds(pl.multiple_of(t * 2 * HALF, 2 * HALF), 2 * HALF)]
        turned = jnp.concatenate([-y[:, HALF:], y[:, :HALF]], axis=1)
        z = three_pass_dot(forward, split_value(jnp.concatenate([y, turned], axis=0)))
        spread = jnp.concatenate(
            [jnp.broadcast_to(weights[a : a + 1], (32, 2 * HALF)) for a in range(win_rows)],
            axis=0,
        )
        z = z * freq * spread
        turned = jnp.concatenate([z[:, HALF:], -z[:, :HALF]], axis=1)
        e_ref[here, :] = three_pass_dot(backward, split_value(jnp.concatenate([z, turned], axis=0)))
        return carry

    lax.fori_loop(0, tiles, one_tile, 0)
    pieces = three_pass_dot(split_value(e_ref[...]), (nh_ref[...], nl_ref[...]))
    out_ref[...] = jnp.zeros_like(out_ref)
    for t in range(tiles):
        out_ref[:, t * LANES : (t + 2) * LANES] += pieces[t * rows : (t + 1) * rows]


def analyze_weigh_synthesize(region, window_weight, freq_weight):
    rows, cols = region.shape
    windows = (cols - 16) // 16
    tiles = -(-windows // WINDOWS_PER_TILE)
    wide = (tiles + 1) * LANES
    window_weight = jnp.pad(window_weight, ((0, 0), (0, tiles * WINDOWS_PER_TILE - windows)))
    padded = jnp.pad(region, ((0, 0), (0, wide - cols)))
    win_rows = rows // 16 - 1
    constants = []
    for table in transform_tables(win_rows):
        constants += split_constant(table)
    freq = jnp.broadcast_to(
        freq_weight.reshape(1, 32, 1, 1, 32), (win_rows, 32, 2, WINDOWS_PER_TILE, 32)
    ).reshape(win_rows * 32, 2 * HALF)
    weights = jnp.broadcast_to(
        window_weight.reshape(win_rows, tiles, 1, WINDOWS_PER_TILE, 1),
        (win_rows, tiles, 2, WINDOWS_PER_TILE, 32),
    ).reshape(win_rows, tiles * 2 * HALF)
    vmem = pl.BlockSpec(memory_space=pltpu.VMEM)
    out = pl.pallas_call(
        transform_kernel,
        out_shape=jax.ShapeDtypeStruct((rows, wide), jnp.float32),
        in_specs=[vmem] * 11,
        out_specs=vmem,
        scratch_shapes=[
            pltpu.VMEM((tiles * rows, 2 * HALF), jnp.float32),
            pltpu.VMEM((tiles * rows, 2 * HALF), jnp.float32),
        ],
    )(padded, *constants, freq, weights)
    return out[:, :cols]


def per_device(iterate, residual, direction, window_weight, freq_weight):
    height, breadth = direction.shape
    rim_weight = jnp.pad(window_weight[:, -1:], ((0, 0), (0, 15)))
    from_left = passed_along(
        jnp.concatenate([direction[:, -16:], rim_weight], axis=0), COL, 1
    )
    from_right = passed_along(direction[:, :16], COL, -1)
    widened = jnp.concatenate([from_left[:height], direction, from_right], axis=1)
    weights_wide = jnp.concatenate([from_left[height:, :1], window_weight], axis=1)
    middle = analyze_weigh_synthesize(widened, weights_wide[:-1], freq_weight)
    top_weight = jnp.pad(weights_wide[-1:], ((0, 0), (0, widened.shape[1] - weights_wide.shape[1])))
    from_above = passed_along(
        jnp.concatenate([widened[-16:], top_weight], axis=0), "row", 1
    )
    from_below = passed_along(widened[:16], "row", -1)
    top = analyze_weigh_synthesize(
        jnp.concatenate([from_above[:16], widened[:16]], axis=0),
        from_above[16:, : weights_wide.shape[1]],
        freq_weight,
    )
    bottom = analyze_weigh_synthesize(
        jnp.concatenate([widened[-16:], from_below], axis=0),
        weights_wide[-1:],
        freq_weight,
    )
    inner = slice(16, 16 + breadth)
    synthesized = middle[:, inner] + jnp.concatenate(
        [top[16:, inner], jnp.zeros((height - 32, breadth), jnp.float32), bottom[:16, inner]],
        axis=0,
    )
    applied = synthesized + damping * direction
    products = jnp.stack(
        [residual * residual, direction * applied, residual * applied, applied * applied]
    )
    sums = summed_everywhere(jnp.sum(products, axis=(1, 2)), DOUBLING)
    norm_now, curvature, cross_term, image_norm = sums[0], sums[1], sums[2], sums[3]
    step_length = norm_now / curvature
    new_iterate = iterate + step_length * direction
    new_residual = residual - step_length * applied
    norm_next = norm_now - 2.0 * step_length * cross_term + step_length * step_length * image_norm
    new_direction = new_residual + norm_next / norm_now * direction
    return (new_iterate, new_residual, new_direction)


def solution(mesh):
    finer = Mesh(
        mesh.devices.reshape(mesh.shape["row"], 4, 4, 2, 2),
        ("row", "col_0", "col_1", "col_2", "col_3"),
    )
    return jax.shard_map(
        per_device,
        mesh=finer,
        in_specs=(P("row", COL), P("row", COL), P("row", COL), P("row", COL), P()),
        out_specs=(P("row", COL), P("row", COL), P("row", COL)),
        check_vma=False,
    )
```

```python
import jax
import numpy as np
import jax.numpy as jnp
from jax import lax
from jax.sharding import Mesh
from jax.sharding import PartitionSpec as P
from jax.experimental import pallas as pl
from jax.experimental.pallas import tpu as pltpu

COL = ("col_0", "col_1", "col_2", "col_3")
DOUBLING = (
    ("col_3", 1),
    ("row", 1),
    ("row", 2),
    ("col_0", 1),
    ("col_0", 2),
    ("col_1", 1),
    ("col_1", 2),
    ("col_2", 1),
)


precise = lax.Precision.HIGHEST
damping = 0.5


def passed_along(value, axis, steps):
    count = lax.axis_size(axis)
    leading, last = (max(0, -steps), min(count, count - steps))
    return lax.ppermute(value, axis, [(source, source + steps) for source in range(leading, last)])


def passed_diagonally(value, steps):
    rows, cols = lax.axis_size("row"), lax.axis_size(COL)
    pairs = [
        (r * cols + c, (r + steps) * cols + (c + steps))
        for r in range(max(0, -steps), min(rows, rows - steps))
        for c in range(max(0, -steps), min(cols, cols - steps))
    ]
    return lax.ppermute(value, ("row",) + COL, pairs)


def summed_everywhere(x, steps):
    for axis, mask in steps:
        count = lax.axis_size(axis)
        x = x + lax.ppermute(x, axis, [(i, i ^ mask) for i in range(count)])
    return x


def tables():
    positions = jnp.arange(32, dtype=jnp.float32)
    window = jnp.exp(-0.5 * ((positions - 15.5) / 8.0) ** 2)
    phases = 2.0 * jnp.pi * jnp.outer(positions, positions) / 32.0
    cos_part = jnp.cos(phases) * window[None, :] / jnp.sqrt(32.0)
    sin_part = -jnp.sin(phases) * window[None, :] / jnp.sqrt(32.0)
    column_table = jnp.concatenate([cos_part.T, sin_part.T], axis=1)
    cos_split = cos_part.reshape(32, 2, 16)
    sin_split = sin_part.reshape(32, 2, 16)
    upper = jnp.stack([cos_split, -sin_split], axis=-1)
    lower = jnp.stack([sin_split, cos_split], axis=-1)
    row_table = jnp.concatenate([upper, lower], axis=0).reshape(64, 64)
    return (column_table, row_table)


def analyze(region, column_table, row_table):
    win_rows = region.shape[0] // 16 - 1
    win_cols = region.shape[1] // 16 - 1
    blocks = region.reshape(win_rows + 1, 16, win_cols + 1, 16)
    section_one = jnp.einsum(
        "akbl,lp->akpb", blocks[:, :, :win_cols], column_table[:16], precision=precise
    )
    section_one = section_one + jnp.einsum(
        "akbl,lp->akpb", blocks[:, :, 1:], column_table[16:], precision=precise
    )
    section_one = section_one.reshape(win_rows + 1, 16, 2, 32, win_cols)
    paired = jnp.stack([section_one[:-1], section_one[1:]], axis=1).reshape(
        win_rows, 64, 32, win_cols
    )
    return jnp.einsum("tm,amvb->atvb", row_table, paired, precision=precise)


def weigh(coefficients, window_weight, freq_weight):
    doubled = jnp.concatenate([freq_weight, freq_weight], axis=0)
    return coefficients * doubled[None, :, :, None] * window_weight[:, None, None, :]


def synthesize(coefficients, column_table, row_table):
    win_rows = coefficients.shape[0]
    win_cols = coefficients.shape[3]
    spread = jnp.einsum("tm,atvb->amvb", row_table, coefficients, precision=precise)
    spread = spread.reshape(win_rows, 2, 16, 64, win_cols)
    stacked = jnp.pad(spread[:, 0], ((0, 1), (0, 0), (0, 0), (0, 0))) + jnp.pad(
        spread[:, 1], ((1, 0), (0, 0), (0, 0), (0, 0))
    )
    lower_piece = jnp.einsum("akpb,lp->akbl", stacked, column_table[:16], precision=precise)
    upper_piece = jnp.einsum("akpb,lp->akbl", stacked, column_table[16:], precision=precise)
    blocks = jnp.pad(lower_piece, ((0, 0), (0, 0), (0, 1), (0, 0))) + jnp.pad(
        upper_piece, ((0, 0), (0, 0), (1, 0), (0, 0))
    )
    return blocks.reshape(16 * (win_rows + 1), 16 * (win_cols + 1))


LANES = 128
WINDOWS_PER_TILE = LANES // 16
HALF = WINDOWS_PER_TILE * 32


def numpy_tables():
    positions = np.arange(32, dtype=np.float32)
    window = np.exp(np.float32(-0.5) * ((positions - np.float32(15.5)) / np.float32(8.0)) ** 2)
    phases = np.float32(2.0 * np.pi) * np.outer(positions, positions) / np.float32(32.0)
    scale = np.sqrt(np.float32(32.0))
    cos_part = np.cos(phases) * window[None, :] / scale
    sin_part = -np.sin(phases) * window[None, :] / scale
    return cos_part.astype(np.float32), sin_part.astype(np.float32)


def transform_tables(win_rows):
    cos_part, sin_part = numpy_tables()
    column_table = np.stack([cos_part.T, sin_part.T], axis=1)
    columns = np.zeros((2 * WINDOWS_PER_TILE, 16, 2, WINDOWS_PER_TILE, 32), np.float32)
    for k in range(WINDOWS_PER_TILE):
        columns[k, :, :, k] = column_table[:16]
        columns[k + 1, :, :, k] = column_table[16:]
    columns = columns.reshape(2 * LANES, 2 * HALF)
    blocks = win_rows + 1
    real = np.zeros((win_rows, 32, blocks * 16), np.float32)
    imag = np.zeros((win_rows, 32, blocks * 16), np.float32)
    for a in range(win_rows):
        real[a, :, 16 * a : 16 * a + 32] = cos_part
        imag[a, :, 16 * a : 16 * a + 32] = sin_part
    real = real.reshape(win_rows * 32, blocks * 16)
    imag = imag.reshape(win_rows * 32, blocks * 16)
    forward = np.concatenate([real, imag], axis=1)
    backward = np.concatenate([real.T, imag.T], axis=1)
    return [columns, np.ascontiguousarray(columns.T), forward, backward]


def split_constant(table):
    high = table.astype(jnp.bfloat16)
    low = (table - high.astype(np.float32)).astype(jnp.bfloat16)
    return [jnp.asarray(high), jnp.asarray(low)]


def split_value(value):
    high = value.astype(jnp.bfloat16)
    return high, (value - high.astype(jnp.float32)).astype(jnp.bfloat16)


def three_pass_dot(a, b):
    total = jnp.dot(a[0], b[1], preferred_element_type=jnp.float32)
    total += jnp.dot(a[1], b[0], preferred_element_type=jnp.float32)
    return total + jnp.dot(a[0], b[0], preferred_element_type=jnp.float32)


def constant_first_dot(a, b):
    rows = a[0].shape[0]
    both = jnp.dot(
        jnp.concatenate([a[0], a[1]], axis=0), b[0], preferred_element_type=jnp.float32
    )
    total = jnp.dot(a[0], b[1], preferred_element_type=jnp.float32)
    total += both[rows:]
    return total + both[:rows]


def transform_kernel(
    x_ref, mh_ref, ml_ref, nh_ref, nl_ref, fh_ref, fl_ref, gh_ref, gl_ref, fw_ref, ww_ref,
    out_ref, y_ref, e_ref,
):
    rows = x_ref.shape[0]
    win_rows = rows // 16 - 1
    tiles = (x_ref.shape[1] - LANES) // LANES
    stacked_x = jnp.concatenate(
        [x_ref[:, t * LANES : (t + 2) * LANES] for t in range(tiles)], axis=0
    )
    y_ref[...] = three_pass_dot(split_value(stacked_x), (mh_ref[...], ml_ref[...]))
    forward = (fh_ref[...], fl_ref[...])
    backward = (gh_ref[...], gl_ref[...])
    freq = fw_ref[...]

    def one_tile(t, carry):
        here = pl.ds(pl.multiple_of(t * rows, 8), rows)
        y = y_ref[here, :]
        weights = ww_ref[:, pl.ds(pl.multiple_of(t * 2 * HALF, 2 * HALF), 2 * HALF)]
        turned = jnp.concatenate([-y[:, HALF:], y[:, :HALF]], axis=1)
        z = constant_first_dot(forward, split_value(jnp.concatenate([y, turned], axis=0)))
        spread = jnp.concatenate(
            [jnp.broadcast_to(weights[a : a + 1], (32, 2 * HALF)) for a in range(win_rows)],
            axis=0,
        )
        z = z * freq * spread
        turned = jnp.concatenate([z[:, HALF:], -z[:, :HALF]], axis=1)
        e_ref[here, :] = constant_first_dot(backward, split_value(jnp.concatenate([z, turned], axis=0)))
        return carry

    lax.fori_loop(0, tiles, one_tile, 0, unroll=True)
    pieces = three_pass_dot(split_value(e_ref[...]), (nh_ref[...], nl_ref[...]))
    out_ref[...] = jnp.zeros_like(out_ref)
    for t in range(tiles):
        out_ref[:, t * LANES : (t + 2) * LANES] += pieces[t * rows : (t + 1) * rows]


def analyze_weigh_synthesize(region, window_weight, freq_weight):
    rows, cols = region.shape
    windows = (cols - 16) // 16
    tiles = -(-windows // WINDOWS_PER_TILE)
    wide = (tiles + 1) * LANES
    window_weight = jnp.pad(window_weight, ((0, 0), (0, tiles * WINDOWS_PER_TILE - windows)))
    padded = jnp.pad(region, ((0, 0), (0, wide - cols)))
    win_rows = rows // 16 - 1
    constants = []
    for table in transform_tables(win_rows):
        constants += split_constant(table)
    freq = jnp.broadcast_to(
        freq_weight.reshape(1, 32, 1, 1, 32), (win_rows, 32, 2, WINDOWS_PER_TILE, 32)
    ).reshape(win_rows * 32, 2 * HALF)
    weights = jnp.broadcast_to(
        window_weight.reshape(win_rows, tiles, 1, WINDOWS_PER_TILE, 1),
        (win_rows, tiles, 2, WINDOWS_PER_TILE, 32),
    ).reshape(win_rows, tiles * 2 * HALF)
    vmem = pl.BlockSpec(memory_space=pltpu.VMEM)
    out = pl.pallas_call(
        transform_kernel,
        out_shape=jax.ShapeDtypeStruct((rows, wide), jnp.float32),
        in_specs=[vmem] * 11,
        out_specs=vmem,
        scratch_shapes=[
            pltpu.VMEM((tiles * rows, 2 * HALF), jnp.float32),
            pltpu.VMEM((tiles * rows, 2 * HALF), jnp.float32),
        ],
    )(padded, *constants, freq, weights)
    return out[:, :cols]


def per_device(iterate, residual, direction, window_weight, freq_weight):
    height, breadth = direction.shape
    count = window_weight.shape[1]
    top_weight = jnp.pad(window_weight[-1:], ((0, 0), (0, breadth - count)))
    from_above = passed_along(jnp.concatenate([direction[-16:], top_weight], axis=0), "row", 1)
    from_below = passed_along(direction[:16], "row", -1)
    tall = jnp.concatenate([from_above[:16], direction, from_below], axis=0)
    weights_tall = jnp.concatenate([from_above[16:, :count], window_weight], axis=0)
    middle = analyze_weigh_synthesize(tall, weights_tall[:, :-1], freq_weight)
    rim_weight = jnp.pad(weights_tall[:, -1:], ((0, 0), (0, 15)))
    from_left = passed_along(jnp.concatenate([tall[:, -16:], rim_weight], axis=0), COL, 1)
    from_right = passed_along(tall[:, :16], COL, -1)
    rows = tall.shape[0]
    edges = analyze_weigh_synthesize(
        jnp.concatenate([from_left[:rows], tall[:, :16], tall[:, -16:], from_right], axis=1),
        jnp.concatenate(
            [from_left[rows:, :1], jnp.zeros_like(weights_tall[:, :1]), weights_tall[:, -1:]],
            axis=1,
        ),
        freq_weight,
    )
    own = slice(16, 16 + height)
    synthesized = middle[own, :breadth] + jnp.concatenate(
        [
            edges[own, 16:32],
            jnp.zeros((height, breadth - 32), jnp.float32),
            edges[own, 32:48],
        ],
        axis=1,
    )
    applied = synthesized + damping * direction
    products = jnp.stack(
        [residual * residual, direction * applied, residual * applied, applied * applied]
    )
    sums = summed_everywhere(jnp.sum(products, axis=(1, 2)), DOUBLING)
    norm_now, curvature, cross_term, image_norm = sums[0], sums[1], sums[2], sums[3]
    step_length = norm_now / curvature
    new_iterate = iterate + step_length * direction
    new_residual = residual - step_length * applied
    norm_next = norm_now - 2.0 * step_length * cross_term + step_length * step_length * image_norm
    new_direction = new_residual + norm_next / norm_now * direction
    return (new_iterate, new_residual, new_direction)


def solution(mesh):
    finer = Mesh(
        mesh.devices.reshape(mesh.shape["row"], 4, 4, 2, 2),
        ("row", "col_0", "col_1", "col_2", "col_3"),
    )
    return jax.shard_map(
        per_device,
        mesh=finer,
        in_specs=(P("row", COL), P("row", COL), P("row", COL), P("row", COL), P()),
        out_specs=(P("row", COL), P("row", COL), P("row", COL)),
        check_vma=False,
    )
```

```python
import jax
import numpy as np
import jax.numpy as jnp
from jax import lax
from jax.sharding import Mesh
from jax.sharding import PartitionSpec as P
from jax.experimental import pallas as pl
from jax.experimental.pallas import tpu as pltpu

COL = ("col_0", "col_1", "col_2", "col_3")
DOUBLING = (
    ("col_3", 1),
    ("row", 1),
    ("row", 2),
    ("col_0", 1),
    ("col_0", 2),
    ("col_1", 1),
    ("col_1", 2),
    ("col_2", 1),
)


precise = lax.Precision.HIGHEST
damping = 0.5


def passed_along(value, axis, steps):
    count = lax.axis_size(axis)
    leading, last = (max(0, -steps), min(count, count - steps))
    return lax.ppermute(value, axis, [(source, source + steps) for source in range(leading, last)])


def passed_diagonally(value, steps):
    rows, cols = lax.axis_size("row"), lax.axis_size(COL)
    pairs = [
        (r * cols + c, (r + steps) * cols + (c + steps))
        for r in range(max(0, -steps), min(rows, rows - steps))
        for c in range(max(0, -steps), min(cols, cols - steps))
    ]
    return lax.ppermute(value, ("row",) + COL, pairs)


def summed_everywhere(x, steps):
    for axis, mask in steps:
        count = lax.axis_size(axis)
        x = x + lax.ppermute(x, axis, [(i, i ^ mask) for i in range(count)])
    return x


def tables():
    positions = jnp.arange(32, dtype=jnp.float32)
    window = jnp.exp(-0.5 * ((positions - 15.5) / 8.0) ** 2)
    phases = 2.0 * jnp.pi * jnp.outer(positions, positions) / 32.0
    cos_part = jnp.cos(phases) * window[None, :] / jnp.sqrt(32.0)
    sin_part = -jnp.sin(phases) * window[None, :] / jnp.sqrt(32.0)
    column_table = jnp.concatenate([cos_part.T, sin_part.T], axis=1)
    cos_split = cos_part.reshape(32, 2, 16)
    sin_split = sin_part.reshape(32, 2, 16)
    upper = jnp.stack([cos_split, -sin_split], axis=-1)
    lower = jnp.stack([sin_split, cos_split], axis=-1)
    row_table = jnp.concatenate([upper, lower], axis=0).reshape(64, 64)
    return (column_table, row_table)


def analyze(region, column_table, row_table):
    win_rows = region.shape[0] // 16 - 1
    win_cols = region.shape[1] // 16 - 1
    blocks = region.reshape(win_rows + 1, 16, win_cols + 1, 16)
    section_one = jnp.einsum(
        "akbl,lp->akpb", blocks[:, :, :win_cols], column_table[:16], precision=precise
    )
    section_one = section_one + jnp.einsum(
        "akbl,lp->akpb", blocks[:, :, 1:], column_table[16:], precision=precise
    )
    section_one = section_one.reshape(win_rows + 1, 16, 2, 32, win_cols)
    paired = jnp.stack([section_one[:-1], section_one[1:]], axis=1).reshape(
        win_rows, 64, 32, win_cols
    )
    return jnp.einsum("tm,amvb->atvb", row_table, paired, precision=precise)


def weigh(coefficients, window_weight, freq_weight):
    doubled = jnp.concatenate([freq_weight, freq_weight], axis=0)
    return coefficients * doubled[None, :, :, None] * window_weight[:, None, None, :]


def synthesize(coefficients, column_table, row_table):
    win_rows = coefficients.shape[0]
    win_cols = coefficients.shape[3]
    spread = jnp.einsum("tm,atvb->amvb", row_table, coefficients, precision=precise)
    spread = spread.reshape(win_rows, 2, 16, 64, win_cols)
    stacked = jnp.pad(spread[:, 0], ((0, 1), (0, 0), (0, 0), (0, 0))) + jnp.pad(
        spread[:, 1], ((1, 0), (0, 0), (0, 0), (0, 0))
    )
    lower_piece = jnp.einsum("akpb,lp->akbl", stacked, column_table[:16], precision=precise)
    upper_piece = jnp.einsum("akpb,lp->akbl", stacked, column_table[16:], precision=precise)
    blocks = jnp.pad(lower_piece, ((0, 0), (0, 0), (0, 1), (0, 0))) + jnp.pad(
        upper_piece, ((0, 0), (0, 0), (1, 0), (0, 0))
    )
    return blocks.reshape(16 * (win_rows + 1), 16 * (win_cols + 1))


LANES = 128
WINDOWS_PER_TILE = LANES // 16
HALF = WINDOWS_PER_TILE * 32


def numpy_tables():
    positions = np.arange(32, dtype=np.float32)
    window = np.exp(np.float32(-0.5) * ((positions - np.float32(15.5)) / np.float32(8.0)) ** 2)
    phases = np.float32(2.0 * np.pi) * np.outer(positions, positions) / np.float32(32.0)
    scale = np.sqrt(np.float32(32.0))
    cos_part = np.cos(phases) * window[None, :] / scale
    sin_part = -np.sin(phases) * window[None, :] / scale
    return cos_part.astype(np.float32), sin_part.astype(np.float32)


def transform_tables(win_rows):
    cos_part, sin_part = numpy_tables()
    column_table = np.stack([cos_part.T, sin_part.T], axis=1)
    columns = np.zeros((2 * WINDOWS_PER_TILE, 16, 2, WINDOWS_PER_TILE, 32), np.float32)
    for k in range(WINDOWS_PER_TILE):
        columns[k, :, :, k] = column_table[:16]
        columns[k + 1, :, :, k] = column_table[16:]
    columns = columns.reshape(2 * LANES, 2 * HALF)
    blocks = win_rows + 1
    real = np.zeros((win_rows, 32, blocks * 16), np.float32)
    imag = np.zeros((win_rows, 32, blocks * 16), np.float32)
    for a in range(win_rows):
        real[a, :, 16 * a : 16 * a + 32] = cos_part
        imag[a, :, 16 * a : 16 * a + 32] = sin_part
    real = real.reshape(win_rows * 32, blocks * 16)
    imag = imag.reshape(win_rows * 32, blocks * 16)
    forward = np.concatenate([real, imag], axis=1)
    backward = np.concatenate([real.T, imag.T], axis=1)
    return [columns, forward, backward]


def split_constant(table):
    high = table.astype(jnp.bfloat16)
    low = (table - high.astype(np.float32)).astype(jnp.bfloat16)
    return [jnp.asarray(high), jnp.asarray(low)]


def split_value(value):
    high = value.astype(jnp.bfloat16)
    return high, (value - high.astype(jnp.float32)).astype(jnp.bfloat16)


def three_pass_dot(a, b):
    total = jnp.dot(a[0], b[1], preferred_element_type=jnp.float32)
    total += jnp.dot(a[1], b[0], preferred_element_type=jnp.float32)
    return total + jnp.dot(a[0], b[0], preferred_element_type=jnp.float32)


def transposed_dot(a, b):
    def one(x, y):
        return lax.dot_general(
            x, y, (((1,), (1,)), ((), ())), preferred_element_type=jnp.float32
        )
    return one(a[0], b[1]) + one(a[1], b[0]) + one(a[0], b[0])


def constant_first_dot(a, b):
    rows = a[0].shape[0]
    both = jnp.dot(
        jnp.concatenate([a[0], a[1]], axis=0), b[0], preferred_element_type=jnp.float32
    )
    total = jnp.dot(a[0], b[1], preferred_element_type=jnp.float32)
    total += both[rows:]
    return total + both[:rows]


def transform_kernel(
    x_ref, mh_ref, ml_ref, fh_ref, fl_ref, gh_ref, gl_ref, fw_ref, ww_ref,
    out_ref, y_ref, e_ref,
):
    rows = x_ref.shape[0]
    win_rows = rows // 16 - 1
    tiles = (x_ref.shape[1] - LANES) // LANES
    stacked_x = jnp.concatenate(
        [x_ref[:, t * LANES : (t + 2) * LANES] for t in range(tiles)], axis=0
    )
    y_ref[...] = three_pass_dot(split_value(stacked_x), (mh_ref[...], ml_ref[...]))
    forward = (fh_ref[...], fl_ref[...])
    backward = (gh_ref[...], gl_ref[...])
    freq = fw_ref[...]

    def one_tile(t, carry):
        here = pl.ds(pl.multiple_of(t * rows, 8), rows)
        y = y_ref[here, :]
        weights = ww_ref[:, pl.ds(pl.multiple_of(t * 2 * HALF, 2 * HALF), 2 * HALF)]
        turned = jnp.concatenate([-y[:, HALF:], y[:, :HALF]], axis=1)
        z = constant_first_dot(forward, split_value(jnp.concatenate([y, turned], axis=0)))
        spread = jnp.concatenate(
            [jnp.broadcast_to(weights[a : a + 1], (32, 2 * HALF)) for a in range(win_rows)],
            axis=0,
        )
        z = z * freq * spread
        turned = jnp.concatenate([z[:, HALF:], -z[:, :HALF]], axis=1)
        e_ref[here, :] = constant_first_dot(backward, split_value(jnp.concatenate([z, turned], axis=0)))
        return carry

    lax.fori_loop(0, tiles, one_tile, 0, unroll=True)
    pieces = transposed_dot(split_value(e_ref[...]), (mh_ref[...], ml_ref[...]))
    out_ref[...] = jnp.zeros_like(out_ref)
    for t in range(tiles):
        out_ref[:, t * LANES : (t + 2) * LANES] += pieces[t * rows : (t + 1) * rows]


def analyze_weigh_synthesize(region, window_weight, freq_weight):
    rows, cols = region.shape
    windows = (cols - 16) // 16
    tiles = -(-windows // WINDOWS_PER_TILE)
    wide = (tiles + 1) * LANES
    window_weight = jnp.pad(window_weight, ((0, 0), (0, tiles * WINDOWS_PER_TILE - windows)))
    padded = jnp.pad(region, ((0, 0), (0, wide - cols)))
    win_rows = rows // 16 - 1
    constants = []
    for table in transform_tables(win_rows):
        constants += split_constant(table)
    freq = jnp.broadcast_to(
        freq_weight.reshape(1, 32, 1, 1, 32), (win_rows, 32, 2, WINDOWS_PER_TILE, 32)
    ).reshape(win_rows * 32, 2 * HALF)
    weights = jnp.broadcast_to(
        window_weight.reshape(win_rows, tiles, 1, WINDOWS_PER_TILE, 1),
        (win_rows, tiles, 2, WINDOWS_PER_TILE, 32),
    ).reshape(win_rows, tiles * 2 * HALF)
    vmem = pl.BlockSpec(memory_space=pltpu.VMEM)
    out = pl.pallas_call(
        transform_kernel,
        out_shape=jax.ShapeDtypeStruct((rows, wide), jnp.float32),
        in_specs=[vmem] * 9,
        out_specs=vmem,
        scratch_shapes=[
            pltpu.VMEM((tiles * rows, 2 * HALF), jnp.float32),
            pltpu.VMEM((tiles * rows, 2 * HALF), jnp.float32),
        ],
    )(padded, *constants, freq, weights)
    return out[:, :cols]


def per_device(iterate, residual, direction, window_weight, freq_weight):
    height, breadth = direction.shape
    rim_weight = jnp.pad(window_weight[:, -1:], ((0, 0), (0, 15)))
    from_left = passed_along(
        jnp.concatenate([direction[:, -16:], rim_weight], axis=0), COL, 1
    )
    from_right = passed_along(direction[:, :16], COL, -1)
    widened = jnp.concatenate([from_left[:height], direction, from_right], axis=1)
    weights_wide = jnp.concatenate([from_left[height:, :1], window_weight], axis=1)
    top_weight = jnp.pad(weights_wide[-1:], ((0, 0), (0, widened.shape[1] - weights_wide.shape[1])))
    from_above = passed_along(
        jnp.concatenate([widened[-16:], top_weight], axis=0), "row", 1
    )
    from_below = passed_along(widened[:16], "row", -1)
    region = jnp.concatenate([from_above[:16], widened, from_below], axis=0)
    weights_all = jnp.concatenate(
        [from_above[16:, : weights_wide.shape[1]], weights_wide], axis=0
    )
    spread = analyze_weigh_synthesize(region, weights_all, freq_weight)
    synthesized = spread[16 : 16 + height, 16 : 16 + breadth]
    applied = synthesized + damping * direction
    products = jnp.stack(
        [residual * residual, direction * applied, residual * applied, applied * applied]
    )
    sums = summed_everywhere(jnp.sum(products, axis=(1, 2)), DOUBLING)
    norm_now, curvature, cross_term, image_norm = sums[0], sums[1], sums[2], sums[3]
    step_length = norm_now / curvature
    new_iterate = iterate + step_length * direction
    new_residual = residual - step_length * applied
    norm_next = norm_now - 2.0 * step_length * cross_term + step_length * step_length * image_norm
    new_direction = new_residual + norm_next / norm_now * direction
    return (new_iterate, new_residual, new_direction)


def solution(mesh):
    finer = Mesh(
        mesh.devices.reshape(mesh.shape["row"], 4, 4, 2, 2),
        ("row", "col_0", "col_1", "col_2", "col_3"),
    )
    return jax.shard_map(
        per_device,
        mesh=finer,
        in_specs=(P("row", COL), P("row", COL), P("row", COL), P("row", COL), P()),
        out_specs=(P("row", COL), P("row", COL), P("row", COL)),
        check_vma=False,
    )
```

```python
import jax
import numpy as np
import jax.numpy as jnp
from jax import lax
from jax.sharding import Mesh
from jax.sharding import PartitionSpec as P
from jax.experimental import pallas as pl
from jax.experimental.pallas import tpu as pltpu

COL = ("col_0", "col_1", "col_2", "col_3")
DOUBLING = (
    ("col_3", 1),
    ("row", 1),
    ("row", 2),
    ("col_0", 1),
    ("col_0", 2),
    ("col_1", 1),
    ("col_1", 2),
    ("col_2", 1),
)


precise = lax.Precision.HIGHEST
damping = 0.5


def passed_along(value, axis, steps):
    count = lax.axis_size(axis)
    leading, last = (max(0, -steps), min(count, count - steps))
    return lax.ppermute(value, axis, [(source, source + steps) for source in range(leading, last)])


def passed_diagonally(value, steps):
    rows, cols = lax.axis_size("row"), lax.axis_size(COL)
    pairs = [
        (r * cols + c, (r + steps) * cols + (c + steps))
        for r in range(max(0, -steps), min(rows, rows - steps))
        for c in range(max(0, -steps), min(cols, cols - steps))
    ]
    return lax.ppermute(value, ("row",) + COL, pairs)


def summed_everywhere(x, steps):
    for axis, mask in steps:
        count = lax.axis_size(axis)
        x = x + lax.ppermute(x, axis, [(i, i ^ mask) for i in range(count)])
    return x


def tables():
    positions = jnp.arange(32, dtype=jnp.float32)
    window = jnp.exp(-0.5 * ((positions - 15.5) / 8.0) ** 2)
    phases = 2.0 * jnp.pi * jnp.outer(positions, positions) / 32.0
    cos_part = jnp.cos(phases) * window[None, :] / jnp.sqrt(32.0)
    sin_part = -jnp.sin(phases) * window[None, :] / jnp.sqrt(32.0)
    column_table = jnp.concatenate([cos_part.T, sin_part.T], axis=1)
    cos_split = cos_part.reshape(32, 2, 16)
    sin_split = sin_part.reshape(32, 2, 16)
    upper = jnp.stack([cos_split, -sin_split], axis=-1)
    lower = jnp.stack([sin_split, cos_split], axis=-1)
    row_table = jnp.concatenate([upper, lower], axis=0).reshape(64, 64)
    return (column_table, row_table)


def analyze(region, column_table, row_table):
    win_rows = region.shape[0] // 16 - 1
    win_cols = region.shape[1] // 16 - 1
    blocks = region.reshape(win_rows + 1, 16, win_cols + 1, 16)
    section_one = jnp.einsum(
        "akbl,lp->akpb", blocks[:, :, :win_cols], column_table[:16], precision=precise
    )
    section_one = section_one + jnp.einsum(
        "akbl,lp->akpb", blocks[:, :, 1:], column_table[16:], precision=precise
    )
    section_one = section_one.reshape(win_rows + 1, 16, 2, 32, win_cols)
    paired = jnp.stack([section_one[:-1], section_one[1:]], axis=1).reshape(
        win_rows, 64, 32, win_cols
    )
    return jnp.einsum("tm,amvb->atvb", row_table, paired, precision=precise)


def weigh(coefficients, window_weight, freq_weight):
    doubled = jnp.concatenate([freq_weight, freq_weight], axis=0)
    return coefficients * doubled[None, :, :, None] * window_weight[:, None, None, :]


def synthesize(coefficients, column_table, row_table):
    win_rows = coefficients.shape[0]
    win_cols = coefficients.shape[3]
    spread = jnp.einsum("tm,atvb->amvb", row_table, coefficients, precision=precise)
    spread = spread.reshape(win_rows, 2, 16, 64, win_cols)
    stacked = jnp.pad(spread[:, 0], ((0, 1), (0, 0), (0, 0), (0, 0))) + jnp.pad(
        spread[:, 1], ((1, 0), (0, 0), (0, 0), (0, 0))
    )
    lower_piece = jnp.einsum("akpb,lp->akbl", stacked, column_table[:16], precision=precise)
    upper_piece = jnp.einsum("akpb,lp->akbl", stacked, column_table[16:], precision=precise)
    blocks = jnp.pad(lower_piece, ((0, 0), (0, 0), (0, 1), (0, 0))) + jnp.pad(
        upper_piece, ((0, 0), (0, 0), (1, 0), (0, 0))
    )
    return blocks.reshape(16 * (win_rows + 1), 16 * (win_cols + 1))


LANES = 128
WINDOWS_PER_TILE = LANES // 16
HALF = WINDOWS_PER_TILE * 32


def numpy_tables():
    positions = np.arange(32, dtype=np.float32)
    window = np.exp(np.float32(-0.5) * ((positions - np.float32(15.5)) / np.float32(8.0)) ** 2)
    phases = np.float32(2.0 * np.pi) * np.outer(positions, positions) / np.float32(32.0)
    scale = np.sqrt(np.float32(32.0))
    cos_part = np.cos(phases) * window[None, :] / scale
    sin_part = -np.sin(phases) * window[None, :] / scale
    return cos_part.astype(np.float32), sin_part.astype(np.float32)


def transform_tables(win_rows):
    cos_part, sin_part = numpy_tables()
    column_table = np.stack([cos_part.T, sin_part.T], axis=1)
    columns = np.zeros((2 * WINDOWS_PER_TILE, 16, 2, WINDOWS_PER_TILE, 32), np.float32)
    for k in range(WINDOWS_PER_TILE):
        columns[k, :, :, k] = column_table[:16]
        columns[k + 1, :, :, k] = column_table[16:]
    columns = columns.reshape(2 * LANES, 2 * HALF)
    blocks = win_rows + 1
    real = np.zeros((win_rows, 32, blocks * 16), np.float32)
    imag = np.zeros((win_rows, 32, blocks * 16), np.float32)
    for a in range(win_rows):
        real[a, :, 16 * a : 16 * a + 32] = cos_part
        imag[a, :, 16 * a : 16 * a + 32] = sin_part
    real = real.reshape(win_rows * 32, blocks * 16)
    imag = imag.reshape(win_rows * 32, blocks * 16)
    forward = np.concatenate([real, imag], axis=1)
    backward = np.concatenate([real.T, imag.T], axis=1)
    return [columns, forward, backward]


def split_constant(table):
    high = table.astype(jnp.bfloat16)
    low = (table - high.astype(np.float32)).astype(jnp.bfloat16)
    return [jnp.asarray(high), jnp.asarray(low)]


def split_value(value):
    high = value.astype(jnp.bfloat16)
    return high, (value - high.astype(jnp.float32)).astype(jnp.bfloat16)


def three_pass_dot(a, b):
    total = jnp.dot(a[0], b[1], preferred_element_type=jnp.float32)
    total += jnp.dot(a[1], b[0], preferred_element_type=jnp.float32)
    return total + jnp.dot(a[0], b[0], preferred_element_type=jnp.float32)


def transposed_dot(a, b):
    def one(x, y):
        return lax.dot_general(
            x, y, (((1,), (1,)), ((), ())), preferred_element_type=jnp.float32
        )
    return one(a[0], b[1]) + one(a[1], b[0]) + one(a[0], b[0])


def constant_first_dot(a, b):
    rows = a[0].shape[0]
    both = jnp.dot(
        jnp.concatenate([a[0], a[1]], axis=0), b[0], preferred_element_type=jnp.float32
    )
    total = jnp.dot(a[0], b[1], preferred_element_type=jnp.float32)
    total += both[rows:]
    return total + both[:rows]


def transform_kernel(
    x_ref, mh_ref, ml_ref, fh_ref, fl_ref, gh_ref, gl_ref, fw_ref, ww_ref,
    out_ref, y_ref, e_ref,
):
    rows = x_ref.shape[0]
    win_rows = rows // 16 - 1
    tiles = (x_ref.shape[1] - LANES) // LANES
    stacked_x = jnp.concatenate(
        [x_ref[:, t * LANES : (t + 2) * LANES] for t in range(tiles)], axis=0
    )
    y_ref[...] = three_pass_dot(split_value(stacked_x), (mh_ref[...], ml_ref[...]))
    forward = (fh_ref[...], fl_ref[...])
    backward = (gh_ref[...], gl_ref[...])
    freq = fw_ref[...]

    def one_tile(t, carry):
        here = pl.ds(pl.multiple_of(t * rows, 8), rows)
        y = y_ref[here, :]
        weights = ww_ref[:, pl.ds(pl.multiple_of(t * 2 * HALF, 2 * HALF), 2 * HALF)]
        turned = jnp.concatenate([-y[:, HALF:], y[:, :HALF]], axis=1)
        z = constant_first_dot(forward, split_value(jnp.concatenate([y, turned], axis=0)))
        spread = jnp.concatenate(
            [jnp.broadcast_to(weights[a : a + 1], (32, 2 * HALF)) for a in range(win_rows)],
            axis=0,
        )
        z = z * freq * spread
        turned = jnp.concatenate([z[:, HALF:], -z[:, :HALF]], axis=1)
        e_ref[here, :] = constant_first_dot(backward, split_value(jnp.concatenate([z, turned], axis=0)))
        return carry

    lax.fori_loop(0, tiles, one_tile, 0, unroll=True)
    pieces = transposed_dot(split_value(e_ref[...]), (mh_ref[...], ml_ref[...]))
    out_ref[...] = jnp.zeros_like(out_ref)
    for t in range(tiles):
        out_ref[:, t * LANES : (t + 2) * LANES] += pieces[t * rows : (t + 1) * rows]


def analyze_weigh_synthesize(region, window_weight, freq_weight):
    rows, cols = region.shape
    windows = (cols - 16) // 16
    tiles = -(-windows // WINDOWS_PER_TILE)
    wide = (tiles + 1) * LANES
    window_weight = jnp.pad(window_weight, ((0, 0), (0, tiles * WINDOWS_PER_TILE - windows)))
    padded = jnp.pad(region, ((0, 0), (0, wide - cols)))
    win_rows = rows // 16 - 1
    constants = []
    for table in transform_tables(win_rows):
        constants += split_constant(table)
    freq = jnp.broadcast_to(
        freq_weight.reshape(1, 32, 1, 1, 32), (win_rows, 32, 2, WINDOWS_PER_TILE, 32)
    ).reshape(win_rows * 32, 2 * HALF)
    weights = jnp.broadcast_to(
        window_weight.reshape(win_rows, tiles, 1, WINDOWS_PER_TILE, 1),
        (win_rows, tiles, 2, WINDOWS_PER_TILE, 32),
    ).reshape(win_rows, tiles * 2 * HALF)
    vmem = pl.BlockSpec(memory_space=pltpu.VMEM)
    out = pl.pallas_call(
        transform_kernel,
        out_shape=jax.ShapeDtypeStruct((rows, wide), jnp.float32),
        in_specs=[vmem] * 9,
        out_specs=vmem,
        scratch_shapes=[
            pltpu.VMEM((tiles * rows, 2 * HALF), jnp.float32),
            pltpu.VMEM((tiles * rows, 2 * HALF), jnp.float32),
        ],
    )(padded, *constants, freq, weights)
    return out[:, :cols]


def update_kernel(sums_ref, iterate_ref, residual_ref, direction_ref, applied_ref,
                  iterate_out, residual_out, direction_out):
    sums = sums_ref[...]
    norm_now, curvature, cross_term, image_norm = (sums[:, i : i + 1] for i in range(4))
    step_length = norm_now / curvature
    norm_next = norm_now - 2.0 * step_length * cross_term + step_length * step_length * image_norm
    ratio = norm_next / norm_now
    direction = direction_ref[...]
    iterate_out[...] = iterate_ref[...] + step_length * direction
    new_residual = residual_ref[...] - step_length * applied_ref[...]
    residual_out[...] = new_residual
    direction_out[...] = new_residual + ratio * direction


def updated(sums, iterate, residual, direction, applied):
    height, breadth = iterate.shape
    rows = 8
    block = pl.BlockSpec((rows, breadth), lambda i: (i, 0))
    shape = jax.ShapeDtypeStruct(iterate.shape, jnp.float32)
    return pl.pallas_call(
        update_kernel,
        grid=(height // rows,),
        out_shape=(shape, shape, shape),
        in_specs=[pl.BlockSpec((1, 4), lambda i: (0, 0))] + [block] * 4,
        out_specs=(block, block, block),
    )(sums, iterate, residual, direction, applied)


def per_device(iterate, residual, direction, window_weight, freq_weight):
    height, breadth = direction.shape
    rim_weight = jnp.pad(window_weight[:, -1:], ((0, 0), (0, 15)))
    from_left = passed_along(
        jnp.concatenate([direction[:, -16:], rim_weight], axis=0), COL, 1
    )
    from_right = passed_along(direction[:, :16], COL, -1)
    widened = jnp.concatenate([from_left[:height], direction, from_right], axis=1)
    weights_wide = jnp.concatenate([from_left[height:, :1], window_weight], axis=1)
    top_weight = jnp.pad(weights_wide[-1:], ((0, 0), (0, widened.shape[1] - weights_wide.shape[1])))
    from_above = passed_along(
        jnp.concatenate([widened[-16:], top_weight], axis=0), "row", 1
    )
    from_below = passed_along(widened[:16], "row", -1)
    region = jnp.concatenate([from_above[:16], widened, from_below], axis=0)
    weights_all = jnp.concatenate(
        [from_above[16:, : weights_wide.shape[1]], weights_wide], axis=0
    )
    spread = analyze_weigh_synthesize(region, weights_all, freq_weight)
    synthesized = spread[16 : 16 + height, 16 : 16 + breadth]
    applied = synthesized + damping * direction
    products = jnp.stack(
        [residual * residual, direction * applied, residual * applied, applied * applied]
    )
    sums = summed_everywhere(jnp.sum(products, axis=(1, 2)), DOUBLING)
    return updated(sums.reshape(1, 4), iterate, residual, direction, applied)


def solution(mesh):
    finer = Mesh(
        mesh.devices.reshape(mesh.shape["row"], 4, 4, 2, 2),
        ("row", "col_0", "col_1", "col_2", "col_3"),
    )
    return jax.shard_map(
        per_device,
        mesh=finer,
        in_specs=(P("row", COL), P("row", COL), P("row", COL), P("row", COL), P()),
        out_specs=(P("row", COL), P("row", COL), P("row", COL)),
        check_vma=False,
    )
```

```python
import jax
import numpy as np
import jax.numpy as jnp
from jax import lax
from jax.sharding import Mesh
from jax.sharding import PartitionSpec as P
from jax.experimental import pallas as pl
from jax.experimental.pallas import tpu as pltpu

COL = ("col_0", "col_1", "col_2", "col_3")
DOUBLING = (
    ("col_3", 1),
    ("row", 1),
    ("row", 2),
    ("col_0", 1),
    ("col_0", 2),
    ("col_1", 1),
    ("col_1", 2),
    ("col_2", 1),
)


precise = lax.Precision.HIGHEST
damping = 0.5


def passed_along(value, axis, steps):
    count = lax.axis_size(axis)
    leading, last = (max(0, -steps), min(count, count - steps))
    return lax.ppermute(value, axis, [(source, source + steps) for source in range(leading, last)])


def passed_diagonally(value, steps):
    rows, cols = lax.axis_size("row"), lax.axis_size(COL)
    pairs = [
        (r * cols + c, (r + steps) * cols + (c + steps))
        for r in range(max(0, -steps), min(rows, rows - steps))
        for c in range(max(0, -steps), min(cols, cols - steps))
    ]
    return lax.ppermute(value, ("row",) + COL, pairs)


def summed_everywhere(x, steps):
    for axis, mask in steps:
        count = lax.axis_size(axis)
        x = x + lax.ppermute(x, axis, [(i, i ^ mask) for i in range(count)])
    return x


def tables():
    positions = jnp.arange(32, dtype=jnp.float32)
    window = jnp.exp(-0.5 * ((positions - 15.5) / 8.0) ** 2)
    phases = 2.0 * jnp.pi * jnp.outer(positions, positions) / 32.0
    cos_part = jnp.cos(phases) * window[None, :] / jnp.sqrt(32.0)
    sin_part = -jnp.sin(phases) * window[None, :] / jnp.sqrt(32.0)
    column_table = jnp.concatenate([cos_part.T, sin_part.T], axis=1)
    cos_split = cos_part.reshape(32, 2, 16)
    sin_split = sin_part.reshape(32, 2, 16)
    upper = jnp.stack([cos_split, -sin_split], axis=-1)
    lower = jnp.stack([sin_split, cos_split], axis=-1)
    row_table = jnp.concatenate([upper, lower], axis=0).reshape(64, 64)
    return (column_table, row_table)


def analyze(region, column_table, row_table):
    win_rows = region.shape[0] // 16 - 1
    win_cols = region.shape[1] // 16 - 1
    blocks = region.reshape(win_rows + 1, 16, win_cols + 1, 16)
    section_one = jnp.einsum(
        "akbl,lp->akpb", blocks[:, :, :win_cols], column_table[:16], precision=precise
    )
    section_one = section_one + jnp.einsum(
        "akbl,lp->akpb", blocks[:, :, 1:], column_table[16:], precision=precise
    )
    section_one = section_one.reshape(win_rows + 1, 16, 2, 32, win_cols)
    paired = jnp.stack([section_one[:-1], section_one[1:]], axis=1).reshape(
        win_rows, 64, 32, win_cols
    )
    return jnp.einsum("tm,amvb->atvb", row_table, paired, precision=precise)


def weigh(coefficients, window_weight, freq_weight):
    doubled = jnp.concatenate([freq_weight, freq_weight], axis=0)
    return coefficients * doubled[None, :, :, None] * window_weight[:, None, None, :]


def synthesize(coefficients, column_table, row_table):
    win_rows = coefficients.shape[0]
    win_cols = coefficients.shape[3]
    spread = jnp.einsum("tm,atvb->amvb", row_table, coefficients, precision=precise)
    spread = spread.reshape(win_rows, 2, 16, 64, win_cols)
    stacked = jnp.pad(spread[:, 0], ((0, 1), (0, 0), (0, 0), (0, 0))) + jnp.pad(
        spread[:, 1], ((1, 0), (0, 0), (0, 0), (0, 0))
    )
    lower_piece = jnp.einsum("akpb,lp->akbl", stacked, column_table[:16], precision=precise)
    upper_piece = jnp.einsum("akpb,lp->akbl", stacked, column_table[16:], precision=precise)
    blocks = jnp.pad(lower_piece, ((0, 0), (0, 0), (0, 1), (0, 0))) + jnp.pad(
        upper_piece, ((0, 0), (0, 0), (1, 0), (0, 0))
    )
    return blocks.reshape(16 * (win_rows + 1), 16 * (win_cols + 1))


LANES = 128
UPDATE_ROWS = 32
WINDOWS_PER_TILE = LANES // 16
HALF = WINDOWS_PER_TILE * 32


def numpy_tables():
    positions = np.arange(32, dtype=np.float32)
    window = np.exp(np.float32(-0.5) * ((positions - np.float32(15.5)) / np.float32(8.0)) ** 2)
    phases = np.float32(2.0 * np.pi) * np.outer(positions, positions) / np.float32(32.0)
    scale = np.sqrt(np.float32(32.0))
    cos_part = np.cos(phases) * window[None, :] / scale
    sin_part = -np.sin(phases) * window[None, :] / scale
    return cos_part.astype(np.float32), sin_part.astype(np.float32)


def transform_tables(win_rows):
    cos_part, sin_part = numpy_tables()
    column_table = np.stack([cos_part.T, sin_part.T], axis=1)
    columns = np.zeros((2 * WINDOWS_PER_TILE, 16, 2, WINDOWS_PER_TILE, 32), np.float32)
    for k in range(WINDOWS_PER_TILE):
        columns[k, :, :, k] = column_table[:16]
        columns[k + 1, :, :, k] = column_table[16:]
    columns = columns.reshape(2 * LANES, 2 * HALF)
    blocks = win_rows + 1
    real = np.zeros((win_rows, 32, blocks * 16), np.float32)
    imag = np.zeros((win_rows, 32, blocks * 16), np.float32)
    for a in range(win_rows):
        real[a, :, 16 * a : 16 * a + 32] = cos_part
        imag[a, :, 16 * a : 16 * a + 32] = sin_part
    real = real.reshape(win_rows * 32, blocks * 16)
    imag = imag.reshape(win_rows * 32, blocks * 16)
    forward = np.concatenate([real, imag], axis=1)
    backward = np.concatenate([real.T, imag.T], axis=1)
    return [columns, forward, backward]


def split_constant(table):
    high = table.astype(jnp.bfloat16)
    low = (table - high.astype(np.float32)).astype(jnp.bfloat16)
    return [jnp.asarray(high), jnp.asarray(low)]


def split_value(value):
    high = value.astype(jnp.bfloat16)
    return high, (value - high.astype(jnp.float32)).astype(jnp.bfloat16)


def three_pass_dot(a, b):
    total = jnp.dot(a[0], b[1], preferred_element_type=jnp.float32)
    total += jnp.dot(a[1], b[0], preferred_element_type=jnp.float32)
    return total + jnp.dot(a[0], b[0], preferred_element_type=jnp.float32)


def transposed_dot(a, b):
    def one(x, y):
        return lax.dot_general(
            x, y, (((1,), (1,)), ((), ())), preferred_element_type=jnp.float32
        )
    return one(a[0], b[1]) + one(a[1], b[0]) + one(a[0], b[0])


def constant_first_dot(a, b):
    rows = a[0].shape[0]
    both = jnp.dot(
        jnp.concatenate([a[0], a[1]], axis=0), b[0], preferred_element_type=jnp.float32
    )
    total = jnp.dot(a[0], b[1], preferred_element_type=jnp.float32)
    total += both[rows:]
    return total + both[:rows]


def transform_kernel(
    x_ref, mh_ref, ml_ref, fh_ref, fl_ref, gh_ref, gl_ref, fw_ref, ww_ref,
    out_ref, y_ref, e_ref,
):
    rows = x_ref.shape[0]
    win_rows = rows // 16 - 1
    tiles = (x_ref.shape[1] - LANES) // LANES
    stacked_x = jnp.concatenate(
        [x_ref[:, t * LANES : (t + 2) * LANES] for t in range(tiles)], axis=0
    )
    y_ref[...] = three_pass_dot(split_value(stacked_x), (mh_ref[...], ml_ref[...]))
    forward = (fh_ref[...], fl_ref[...])
    backward = (gh_ref[...], gl_ref[...])
    freq = fw_ref[...]

    def one_tile(t, carry):
        here = pl.ds(pl.multiple_of(t * rows, 8), rows)
        y = y_ref[here, :]
        weights = ww_ref[:, pl.ds(pl.multiple_of(t * 2 * HALF, 2 * HALF), 2 * HALF)]
        turned = jnp.concatenate([-y[:, HALF:], y[:, :HALF]], axis=1)
        z = constant_first_dot(forward, split_value(jnp.concatenate([y, turned], axis=0)))
        spread = jnp.concatenate(
            [jnp.broadcast_to(weights[a : a + 1], (32, 2 * HALF)) for a in range(win_rows)],
            axis=0,
        )
        z = z * freq * spread
        turned = jnp.concatenate([z[:, HALF:], -z[:, :HALF]], axis=1)
        e_ref[here, :] = constant_first_dot(backward, split_value(jnp.concatenate([z, turned], axis=0)))
        return carry

    lax.fori_loop(0, tiles, one_tile, 0, unroll=True)
    pieces = transposed_dot(split_value(e_ref[...]), (mh_ref[...], ml_ref[...]))
    out_ref[...] = jnp.zeros_like(out_ref)
    for t in range(tiles):
        out_ref[:, t * LANES : (t + 2) * LANES] += pieces[t * rows : (t + 1) * rows]


def analyze_weigh_synthesize(region, window_weight, freq_weight):
    rows, cols = region.shape
    windows = (cols - 16) // 16
    tiles = -(-windows // WINDOWS_PER_TILE)
    wide = (tiles + 1) * LANES
    window_weight = jnp.pad(window_weight, ((0, 0), (0, tiles * WINDOWS_PER_TILE - windows)))
    padded = jnp.pad(region, ((0, 0), (0, wide - cols)))
    win_rows = rows // 16 - 1
    constants = []
    for table in transform_tables(win_rows):
        constants += split_constant(table)
    freq = jnp.broadcast_to(
        freq_weight.reshape(1, 32, 1, 1, 32), (win_rows, 32, 2, WINDOWS_PER_TILE, 32)
    ).reshape(win_rows * 32, 2 * HALF)
    weights = jnp.broadcast_to(
        window_weight.reshape(win_rows, tiles, 1, WINDOWS_PER_TILE, 1),
        (win_rows, tiles, 2, WINDOWS_PER_TILE, 32),
    ).reshape(win_rows, tiles * 2 * HALF)
    vmem = pl.BlockSpec(memory_space=pltpu.VMEM)
    out = pl.pallas_call(
        transform_kernel,
        out_shape=jax.ShapeDtypeStruct((rows, wide), jnp.float32),
        in_specs=[vmem] * 9,
        out_specs=vmem,
        scratch_shapes=[
            pltpu.VMEM((tiles * rows, 2 * HALF), jnp.float32),
            pltpu.VMEM((tiles * rows, 2 * HALF), jnp.float32),
        ],
    )(padded, *constants, freq, weights)
    return out[:, :cols]


def update_kernel(sums_ref, iterate_ref, residual_ref, direction_ref, applied_ref,
                  iterate_out, residual_out, direction_out):
    sums = sums_ref[...]
    norm_now, curvature, cross_term, image_norm = (sums[:, i : i + 1] for i in range(4))
    step_length = norm_now / curvature
    norm_next = norm_now - 2.0 * step_length * cross_term + step_length * step_length * image_norm
    ratio = norm_next / norm_now
    direction = direction_ref[...]
    iterate_out[...] = iterate_ref[...] + step_length * direction
    new_residual = residual_ref[...] - step_length * applied_ref[...]
    residual_out[...] = new_residual
    direction_out[...] = new_residual + ratio * direction


def updated(sums, iterate, residual, direction, applied):
    height, breadth = iterate.shape
    rows = UPDATE_ROWS
    block = pl.BlockSpec((rows, breadth), lambda i: (i, 0))
    shape = jax.ShapeDtypeStruct(iterate.shape, jnp.float32)
    return pl.pallas_call(
        update_kernel,
        grid=(height // rows,),
        out_shape=(shape, shape, shape),
        in_specs=[pl.BlockSpec((1, 4), lambda i: (0, 0))] + [block] * 4,
        out_specs=(block, block, block),
    )(sums, iterate, residual, direction, applied)


def per_device(iterate, residual, direction, window_weight, freq_weight):
    height, breadth = direction.shape
    rim_weight = jnp.pad(window_weight[:, -1:], ((0, 0), (0, 15)))
    from_left = passed_along(
        jnp.concatenate([direction[:, -16:], rim_weight], axis=0), COL, 1
    )
    from_right = passed_along(direction[:, :16], COL, -1)
    widened = jnp.concatenate([from_left[:height], direction, from_right], axis=1)
    weights_wide = jnp.concatenate([from_left[height:, :1], window_weight], axis=1)
    top_weight = jnp.pad(weights_wide[-1:], ((0, 0), (0, widened.shape[1] - weights_wide.shape[1])))
    from_above = passed_along(
        jnp.concatenate([widened[-16:], top_weight], axis=0), "row", 1
    )
    from_below = passed_along(widened[:16], "row", -1)
    region = jnp.concatenate([from_above[:16], widened, from_below], axis=0)
    weights_all = jnp.concatenate(
        [from_above[16:, : weights_wide.shape[1]], weights_wide], axis=0
    )
    spread = analyze_weigh_synthesize(region, weights_all, freq_weight)
    synthesized = spread[16 : 16 + height, 16 : 16 + breadth]
    applied = synthesized + damping * direction
    products = jnp.stack(
        [residual * residual, direction * applied, residual * applied, applied * applied]
    )
    sums = summed_everywhere(jnp.sum(products, axis=(1, 2)), DOUBLING)
    return updated(sums.reshape(1, 4), iterate, residual, direction, applied)


def solution(mesh):
    finer = Mesh(
        mesh.devices.reshape(mesh.shape["row"], 4, 4, 2, 2),
        ("row", "col_0", "col_1", "col_2", "col_3"),
    )
    return jax.shard_map(
        per_device,
        mesh=finer,
        in_specs=(P("row", COL), P("row", COL), P("row", COL), P("row", COL), P()),
        out_specs=(P("row", COL), P("row", COL), P("row", COL)),
        check_vma=False,
    )
```

```python
import jax
import numpy as np
import jax.numpy as jnp
from jax import lax
from jax.sharding import Mesh
from jax.sharding import PartitionSpec as P
from jax.experimental import pallas as pl
from jax.experimental.pallas import tpu as pltpu

COL = ("col_0", "col_1", "col_2", "col_3")
DOUBLING = (
    ("col_3", 1),
    ("row", 1),
    ("row", 2),
    ("col_0", 1),
    ("col_0", 2),
    ("col_1", 1),
    ("col_1", 2),
    ("col_2", 1),
)


precise = lax.Precision.HIGHEST
damping = 0.5


def passed_along(value, axis, steps):
    count = lax.axis_size(axis)
    leading, last = (max(0, -steps), min(count, count - steps))
    return lax.ppermute(value, axis, [(source, source + steps) for source in range(leading, last)])


def passed_diagonally(value, steps):
    rows, cols = lax.axis_size("row"), lax.axis_size(COL)
    pairs = [
        (r * cols + c, (r + steps) * cols + (c + steps))
        for r in range(max(0, -steps), min(rows, rows - steps))
        for c in range(max(0, -steps), min(cols, cols - steps))
    ]
    return lax.ppermute(value, ("row",) + COL, pairs)


def summed_everywhere(x, steps):
    for axis, mask in steps:
        count = lax.axis_size(axis)
        x = x + lax.ppermute(x, axis, [(i, i ^ mask) for i in range(count)])
    return x


def tables():
    positions = jnp.arange(32, dtype=jnp.float32)
    window = jnp.exp(-0.5 * ((positions - 15.5) / 8.0) ** 2)
    phases = 2.0 * jnp.pi * jnp.outer(positions, positions) / 32.0
    cos_part = jnp.cos(phases) * window[None, :] / jnp.sqrt(32.0)
    sin_part = -jnp.sin(phases) * window[None, :] / jnp.sqrt(32.0)
    column_table = jnp.concatenate([cos_part.T, sin_part.T], axis=1)
    cos_split = cos_part.reshape(32, 2, 16)
    sin_split = sin_part.reshape(32, 2, 16)
    upper = jnp.stack([cos_split, -sin_split], axis=-1)
    lower = jnp.stack([sin_split, cos_split], axis=-1)
    row_table = jnp.concatenate([upper, lower], axis=0).reshape(64, 64)
    return (column_table, row_table)


def analyze(region, column_table, row_table):
    win_rows = region.shape[0] // 16 - 1
    win_cols = region.shape[1] // 16 - 1
    blocks = region.reshape(win_rows + 1, 16, win_cols + 1, 16)
    section_one = jnp.einsum(
        "akbl,lp->akpb", blocks[:, :, :win_cols], column_table[:16], precision=precise
    )
    section_one = section_one + jnp.einsum(
        "akbl,lp->akpb", blocks[:, :, 1:], column_table[16:], precision=precise
    )
    section_one = section_one.reshape(win_rows + 1, 16, 2, 32, win_cols)
    paired = jnp.stack([section_one[:-1], section_one[1:]], axis=1).reshape(
        win_rows, 64, 32, win_cols
    )
    return jnp.einsum("tm,amvb->atvb", row_table, paired, precision=precise)


def weigh(coefficients, window_weight, freq_weight):
    doubled = jnp.concatenate([freq_weight, freq_weight], axis=0)
    return coefficients * doubled[None, :, :, None] * window_weight[:, None, None, :]


def synthesize(coefficients, column_table, row_table):
    win_rows = coefficients.shape[0]
    win_cols = coefficients.shape[3]
    spread = jnp.einsum("tm,atvb->amvb", row_table, coefficients, precision=precise)
    spread = spread.reshape(win_rows, 2, 16, 64, win_cols)
    stacked = jnp.pad(spread[:, 0], ((0, 1), (0, 0), (0, 0), (0, 0))) + jnp.pad(
        spread[:, 1], ((1, 0), (0, 0), (0, 0), (0, 0))
    )
    lower_piece = jnp.einsum("akpb,lp->akbl", stacked, column_table[:16], precision=precise)
    upper_piece = jnp.einsum("akpb,lp->akbl", stacked, column_table[16:], precision=precise)
    blocks = jnp.pad(lower_piece, ((0, 0), (0, 0), (0, 1), (0, 0))) + jnp.pad(
        upper_piece, ((0, 0), (0, 0), (1, 0), (0, 0))
    )
    return blocks.reshape(16 * (win_rows + 1), 16 * (win_cols + 1))


LANES = 128
UPDATE_ROWS = 32
WINDOWS_PER_TILE = LANES // 16
HALF = WINDOWS_PER_TILE * 32


def numpy_tables():
    positions = np.arange(32, dtype=np.float32)
    window = np.exp(np.float32(-0.5) * ((positions - np.float32(15.5)) / np.float32(8.0)) ** 2)
    phases = np.float32(2.0 * np.pi) * np.outer(positions, positions) / np.float32(32.0)
    scale = np.sqrt(np.float32(32.0))
    cos_part = np.cos(phases) * window[None, :] / scale
    sin_part = -np.sin(phases) * window[None, :] / scale
    return cos_part.astype(np.float32), sin_part.astype(np.float32)


def transform_tables(win_rows):
    cos_part, sin_part = numpy_tables()
    column_table = np.stack([cos_part.T, sin_part.T], axis=1)
    columns = np.zeros((2 * WINDOWS_PER_TILE, 16, 2, WINDOWS_PER_TILE, 32), np.float32)
    for k in range(WINDOWS_PER_TILE):
        columns[k, :, :, k] = column_table[:16]
        columns[k + 1, :, :, k] = column_table[16:]
    columns = columns.reshape(2 * LANES, 2 * HALF)
    blocks = win_rows + 1
    real = np.zeros((win_rows, 32, blocks * 16), np.float32)
    imag = np.zeros((win_rows, 32, blocks * 16), np.float32)
    for a in range(win_rows):
        real[a, :, 16 * a : 16 * a + 32] = cos_part
        imag[a, :, 16 * a : 16 * a + 32] = sin_part
    real = real.reshape(win_rows * 32, blocks * 16)
    imag = imag.reshape(win_rows * 32, blocks * 16)
    forward = np.concatenate([real, imag], axis=1)
    backward = np.concatenate([real.T, imag.T], axis=1)
    return [columns, forward, backward]


def split_constant(table):
    high = table.astype(jnp.bfloat16)
    low = (table - high.astype(np.float32)).astype(jnp.bfloat16)
    return [jnp.asarray(high), jnp.asarray(low)]


def split_value(value):
    high = value.astype(jnp.bfloat16)
    return high, (value - high.astype(jnp.float32)).astype(jnp.bfloat16)


def three_pass_dot(a, b):
    total = jnp.dot(a[0], b[1], preferred_element_type=jnp.float32)
    total += jnp.dot(a[1], b[0], preferred_element_type=jnp.float32)
    return total + jnp.dot(a[0], b[0], preferred_element_type=jnp.float32)


def transposed_dot(a, b):
    def one(x, y):
        return lax.dot_general(
            x, y, (((1,), (1,)), ((), ())), preferred_element_type=jnp.float32
        )
    return one(a[0], b[1]) + one(a[1], b[0]) + one(a[0], b[0])


def constant_first_dot(a, b):
    rows = a[0].shape[0]
    both = jnp.dot(
        jnp.concatenate([a[0], a[1]], axis=0), b[0], preferred_element_type=jnp.float32
    )
    total = jnp.dot(a[0], b[1], preferred_element_type=jnp.float32)
    total += both[rows:]
    return total + both[:rows]


def transform_kernel(
    above_ref, middle_ref, below_ref, mh_ref, ml_ref, fh_ref, fl_ref, gh_ref, gl_ref, fw_ref,
    ww_ref, out_ref, y_ref, e_ref,
):
    x = jnp.concatenate([above_ref[:16], middle_ref[...], below_ref[...]], axis=0)
    rows = x.shape[0]
    win_rows = rows // 16 - 1
    tiles = (x.shape[1] - LANES) // LANES
    stacked_x = jnp.concatenate(
        [x[:, t * LANES : (t + 2) * LANES] for t in range(tiles)], axis=0
    )
    y_ref[...] = three_pass_dot(split_value(stacked_x), (mh_ref[...], ml_ref[...]))
    forward = (fh_ref[...], fl_ref[...])
    backward = (gh_ref[...], gl_ref[...])
    freq = fw_ref[...]

    def one_tile(t, carry):
        here = pl.ds(pl.multiple_of(t * rows, 8), rows)
        y = y_ref[here, :]
        weights = ww_ref[:, pl.ds(pl.multiple_of(t * 2 * HALF, 2 * HALF), 2 * HALF)]
        turned = jnp.concatenate([-y[:, HALF:], y[:, :HALF]], axis=1)
        z = constant_first_dot(forward, split_value(jnp.concatenate([y, turned], axis=0)))
        spread = jnp.concatenate(
            [jnp.broadcast_to(weights[a : a + 1], (32, 2 * HALF)) for a in range(win_rows)],
            axis=0,
        )
        z = z * freq * spread
        turned = jnp.concatenate([z[:, HALF:], -z[:, :HALF]], axis=1)
        e_ref[here, :] = constant_first_dot(backward, split_value(jnp.concatenate([z, turned], axis=0)))
        return carry

    lax.fori_loop(0, tiles, one_tile, 0, unroll=True)
    pieces = transposed_dot(split_value(e_ref[...]), (mh_ref[...], ml_ref[...]))
    out_ref[...] = jnp.zeros_like(out_ref)
    for t in range(tiles):
        out_ref[:, t * LANES : (t + 2) * LANES] += pieces[t * rows : (t + 1) * rows]


def padded_width(cols):
    windows = (cols - 16) // 16
    return (-(-windows // WINDOWS_PER_TILE) + 1) * LANES


def analyze_weigh_synthesize(above, middle, below, window_weight, freq_weight, cols):
    rows = middle.shape[0] + 32
    windows = (cols - 16) // 16
    tiles = -(-windows // WINDOWS_PER_TILE)
    wide = (tiles + 1) * LANES
    window_weight = jnp.pad(window_weight, ((0, 0), (0, tiles * WINDOWS_PER_TILE - windows)))
    win_rows = rows // 16 - 1
    constants = []
    for table in transform_tables(win_rows):
        constants += split_constant(table)
    freq = jnp.broadcast_to(
        freq_weight.reshape(1, 32, 1, 1, 32), (win_rows, 32, 2, WINDOWS_PER_TILE, 32)
    ).reshape(win_rows * 32, 2 * HALF)
    weights = jnp.broadcast_to(
        window_weight.reshape(win_rows, tiles, 1, WINDOWS_PER_TILE, 1),
        (win_rows, tiles, 2, WINDOWS_PER_TILE, 32),
    ).reshape(win_rows, tiles * 2 * HALF)
    vmem = pl.BlockSpec(memory_space=pltpu.VMEM)
    out = pl.pallas_call(
        transform_kernel,
        out_shape=jax.ShapeDtypeStruct((rows, wide), jnp.float32),
        in_specs=[vmem] * 11,
        out_specs=vmem,
        scratch_shapes=[
            pltpu.VMEM((tiles * rows, 2 * HALF), jnp.float32),
            pltpu.VMEM((tiles * rows, 2 * HALF), jnp.float32),
        ],
    )(above, middle, below, *constants, freq, weights)
    return out[:, :cols]


def update_kernel(sums_ref, iterate_ref, residual_ref, direction_ref, applied_ref,
                  iterate_out, residual_out, direction_out):
    sums = sums_ref[...]
    norm_now, curvature, cross_term, image_norm = (sums[:, i : i + 1] for i in range(4))
    step_length = norm_now / curvature
    norm_next = norm_now - 2.0 * step_length * cross_term + step_length * step_length * image_norm
    ratio = norm_next / norm_now
    direction = direction_ref[...]
    iterate_out[...] = iterate_ref[...] + step_length * direction
    new_residual = residual_ref[...] - step_length * applied_ref[...]
    residual_out[...] = new_residual
    direction_out[...] = new_residual + ratio * direction


def updated(sums, iterate, residual, direction, applied):
    height, breadth = iterate.shape
    rows = UPDATE_ROWS
    block = pl.BlockSpec((rows, breadth), lambda i: (i, 0))
    shape = jax.ShapeDtypeStruct(iterate.shape, jnp.float32)
    return pl.pallas_call(
        update_kernel,
        grid=(height // rows,),
        out_shape=(shape, shape, shape),
        in_specs=[pl.BlockSpec((1, 4), lambda i: (0, 0))] + [block] * 4,
        out_specs=(block, block, block),
    )(sums, iterate, residual, direction, applied)


def per_device(iterate, residual, direction, window_weight, freq_weight):
    height, breadth = direction.shape
    rim_weight = jnp.pad(window_weight[:, -1:], ((0, 0), (0, 15)))
    from_left = passed_along(
        jnp.concatenate([direction[:, -16:], rim_weight], axis=0), COL, 1
    )
    from_right = passed_along(direction[:, :16], COL, -1)
    cols = breadth + 32
    wide = padded_width(cols)
    widened = jnp.concatenate(
        [from_left[:height], direction, from_right, jnp.zeros((height, wide - cols), jnp.float32)],
        axis=1,
    )
    weights_wide = jnp.concatenate([from_left[height:, :1], window_weight], axis=1)
    top_weight = jnp.pad(weights_wide[-1:], ((0, 0), (0, widened.shape[1] - weights_wide.shape[1])))
    from_above = passed_along(
        jnp.concatenate([widened[-16:], top_weight], axis=0), "row", 1
    )
    from_below = passed_along(widened[:16], "row", -1)
    weights_all = jnp.concatenate(
        [from_above[16:, : weights_wide.shape[1]], weights_wide], axis=0
    )
    spread = analyze_weigh_synthesize(
        from_above, widened, from_below, weights_all, freq_weight, cols
    )
    synthesized = spread[16 : 16 + height, 16 : 16 + breadth]
    applied = synthesized + damping * direction
    products = jnp.stack(
        [residual * residual, direction * applied, residual * applied, applied * applied]
    )
    sums = summed_everywhere(jnp.sum(products, axis=(1, 2)), DOUBLING)
    return updated(sums.reshape(1, 4), iterate, residual, direction, applied)


def solution(mesh):
    finer = Mesh(
        mesh.devices.reshape(mesh.shape["row"], 4, 4, 2, 2),
        ("row", "col_0", "col_1", "col_2", "col_3"),
    )
    return jax.shard_map(
        per_device,
        mesh=finer,
        in_specs=(P("row", COL), P("row", COL), P("row", COL), P("row", COL), P()),
        out_specs=(P("row", COL), P("row", COL), P("row", COL)),
        check_vma=False,
    )
```

```python
import jax
import numpy as np
import jax.numpy as jnp
from jax import lax
from jax.sharding import Mesh
from jax.sharding import PartitionSpec as P
from jax.experimental import pallas as pl
from jax.experimental.pallas import tpu as pltpu

COL = ("col_0", "col_1", "col_2", "col_3")
DOUBLING = (
    ("col_3", 1),
    ("row", 1),
    ("row", 2),
    ("col_0", 1),
    ("col_0", 2),
    ("col_1", 1),
    ("col_1", 2),
    ("col_2", 1),
)


precise = lax.Precision.HIGHEST
damping = 0.5


def passed_along(value, axis, steps):
    count = lax.axis_size(axis)
    leading, last = (max(0, -steps), min(count, count - steps))
    return lax.ppermute(value, axis, [(source, source + steps) for source in range(leading, last)])


def passed_diagonally(value, steps):
    rows, cols = lax.axis_size("row"), lax.axis_size(COL)
    pairs = [
        (r * cols + c, (r + steps) * cols + (c + steps))
        for r in range(max(0, -steps), min(rows, rows - steps))
        for c in range(max(0, -steps), min(cols, cols - steps))
    ]
    return lax.ppermute(value, ("row",) + COL, pairs)


def summed_everywhere(x, steps):
    for axis, mask in steps:
        count = lax.axis_size(axis)
        x = x + lax.ppermute(x, axis, [(i, i ^ mask) for i in range(count)])
    return x


def tables():
    positions = jnp.arange(32, dtype=jnp.float32)
    window = jnp.exp(-0.5 * ((positions - 15.5) / 8.0) ** 2)
    phases = 2.0 * jnp.pi * jnp.outer(positions, positions) / 32.0
    cos_part = jnp.cos(phases) * window[None, :] / jnp.sqrt(32.0)
    sin_part = -jnp.sin(phases) * window[None, :] / jnp.sqrt(32.0)
    column_table = jnp.concatenate([cos_part.T, sin_part.T], axis=1)
    cos_split = cos_part.reshape(32, 2, 16)
    sin_split = sin_part.reshape(32, 2, 16)
    upper = jnp.stack([cos_split, -sin_split], axis=-1)
    lower = jnp.stack([sin_split, cos_split], axis=-1)
    row_table = jnp.concatenate([upper, lower], axis=0).reshape(64, 64)
    return (column_table, row_table)


def analyze(region, column_table, row_table):
    win_rows = region.shape[0] // 16 - 1
    win_cols = region.shape[1] // 16 - 1
    blocks = region.reshape(win_rows + 1, 16, win_cols + 1, 16)
    section_one = jnp.einsum(
        "akbl,lp->akpb", blocks[:, :, :win_cols], column_table[:16], precision=precise
    )
    section_one = section_one + jnp.einsum(
        "akbl,lp->akpb", blocks[:, :, 1:], column_table[16:], precision=precise
    )
    section_one = section_one.reshape(win_rows + 1, 16, 2, 32, win_cols)
    paired = jnp.stack([section_one[:-1], section_one[1:]], axis=1).reshape(
        win_rows, 64, 32, win_cols
    )
    return jnp.einsum("tm,amvb->atvb", row_table, paired, precision=precise)


def weigh(coefficients, window_weight, freq_weight):
    doubled = jnp.concatenate([freq_weight, freq_weight], axis=0)
    return coefficients * doubled[None, :, :, None] * window_weight[:, None, None, :]


def synthesize(coefficients, column_table, row_table):
    win_rows = coefficients.shape[0]
    win_cols = coefficients.shape[3]
    spread = jnp.einsum("tm,atvb->amvb", row_table, coefficients, precision=precise)
    spread = spread.reshape(win_rows, 2, 16, 64, win_cols)
    stacked = jnp.pad(spread[:, 0], ((0, 1), (0, 0), (0, 0), (0, 0))) + jnp.pad(
        spread[:, 1], ((1, 0), (0, 0), (0, 0), (0, 0))
    )
    lower_piece = jnp.einsum("akpb,lp->akbl", stacked, column_table[:16], precision=precise)
    upper_piece = jnp.einsum("akpb,lp->akbl", stacked, column_table[16:], precision=precise)
    blocks = jnp.pad(lower_piece, ((0, 0), (0, 0), (0, 1), (0, 0))) + jnp.pad(
        upper_piece, ((0, 0), (0, 0), (1, 0), (0, 0))
    )
    return blocks.reshape(16 * (win_rows + 1), 16 * (win_cols + 1))


LANES = 128
UPDATE_ROWS = 32
WINDOWS_PER_TILE = LANES // 16
HALF = WINDOWS_PER_TILE * 32


def numpy_tables():
    positions = np.arange(32, dtype=np.float32)
    window = np.exp(np.float32(-0.5) * ((positions - np.float32(15.5)) / np.float32(8.0)) ** 2)
    phases = np.float32(2.0 * np.pi) * np.outer(positions, positions) / np.float32(32.0)
    scale = np.sqrt(np.float32(32.0))
    cos_part = np.cos(phases) * window[None, :] / scale
    sin_part = -np.sin(phases) * window[None, :] / scale
    return cos_part.astype(np.float32), sin_part.astype(np.float32)


def transform_tables(win_rows):
    cos_part, sin_part = numpy_tables()
    column_table = np.stack([cos_part.T, sin_part.T], axis=1)
    columns = np.zeros((2 * WINDOWS_PER_TILE, 16, 2, WINDOWS_PER_TILE, 32), np.float32)
    for k in range(WINDOWS_PER_TILE):
        columns[k, :, :, k] = column_table[:16]
        columns[k + 1, :, :, k] = column_table[16:]
    columns = columns.reshape(2 * LANES, 2 * HALF)
    blocks = win_rows + 1
    real = np.zeros((win_rows, 32, blocks * 16), np.float32)
    imag = np.zeros((win_rows, 32, blocks * 16), np.float32)
    for a in range(win_rows):
        real[a, :, 16 * a : 16 * a + 32] = cos_part
        imag[a, :, 16 * a : 16 * a + 32] = sin_part
    real = real.reshape(win_rows * 32, blocks * 16)
    imag = imag.reshape(win_rows * 32, blocks * 16)
    forward = np.concatenate([real, imag], axis=1)
    backward = np.concatenate([real.T, imag.T], axis=1)
    return [columns, forward, backward]


def split_constant(table):
    high = table.astype(jnp.bfloat16)
    low = (table - high.astype(np.float32)).astype(jnp.bfloat16)
    return [jnp.asarray(high), jnp.asarray(low)]


def split_value(value):
    high = value.astype(jnp.bfloat16)
    return high, (value - high.astype(jnp.float32)).astype(jnp.bfloat16)


def three_pass_dot(a, b):
    total = jnp.dot(a[0], b[1], preferred_element_type=jnp.float32)
    total += jnp.dot(a[1], b[0], preferred_element_type=jnp.float32)
    return total + jnp.dot(a[0], b[0], preferred_element_type=jnp.float32)


def transposed_dot(a, b):
    def one(x, y):
        return lax.dot_general(
            x, y, (((1,), (1,)), ((), ())), preferred_element_type=jnp.float32
        )
    return one(a[0], b[1]) + one(a[1], b[0]) + one(a[0], b[0])


def constant_first_dot(a, b):
    rows = a[0].shape[0]
    both = jnp.dot(
        jnp.concatenate([a[0], a[1]], axis=0), b[0], preferred_element_type=jnp.float32
    )
    total = jnp.dot(a[0], b[1], preferred_element_type=jnp.float32)
    total += both[rows:]
    return total + both[:rows]


def transform_kernel(
    above_ref, middle_ref, below_ref, mh_ref, ml_ref, fh_ref, fl_ref, gh_ref, gl_ref, fw_ref,
    ww_ref, out_ref, y_ref, e_ref,
):
    x = jnp.concatenate([above_ref[:16], middle_ref[...], below_ref[...]], axis=0)
    rows = x.shape[0]
    win_rows = rows // 16 - 1
    tiles = (x.shape[1] - LANES) // LANES
    stacked_x = jnp.concatenate(
        [x[:, t * LANES : (t + 2) * LANES] for t in range(tiles)], axis=0
    )
    y_ref[...] = three_pass_dot(split_value(stacked_x), (mh_ref[...], ml_ref[...]))
    forward = (fh_ref[...], fl_ref[...])
    backward = (gh_ref[...], gl_ref[...])
    freq = fw_ref[...]

    def one_tile(t, carry):
        here = pl.ds(pl.multiple_of(t * rows, 8), rows)
        y = y_ref[here, :]
        weights = ww_ref[:, pl.ds(pl.multiple_of(t * 2 * HALF, 2 * HALF), 2 * HALF)]
        turned = jnp.concatenate([-y[:, HALF:], y[:, :HALF]], axis=1)
        z = constant_first_dot(forward, split_value(jnp.concatenate([y, turned], axis=0)))
        spread = jnp.concatenate(
            [jnp.broadcast_to(weights[a : a + 1], (32, 2 * HALF)) for a in range(win_rows)],
            axis=0,
        )
        z = z * freq * spread
        turned = jnp.concatenate([z[:, HALF:], -z[:, :HALF]], axis=1)
        e_ref[here, :] = constant_first_dot(backward, split_value(jnp.concatenate([z, turned], axis=0)))
        return carry

    lax.fori_loop(0, tiles, one_tile, 0, unroll=True)
    pieces = transposed_dot(split_value(e_ref[...]), (mh_ref[...], ml_ref[...]))
    out_ref[...] = jnp.zeros_like(out_ref)
    for t in range(tiles):
        out_ref[:, t * LANES : (t + 2) * LANES] += pieces[t * rows : (t + 1) * rows]


def padded_width(cols):
    windows = (cols - 16) // 16
    return (-(-windows // WINDOWS_PER_TILE) + 1) * LANES


def analyze_weigh_synthesize(above, middle, below, window_weight, freq_weight, cols):
    rows = middle.shape[0] + 32
    windows = (cols - 16) // 16
    tiles = -(-windows // WINDOWS_PER_TILE)
    wide = (tiles + 1) * LANES
    window_weight = jnp.pad(window_weight, ((0, 0), (0, tiles * WINDOWS_PER_TILE - windows)))
    win_rows = rows // 16 - 1
    constants = []
    for table in transform_tables(win_rows):
        constants += split_constant(table)
    freq = jnp.broadcast_to(
        freq_weight.reshape(1, 32, 1, 1, 32), (win_rows, 32, 2, WINDOWS_PER_TILE, 32)
    ).reshape(win_rows * 32, 2 * HALF)
    weights = jnp.broadcast_to(
        window_weight.reshape(win_rows, tiles, 1, WINDOWS_PER_TILE, 1),
        (win_rows, tiles, 2, WINDOWS_PER_TILE, 32),
    ).reshape(win_rows, tiles * 2 * HALF)
    vmem = pl.BlockSpec(memory_space=pltpu.VMEM)
    out = pl.pallas_call(
        transform_kernel,
        out_shape=jax.ShapeDtypeStruct((rows, wide), jnp.float32),
        in_specs=[vmem] * 11,
        out_specs=vmem,
        scratch_shapes=[
            pltpu.VMEM((tiles * rows, 2 * HALF), jnp.float32),
            pltpu.VMEM((tiles * rows, 2 * HALF), jnp.float32),
        ],
    )(above, middle, below, *constants, freq, weights)
    return out[:, :cols]


def update_kernel(sums_ref, iterate_ref, residual_ref, direction_ref, applied_ref,
                  iterate_out, residual_out, direction_out):
    sums = sums_ref[...]
    norm_now, curvature, cross_term, image_norm = (sums[:, i : i + 1] for i in range(4))
    step_length = norm_now / curvature
    norm_next = norm_now - 2.0 * step_length * cross_term + step_length * step_length * image_norm
    ratio = norm_next / norm_now
    direction = direction_ref[...]
    iterate_out[...] = iterate_ref[...] + step_length * direction
    new_residual = residual_ref[...] - step_length * applied_ref[...]
    residual_out[...] = new_residual
    direction_out[...] = new_residual + ratio * direction


def updated(sums, iterate, residual, direction, applied):
    height, breadth = iterate.shape
    rows = UPDATE_ROWS
    block = pl.BlockSpec((rows, breadth), lambda i: (i, 0))
    shape = jax.ShapeDtypeStruct(iterate.shape, jnp.float32)
    return pl.pallas_call(
        update_kernel,
        grid=(height // rows,),
        out_shape=(shape, shape, shape),
        in_specs=[pl.BlockSpec((1, 4), lambda i: (0, 0))] + [block] * 4,
        out_specs=(block, block, block),
    )(sums, iterate, residual, direction, applied)


def per_device(iterate, residual, direction, window_weight, freq_weight):
    height, breadth = direction.shape
    count = window_weight.shape[1]
    rim_weight = jnp.pad(window_weight[:, -1:], ((0, 0), (0, 15)))
    from_left = passed_along(
        jnp.concatenate([direction[:, -16:], rim_weight], axis=0), COL, 1
    )
    from_right = passed_along(direction[:, :16], COL, -1)
    top_weight = jnp.pad(window_weight[-1:], ((0, 0), (0, breadth - count)))
    from_above = passed_along(jnp.concatenate([direction[-16:], top_weight], axis=0), "row", 1)
    from_below = passed_along(direction[:16], "row", -1)
    corner_weight = jnp.pad(from_left[-1:, :1], ((0, 0), (0, 31)))
    upper_corners = passed_along(
        jnp.concatenate(
            [jnp.concatenate([from_left[height - 16 : height], from_right[-16:]], axis=1), corner_weight],
            axis=0,
        ),
        "row",
        1,
    )
    lower_corners = passed_along(
        jnp.concatenate([from_left[:16], from_right[:16]], axis=1), "row", -1
    )
    cols = breadth + 32
    wide = padded_width(cols)
    def band(left, middle, right):
        rows = middle.shape[0]
        return jnp.concatenate(
            [left, middle, right, jnp.zeros((rows, wide - cols), jnp.float32)], axis=1
        )
    widened = band(from_left[:height], direction, from_right)
    above = band(upper_corners[:16, :16], from_above[:16], upper_corners[:16, 16:])
    below = band(lower_corners[:, :16], from_below, lower_corners[:, 16:])
    weights_all = jnp.concatenate(
        [
            jnp.concatenate([upper_corners[16:, :1], from_above[16:, :count]], axis=1),
            jnp.concatenate([from_left[height:, :1], window_weight], axis=1),
        ],
        axis=0,
    )
    spread = analyze_weigh_synthesize(above, widened, below, weights_all, freq_weight, cols)
    synthesized = spread[16 : 16 + height, 16 : 16 + breadth]
    applied = synthesized + damping * direction
    products = jnp.stack(
        [residual * residual, direction * applied, residual * applied, applied * applied]
    )
    sums = summed_everywhere(jnp.sum(products, axis=(1, 2)), DOUBLING)
    return updated(sums.reshape(1, 4), iterate, residual, direction, applied)


def solution(mesh):
    finer = Mesh(
        mesh.devices.reshape(mesh.shape["row"], 4, 4, 2, 2),
        ("row", "col_0", "col_1", "col_2", "col_3"),
    )
    return jax.shard_map(
        per_device,
        mesh=finer,
        in_specs=(P("row", COL), P("row", COL), P("row", COL), P("row", COL), P()),
        out_specs=(P("row", COL), P("row", COL), P("row", COL)),
        check_vma=False,
    )
```

```python
import jax
import numpy as np
import jax.numpy as jnp
from jax import lax
from jax.sharding import Mesh
from jax.sharding import PartitionSpec as P
from jax.experimental import pallas as pl
from jax.experimental.pallas import tpu as pltpu

COL = ("col_0", "col_1", "col_2", "col_3")
DOUBLING = (
    ("col_3", 1),
    ("row", 1),
    ("row", 2),
    ("col_0", 1),
    ("col_0", 2),
    ("col_1", 1),
    ("col_1", 2),
    ("col_2", 1),
)


precise = lax.Precision.HIGHEST
damping = 0.5


def passed_along(value, axis, steps):
    count = lax.axis_size(axis)
    leading, last = (max(0, -steps), min(count, count - steps))
    return lax.ppermute(value, axis, [(source, source + steps) for source in range(leading, last)])


def passed_diagonally(value, steps):
    rows, cols = lax.axis_size("row"), lax.axis_size(COL)
    pairs = [
        (r * cols + c, (r + steps) * cols + (c + steps))
        for r in range(max(0, -steps), min(rows, rows - steps))
        for c in range(max(0, -steps), min(cols, cols - steps))
    ]
    return lax.ppermute(value, ("row",) + COL, pairs)


def summed_everywhere(x, steps):
    for axis, mask in steps:
        count = lax.axis_size(axis)
        x = x + lax.ppermute(x, axis, [(i, i ^ mask) for i in range(count)])
    return x


def tables():
    positions = jnp.arange(32, dtype=jnp.float32)
    window = jnp.exp(-0.5 * ((positions - 15.5) / 8.0) ** 2)
    phases = 2.0 * jnp.pi * jnp.outer(positions, positions) / 32.0
    cos_part = jnp.cos(phases) * window[None, :] / jnp.sqrt(32.0)
    sin_part = -jnp.sin(phases) * window[None, :] / jnp.sqrt(32.0)
    column_table = jnp.concatenate([cos_part.T, sin_part.T], axis=1)
    cos_split = cos_part.reshape(32, 2, 16)
    sin_split = sin_part.reshape(32, 2, 16)
    upper = jnp.stack([cos_split, -sin_split], axis=-1)
    lower = jnp.stack([sin_split, cos_split], axis=-1)
    row_table = jnp.concatenate([upper, lower], axis=0).reshape(64, 64)
    return (column_table, row_table)


def analyze(region, column_table, row_table):
    win_rows = region.shape[0] // 16 - 1
    win_cols = region.shape[1] // 16 - 1
    blocks = region.reshape(win_rows + 1, 16, win_cols + 1, 16)
    section_one = jnp.einsum(
        "akbl,lp->akpb", blocks[:, :, :win_cols], column_table[:16], precision=precise
    )
    section_one = section_one + jnp.einsum(
        "akbl,lp->akpb", blocks[:, :, 1:], column_table[16:], precision=precise
    )
    section_one = section_one.reshape(win_rows + 1, 16, 2, 32, win_cols)
    paired = jnp.stack([section_one[:-1], section_one[1:]], axis=1).reshape(
        win_rows, 64, 32, win_cols
    )
    return jnp.einsum("tm,amvb->atvb", row_table, paired, precision=precise)


def weigh(coefficients, window_weight, freq_weight):
    doubled = jnp.concatenate([freq_weight, freq_weight], axis=0)
    return coefficients * doubled[None, :, :, None] * window_weight[:, None, None, :]


def synthesize(coefficients, column_table, row_table):
    win_rows = coefficients.shape[0]
    win_cols = coefficients.shape[3]
    spread = jnp.einsum("tm,atvb->amvb", row_table, coefficients, precision=precise)
    spread = spread.reshape(win_rows, 2, 16, 64, win_cols)
    stacked = jnp.pad(spread[:, 0], ((0, 1), (0, 0), (0, 0), (0, 0))) + jnp.pad(
        spread[:, 1], ((1, 0), (0, 0), (0, 0), (0, 0))
    )
    lower_piece = jnp.einsum("akpb,lp->akbl", stacked, column_table[:16], precision=precise)
    upper_piece = jnp.einsum("akpb,lp->akbl", stacked, column_table[16:], precision=precise)
    blocks = jnp.pad(lower_piece, ((0, 0), (0, 0), (0, 1), (0, 0))) + jnp.pad(
        upper_piece, ((0, 0), (0, 0), (1, 0), (0, 0))
    )
    return blocks.reshape(16 * (win_rows + 1), 16 * (win_cols + 1))


LANES = 128
UPDATE_ROWS = 32
TILE_GROUP = 6
WINDOWS_PER_TILE = LANES // 16
HALF = WINDOWS_PER_TILE * 32


def numpy_tables():
    positions = np.arange(32, dtype=np.float32)
    window = np.exp(np.float32(-0.5) * ((positions - np.float32(15.5)) / np.float32(8.0)) ** 2)
    phases = np.float32(2.0 * np.pi) * np.outer(positions, positions) / np.float32(32.0)
    scale = np.sqrt(np.float32(32.0))
    cos_part = np.cos(phases) * window[None, :] / scale
    sin_part = -np.sin(phases) * window[None, :] / scale
    return cos_part.astype(np.float32), sin_part.astype(np.float32)


def transform_tables(win_rows):
    cos_part, sin_part = numpy_tables()
    column_table = np.stack([cos_part.T, sin_part.T], axis=1)
    columns = np.zeros((2 * WINDOWS_PER_TILE, 16, 2, WINDOWS_PER_TILE, 32), np.float32)
    for k in range(WINDOWS_PER_TILE):
        columns[k, :, :, k] = column_table[:16]
        columns[k + 1, :, :, k] = column_table[16:]
    columns = columns.reshape(2 * LANES, 2 * HALF)
    blocks = win_rows + 1
    real = np.zeros((win_rows, 32, blocks * 16), np.float32)
    imag = np.zeros((win_rows, 32, blocks * 16), np.float32)
    for a in range(win_rows):
        real[a, :, 16 * a : 16 * a + 32] = cos_part
        imag[a, :, 16 * a : 16 * a + 32] = sin_part
    real = real.reshape(win_rows * 32, blocks * 16)
    imag = imag.reshape(win_rows * 32, blocks * 16)
    forward = np.concatenate([real, imag], axis=1)
    backward = np.concatenate([real.T, imag.T], axis=1)
    return [columns, forward, backward]


def split_constant(table):
    high = table.astype(jnp.bfloat16)
    low = (table - high.astype(np.float32)).astype(jnp.bfloat16)
    return [jnp.asarray(high), jnp.asarray(low)]


def split_value(value):
    high = value.astype(jnp.bfloat16)
    return high, (value - high.astype(jnp.float32)).astype(jnp.bfloat16)


def three_pass_dot(a, b):
    total = jnp.dot(a[0], b[1], preferred_element_type=jnp.float32)
    total += jnp.dot(a[1], b[0], preferred_element_type=jnp.float32)
    return total + jnp.dot(a[0], b[0], preferred_element_type=jnp.float32)


def transposed_dot(a, b):
    def one(x, y):
        return lax.dot_general(
            x, y, (((1,), (1,)), ((), ())), preferred_element_type=jnp.float32
        )
    return one(a[0], b[1]) + one(a[1], b[0]) + one(a[0], b[0])


def constant_first_dot(a, b):
    rows = a[0].shape[0]
    both = jnp.dot(
        jnp.concatenate([a[0], a[1]], axis=0), b[0], preferred_element_type=jnp.float32
    )
    total = jnp.dot(a[0], b[1], preferred_element_type=jnp.float32)
    total += both[rows:]
    return total + both[:rows]


def transform_kernel(
    above_ref, middle_ref, below_ref, mh_ref, ml_ref, fh_ref, fl_ref, gh_ref, gl_ref, fw_ref,
    ww_ref, out_ref, y_ref, e_ref,
):
    x = jnp.concatenate([above_ref[:16], middle_ref[...], below_ref[...]], axis=0)
    rows = x.shape[0]
    win_rows = rows // 16 - 1
    tiles = (x.shape[1] - LANES) // LANES
    stacked_x = jnp.concatenate(
        [x[:, t * LANES : (t + 2) * LANES] for t in range(tiles)], axis=0
    )
    y_ref[...] = three_pass_dot(split_value(stacked_x), (mh_ref[...], ml_ref[...]))
    forward = (fh_ref[...], fl_ref[...])
    backward = (gh_ref[...], gl_ref[...])
    freq = fw_ref[...]

    def turn(value, sign):
        blocks = []
        for g in range(value.shape[1] // (2 * HALF)):
            re = value[:, 2 * HALF * g : 2 * HALF * g + HALF]
            im = value[:, 2 * HALF * g + HALF : 2 * HALF * (g + 1)]
            blocks += [-im, re] if sign else [im, -re]
        return jnp.concatenate(blocks, axis=1)

    for first in range(0, tiles, TILE_GROUP):
        group = range(first, min(first + TILE_GROUP, tiles))
        y = jnp.concatenate([y_ref[t * rows : (t + 1) * rows, :] for t in group], axis=1)
        weights = ww_ref[:, first * 2 * HALF : (group[-1] + 1) * 2 * HALF]
        z = constant_first_dot(forward, split_value(jnp.concatenate([y, turn(y, True)], axis=0)))
        spread = jnp.concatenate(
            [jnp.broadcast_to(weights[a : a + 1], (32, weights.shape[1])) for a in range(win_rows)],
            axis=0,
        )
        z = z * jnp.concatenate([freq] * len(group), axis=1) * spread
        e = constant_first_dot(backward, split_value(jnp.concatenate([z, turn(z, False)], axis=0)))
        for g, t in enumerate(group):
            e_ref[t * rows : (t + 1) * rows, :] = e[:, 2 * HALF * g : 2 * HALF * (g + 1)]
    pieces = transposed_dot(split_value(e_ref[...]), (mh_ref[...], ml_ref[...]))
    out_ref[...] = jnp.zeros_like(out_ref)
    for t in range(tiles):
        out_ref[:, t * LANES : (t + 2) * LANES] += pieces[t * rows : (t + 1) * rows]


def padded_width(cols):
    windows = (cols - 16) // 16
    return (-(-windows // WINDOWS_PER_TILE) + 1) * LANES


def analyze_weigh_synthesize(above, middle, below, window_weight, freq_weight, cols):
    rows = middle.shape[0] + 32
    windows = (cols - 16) // 16
    tiles = -(-windows // WINDOWS_PER_TILE)
    wide = (tiles + 1) * LANES
    window_weight = jnp.pad(window_weight, ((0, 0), (0, tiles * WINDOWS_PER_TILE - windows)))
    win_rows = rows // 16 - 1
    constants = []
    for table in transform_tables(win_rows):
        constants += split_constant(table)
    freq = jnp.broadcast_to(
        freq_weight.reshape(1, 32, 1, 1, 32), (win_rows, 32, 2, WINDOWS_PER_TILE, 32)
    ).reshape(win_rows * 32, 2 * HALF)
    weights = jnp.broadcast_to(
        window_weight.reshape(win_rows, tiles, 1, WINDOWS_PER_TILE, 1),
        (win_rows, tiles, 2, WINDOWS_PER_TILE, 32),
    ).reshape(win_rows, tiles * 2 * HALF)
    vmem = pl.BlockSpec(memory_space=pltpu.VMEM)
    out = pl.pallas_call(
        transform_kernel,
        out_shape=jax.ShapeDtypeStruct((rows, wide), jnp.float32),
        in_specs=[vmem] * 11,
        out_specs=vmem,
        scratch_shapes=[
            pltpu.VMEM((tiles * rows, 2 * HALF), jnp.float32),
            pltpu.VMEM((tiles * rows, 2 * HALF), jnp.float32),
        ],
    )(above, middle, below, *constants, freq, weights)
    return out[:, :cols]


def update_kernel(sums_ref, iterate_ref, residual_ref, direction_ref, applied_ref,
                  iterate_out, residual_out, direction_out):
    sums = sums_ref[...]
    norm_now, curvature, cross_term, image_norm = (sums[:, i : i + 1] for i in range(4))
    step_length = norm_now / curvature
    norm_next = norm_now - 2.0 * step_length * cross_term + step_length * step_length * image_norm
    ratio = norm_next / norm_now
    direction = direction_ref[...]
    iterate_out[...] = iterate_ref[...] + step_length * direction
    new_residual = residual_ref[...] - step_length * applied_ref[...]
    residual_out[...] = new_residual
    direction_out[...] = new_residual + ratio * direction


def updated(sums, iterate, residual, direction, applied):
    height, breadth = iterate.shape
    rows = UPDATE_ROWS
    block = pl.BlockSpec((rows, breadth), lambda i: (i, 0))
    shape = jax.ShapeDtypeStruct(iterate.shape, jnp.float32)
    return pl.pallas_call(
        update_kernel,
        grid=(height // rows,),
        out_shape=(shape, shape, shape),
        in_specs=[pl.BlockSpec((1, 4), lambda i: (0, 0))] + [block] * 4,
        out_specs=(block, block, block),
    )(sums, iterate, residual, direction, applied)


def per_device(iterate, residual, direction, window_weight, freq_weight):
    height, breadth = direction.shape
    rim_weight = jnp.pad(window_weight[:, -1:], ((0, 0), (0, 15)))
    from_left = passed_along(
        jnp.concatenate([direction[:, -16:], rim_weight], axis=0), COL, 1
    )
    from_right = passed_along(direction[:, :16], COL, -1)
    cols = breadth + 32
    wide = padded_width(cols)
    widened = jnp.concatenate(
        [from_left[:height], direction, from_right, jnp.zeros((height, wide - cols), jnp.float32)],
        axis=1,
    )
    weights_wide = jnp.concatenate([from_left[height:, :1], window_weight], axis=1)
    top_weight = jnp.pad(weights_wide[-1:], ((0, 0), (0, widened.shape[1] - weights_wide.shape[1])))
    from_above = passed_along(
        jnp.concatenate([widened[-16:], top_weight], axis=0), "row", 1
    )
    from_below = passed_along(widened[:16], "row", -1)
    weights_all = jnp.concatenate(
        [from_above[16:, : weights_wide.shape[1]], weights_wide], axis=0
    )
    spread = analyze_weigh_synthesize(
        from_above, widened, from_below, weights_all, freq_weight, cols
    )
    synthesized = spread[16 : 16 + height, 16 : 16 + breadth]
    applied = synthesized + damping * direction
    products = jnp.stack(
        [residual * residual, direction * applied, residual * applied, applied * applied]
    )
    sums = summed_everywhere(jnp.sum(products, axis=(1, 2)), DOUBLING)
    return updated(sums.reshape(1, 4), iterate, residual, direction, applied)


def solution(mesh):
    finer = Mesh(
        mesh.devices.reshape(mesh.shape["row"], 4, 4, 2, 2),
        ("row", "col_0", "col_1", "col_2", "col_3"),
    )
    return jax.shard_map(
        per_device,
        mesh=finer,
        in_specs=(P("row", COL), P("row", COL), P("row", COL), P("row", COL), P()),
        out_specs=(P("row", COL), P("row", COL), P("row", COL)),
        check_vma=False,
    )
```

```python
import jax
import numpy as np
import jax.numpy as jnp
from jax import lax
from jax.sharding import Mesh
from jax.sharding import PartitionSpec as P
from jax.experimental import pallas as pl
from jax.experimental.pallas import tpu as pltpu

COL = ("col_0", "col_1", "col_2", "col_3")
DOUBLING = (
    ("col_3", 1),
    ("row", 1),
    ("row", 2),
    ("col_0", 1),
    ("col_0", 2),
    ("col_1", 1),
    ("col_1", 2),
    ("col_2", 1),
)


precise = lax.Precision.HIGHEST
damping = 0.5


def passed_along(value, axis, steps):
    count = lax.axis_size(axis)
    leading, last = (max(0, -steps), min(count, count - steps))
    return lax.ppermute(value, axis, [(source, source + steps) for source in range(leading, last)])


def passed_diagonally(value, steps):
    rows, cols = lax.axis_size("row"), lax.axis_size(COL)
    pairs = [
        (r * cols + c, (r + steps) * cols + (c + steps))
        for r in range(max(0, -steps), min(rows, rows - steps))
        for c in range(max(0, -steps), min(cols, cols - steps))
    ]
    return lax.ppermute(value, ("row",) + COL, pairs)


def summed_everywhere(x, steps):
    for axis, mask in steps:
        count = lax.axis_size(axis)
        x = x + lax.ppermute(x, axis, [(i, i ^ mask) for i in range(count)])
    return x


def tables():
    positions = jnp.arange(32, dtype=jnp.float32)
    window = jnp.exp(-0.5 * ((positions - 15.5) / 8.0) ** 2)
    phases = 2.0 * jnp.pi * jnp.outer(positions, positions) / 32.0
    cos_part = jnp.cos(phases) * window[None, :] / jnp.sqrt(32.0)
    sin_part = -jnp.sin(phases) * window[None, :] / jnp.sqrt(32.0)
    column_table = jnp.concatenate([cos_part.T, sin_part.T], axis=1)
    cos_split = cos_part.reshape(32, 2, 16)
    sin_split = sin_part.reshape(32, 2, 16)
    upper = jnp.stack([cos_split, -sin_split], axis=-1)
    lower = jnp.stack([sin_split, cos_split], axis=-1)
    row_table = jnp.concatenate([upper, lower], axis=0).reshape(64, 64)
    return (column_table, row_table)


def analyze(region, column_table, row_table):
    win_rows = region.shape[0] // 16 - 1
    win_cols = region.shape[1] // 16 - 1
    blocks = region.reshape(win_rows + 1, 16, win_cols + 1, 16)
    section_one = jnp.einsum(
        "akbl,lp->akpb", blocks[:, :, :win_cols], column_table[:16], precision=precise
    )
    section_one = section_one + jnp.einsum(
        "akbl,lp->akpb", blocks[:, :, 1:], column_table[16:], precision=precise
    )
    section_one = section_one.reshape(win_rows + 1, 16, 2, 32, win_cols)
    paired = jnp.stack([section_one[:-1], section_one[1:]], axis=1).reshape(
        win_rows, 64, 32, win_cols
    )
    return jnp.einsum("tm,amvb->atvb", row_table, paired, precision=precise)


def weigh(coefficients, window_weight, freq_weight):
    doubled = jnp.concatenate([freq_weight, freq_weight], axis=0)
    return coefficients * doubled[None, :, :, None] * window_weight[:, None, None, :]


def synthesize(coefficients, column_table, row_table):
    win_rows = coefficients.shape[0]
    win_cols = coefficients.shape[3]
    spread = jnp.einsum("tm,atvb->amvb", row_table, coefficients, precision=precise)
    spread = spread.reshape(win_rows, 2, 16, 64, win_cols)
    stacked = jnp.pad(spread[:, 0], ((0, 1), (0, 0), (0, 0), (0, 0))) + jnp.pad(
        spread[:, 1], ((1, 0), (0, 0), (0, 0), (0, 0))
    )
    lower_piece = jnp.einsum("akpb,lp->akbl", stacked, column_table[:16], precision=precise)
    upper_piece = jnp.einsum("akpb,lp->akbl", stacked, column_table[16:], precision=precise)
    blocks = jnp.pad(lower_piece, ((0, 0), (0, 0), (0, 1), (0, 0))) + jnp.pad(
        upper_piece, ((0, 0), (0, 0), (1, 0), (0, 0))
    )
    return blocks.reshape(16 * (win_rows + 1), 16 * (win_cols + 1))


LANES = 128
UPDATE_ROWS = 32
TILE_GROUP = 6
WINDOWS_PER_TILE = LANES // 16
HALF = WINDOWS_PER_TILE * 32


def numpy_tables():
    positions = np.arange(32, dtype=np.float32)
    window = np.exp(np.float32(-0.5) * ((positions - np.float32(15.5)) / np.float32(8.0)) ** 2)
    phases = np.float32(2.0 * np.pi) * np.outer(positions, positions) / np.float32(32.0)
    scale = np.sqrt(np.float32(32.0))
    cos_part = np.cos(phases) * window[None, :] / scale
    sin_part = -np.sin(phases) * window[None, :] / scale
    return cos_part.astype(np.float32), sin_part.astype(np.float32)


def transform_tables(win_rows):
    cos_part, sin_part = numpy_tables()
    column_table = np.stack([cos_part.T, sin_part.T], axis=1)
    columns = np.zeros((2 * WINDOWS_PER_TILE, 16, 2, WINDOWS_PER_TILE, 32), np.float32)
    for k in range(WINDOWS_PER_TILE):
        columns[k, :, :, k] = column_table[:16]
        columns[k + 1, :, :, k] = column_table[16:]
    columns = columns.reshape(2 * LANES, 2 * HALF)
    blocks = win_rows + 1
    real = np.zeros((win_rows, 32, blocks * 16), np.float32)
    imag = np.zeros((win_rows, 32, blocks * 16), np.float32)
    for a in range(win_rows):
        real[a, :, 16 * a : 16 * a + 32] = cos_part
        imag[a, :, 16 * a : 16 * a + 32] = sin_part
    real = real.reshape(win_rows * 32, blocks * 16)
    imag = imag.reshape(win_rows * 32, blocks * 16)
    forward = np.concatenate([real, imag], axis=1)
    backward = np.concatenate([real.T, imag.T], axis=1)
    return [columns, forward, backward]


def split_constant(table):
    high = table.astype(jnp.bfloat16)
    low = (table - high.astype(np.float32)).astype(jnp.bfloat16)
    return [jnp.asarray(high), jnp.asarray(low)]


def split_value(value):
    high = value.astype(jnp.bfloat16)
    return high, (value - high.astype(jnp.float32)).astype(jnp.bfloat16)


def three_pass_dot(a, b):
    total = jnp.dot(a[0], b[1], preferred_element_type=jnp.float32)
    total += jnp.dot(a[1], b[0], preferred_element_type=jnp.float32)
    return total + jnp.dot(a[0], b[0], preferred_element_type=jnp.float32)


def transposed_dot(a, b):
    def one(x, y):
        return lax.dot_general(
            x, y, (((1,), (1,)), ((), ())), preferred_element_type=jnp.float32
        )
    return one(a[0], b[1]) + one(a[1], b[0]) + one(a[0], b[0])


def constant_first_dot(a, b):
    rows = a[0].shape[0]
    both = jnp.dot(
        jnp.concatenate([a[0], a[1]], axis=0), b[0], preferred_element_type=jnp.float32
    )
    total = jnp.dot(a[0], b[1], preferred_element_type=jnp.float32)
    total += both[rows:]
    return total + both[:rows]


def transform_kernel(
    above_ref, middle_ref, below_ref, mh_ref, ml_ref, fh_ref, fl_ref, gh_ref, gl_ref, fw_ref,
    ww_ref, out_ref, y_ref, e_ref,
):
    x = jnp.concatenate([above_ref[:16], middle_ref[...], below_ref[...]], axis=0)
    rows = x.shape[0]
    win_rows = rows // 16 - 1
    tiles = (x.shape[1] - LANES) // LANES
    stacked_x = jnp.concatenate(
        [x[:, t * LANES : (t + 2) * LANES] for t in range(tiles)], axis=0
    )
    y_ref[...] = three_pass_dot(split_value(stacked_x), (mh_ref[...], ml_ref[...]))
    forward = (fh_ref[...], fl_ref[...])
    backward = (gh_ref[...], gl_ref[...])
    freq = fw_ref[...]

    def turn(value, sign):
        blocks = []
        for g in range(value.shape[1] // (2 * HALF)):
            re = value[:, 2 * HALF * g : 2 * HALF * g + HALF]
            im = value[:, 2 * HALF * g + HALF : 2 * HALF * (g + 1)]
            blocks += [-im, re] if sign else [im, -re]
        return jnp.concatenate(blocks, axis=1)

    for first in range(0, tiles, TILE_GROUP):
        group = range(first, min(first + TILE_GROUP, tiles))
        y = jnp.concatenate([y_ref[t * rows : (t + 1) * rows, :] for t in group], axis=1)
        weights = ww_ref[:, first * 2 * HALF : (group[-1] + 1) * 2 * HALF]
        z = constant_first_dot(forward, split_value(jnp.concatenate([y, turn(y, True)], axis=0)))
        spread = jnp.concatenate(
            [jnp.broadcast_to(weights[a : a + 1], (32, weights.shape[1])) for a in range(win_rows)],
            axis=0,
        )
        z = z * jnp.concatenate([freq] * len(group), axis=1) * spread
        e = constant_first_dot(backward, split_value(jnp.concatenate([z, turn(z, False)], axis=0)))
        for g, t in enumerate(group):
            e_ref[t * rows : (t + 1) * rows, :] = e[:, 2 * HALF * g : 2 * HALF * (g + 1)]
    pieces = transposed_dot(split_value(e_ref[...]), (mh_ref[...], ml_ref[...]))
    kept = out_ref.shape[0]
    out_ref[...] = jnp.zeros_like(out_ref)
    for t in range(tiles):
        out_ref[:, t * LANES : (t + 2) * LANES] += pieces[t * rows + 16 : t * rows + 16 + kept]


def padded_width(cols):
    windows = (cols - 16) // 16
    return (-(-windows // WINDOWS_PER_TILE) + 1) * LANES


def analyze_weigh_synthesize(above, middle, below, window_weight, freq_weight, cols):
    rows = middle.shape[0] + 32
    windows = (cols - 16) // 16
    tiles = -(-windows // WINDOWS_PER_TILE)
    wide = (tiles + 1) * LANES
    window_weight = jnp.pad(window_weight, ((0, 0), (0, tiles * WINDOWS_PER_TILE - windows)))
    win_rows = rows // 16 - 1
    constants = []
    for table in transform_tables(win_rows):
        constants += split_constant(table)
    freq = jnp.broadcast_to(
        freq_weight.reshape(1, 32, 1, 1, 32), (win_rows, 32, 2, WINDOWS_PER_TILE, 32)
    ).reshape(win_rows * 32, 2 * HALF)
    weights = jnp.broadcast_to(
        window_weight.reshape(win_rows, tiles, 1, WINDOWS_PER_TILE, 1),
        (win_rows, tiles, 2, WINDOWS_PER_TILE, 32),
    ).reshape(win_rows, tiles * 2 * HALF)
    vmem = pl.BlockSpec(memory_space=pltpu.VMEM)
    out = pl.pallas_call(
        transform_kernel,
        out_shape=jax.ShapeDtypeStruct((rows - 32, wide), jnp.float32),
        in_specs=[vmem] * 11,
        out_specs=vmem,
        scratch_shapes=[
            pltpu.VMEM((tiles * rows, 2 * HALF), jnp.float32),
            pltpu.VMEM((tiles * rows, 2 * HALF), jnp.float32),
        ],
    )(above, middle, below, *constants, freq, weights)
    return out[:, :cols]


def update_kernel(sums_ref, iterate_ref, residual_ref, direction_ref, applied_ref,
                  iterate_out, residual_out, direction_out):
    sums = sums_ref[...]
    norm_now, curvature, cross_term, image_norm = (sums[:, i : i + 1] for i in range(4))
    step_length = norm_now / curvature
    norm_next = norm_now - 2.0 * step_length * cross_term + step_length * step_length * image_norm
    ratio = norm_next / norm_now
    direction = direction_ref[...]
    iterate_out[...] = iterate_ref[...] + step_length * direction
    new_residual = residual_ref[...] - step_length * applied_ref[...]
    residual_out[...] = new_residual
    direction_out[...] = new_residual + ratio * direction


def updated(sums, iterate, residual, direction, applied):
    height, breadth = iterate.shape
    rows = UPDATE_ROWS
    block = pl.BlockSpec((rows, breadth), lambda i: (i, 0))
    shape = jax.ShapeDtypeStruct(iterate.shape, jnp.float32)
    return pl.pallas_call(
        update_kernel,
        grid=(height // rows,),
        out_shape=(shape, shape, shape),
        in_specs=[pl.BlockSpec((1, 4), lambda i: (0, 0))] + [block] * 4,
        out_specs=(block, block, block),
    )(sums, iterate, residual, direction, applied)


def per_device(iterate, residual, direction, window_weight, freq_weight):
    height, breadth = direction.shape
    rim_weight = jnp.pad(window_weight[:, -1:], ((0, 0), (0, 15)))
    from_left = passed_along(
        jnp.concatenate([direction[:, -16:], rim_weight], axis=0), COL, 1
    )
    from_right = passed_along(direction[:, :16], COL, -1)
    cols = breadth + 32
    wide = padded_width(cols)
    widened = jnp.concatenate(
        [from_left[:height], direction, from_right, jnp.zeros((height, wide - cols), jnp.float32)],
        axis=1,
    )
    weights_wide = jnp.concatenate([from_left[height:, :1], window_weight], axis=1)
    top_weight = jnp.pad(weights_wide[-1:], ((0, 0), (0, widened.shape[1] - weights_wide.shape[1])))
    from_above = passed_along(
        jnp.concatenate([widened[-16:], top_weight], axis=0), "row", 1
    )
    from_below = passed_along(widened[:16], "row", -1)
    weights_all = jnp.concatenate(
        [from_above[16:, : weights_wide.shape[1]], weights_wide], axis=0
    )
    spread = analyze_weigh_synthesize(
        from_above, widened, from_below, weights_all, freq_weight, cols
    )
    synthesized = spread[:, 16 : 16 + breadth]
    applied = synthesized + damping * direction
    products = jnp.stack(
        [residual * residual, direction * applied, residual * applied, applied * applied]
    )
    sums = summed_everywhere(jnp.sum(products, axis=(1, 2)), DOUBLING)
    return updated(sums.reshape(1, 4), iterate, residual, direction, applied)


def solution(mesh):
    finer = Mesh(
        mesh.devices.reshape(mesh.shape["row"], 4, 4, 2, 2),
        ("row", "col_0", "col_1", "col_2", "col_3"),
    )
    return jax.shard_map(
        per_device,
        mesh=finer,
        in_specs=(P("row", COL), P("row", COL), P("row", COL), P("row", COL), P()),
        out_specs=(P("row", COL), P("row", COL), P("row", COL)),
        check_vma=False,
    )
```

```python
import jax
import numpy as np
import jax.numpy as jnp
from jax import lax
from jax.sharding import Mesh
from jax.sharding import PartitionSpec as P
from jax.experimental import pallas as pl
from jax.experimental.pallas import tpu as pltpu

COL = ("col_0", "col_1", "col_2", "col_3")
DOUBLING = (
    ("col_3", 1),
    ("row", 1),
    ("row", 2),
    ("col_0", 1),
    ("col_0", 2),
    ("col_1", 1),
    ("col_1", 2),
    ("col_2", 1),
)


precise = lax.Precision.HIGHEST
damping = 0.5


def passed_along(value, axis, steps):
    count = lax.axis_size(axis)
    leading, last = (max(0, -steps), min(count, count - steps))
    return lax.ppermute(value, axis, [(source, source + steps) for source in range(leading, last)])


def passed_diagonally(value, steps):
    rows, cols = lax.axis_size("row"), lax.axis_size(COL)
    pairs = [
        (r * cols + c, (r + steps) * cols + (c + steps))
        for r in range(max(0, -steps), min(rows, rows - steps))
        for c in range(max(0, -steps), min(cols, cols - steps))
    ]
    return lax.ppermute(value, ("row",) + COL, pairs)


def summed_everywhere(x, steps):
    for axis, mask in steps:
        count = lax.axis_size(axis)
        x = x + lax.ppermute(x, axis, [(i, i ^ mask) for i in range(count)])
    return x


def tables():
    positions = jnp.arange(32, dtype=jnp.float32)
    window = jnp.exp(-0.5 * ((positions - 15.5) / 8.0) ** 2)
    phases = 2.0 * jnp.pi * jnp.outer(positions, positions) / 32.0
    cos_part = jnp.cos(phases) * window[None, :] / jnp.sqrt(32.0)
    sin_part = -jnp.sin(phases) * window[None, :] / jnp.sqrt(32.0)
    column_table = jnp.concatenate([cos_part.T, sin_part.T], axis=1)
    cos_split = cos_part.reshape(32, 2, 16)
    sin_split = sin_part.reshape(32, 2, 16)
    upper = jnp.stack([cos_split, -sin_split], axis=-1)
    lower = jnp.stack([sin_split, cos_split], axis=-1)
    row_table = jnp.concatenate([upper, lower], axis=0).reshape(64, 64)
    return (column_table, row_table)


def analyze(region, column_table, row_table):
    win_rows = region.shape[0] // 16 - 1
    win_cols = region.shape[1] // 16 - 1
    blocks = region.reshape(win_rows + 1, 16, win_cols + 1, 16)
    section_one = jnp.einsum(
        "akbl,lp->akpb", blocks[:, :, :win_cols], column_table[:16], precision=precise
    )
    section_one = section_one + jnp.einsum(
        "akbl,lp->akpb", blocks[:, :, 1:], column_table[16:], precision=precise
    )
    section_one = section_one.reshape(win_rows + 1, 16, 2, 32, win_cols)
    paired = jnp.stack([section_one[:-1], section_one[1:]], axis=1).reshape(
        win_rows, 64, 32, win_cols
    )
    return jnp.einsum("tm,amvb->atvb", row_table, paired, precision=precise)


def weigh(coefficients, window_weight, freq_weight):
    doubled = jnp.concatenate([freq_weight, freq_weight], axis=0)
    return coefficients * doubled[None, :, :, None] * window_weight[:, None, None, :]


def synthesize(coefficients, column_table, row_table):
    win_rows = coefficients.shape[0]
    win_cols = coefficients.shape[3]
    spread = jnp.einsum("tm,atvb->amvb", row_table, coefficients, precision=precise)
    spread = spread.reshape(win_rows, 2, 16, 64, win_cols)
    stacked = jnp.pad(spread[:, 0], ((0, 1), (0, 0), (0, 0), (0, 0))) + jnp.pad(
        spread[:, 1], ((1, 0), (0, 0), (0, 0), (0, 0))
    )
    lower_piece = jnp.einsum("akpb,lp->akbl", stacked, column_table[:16], precision=precise)
    upper_piece = jnp.einsum("akpb,lp->akbl", stacked, column_table[16:], precision=precise)
    blocks = jnp.pad(lower_piece, ((0, 0), (0, 0), (0, 1), (0, 0))) + jnp.pad(
        upper_piece, ((0, 0), (0, 0), (1, 0), (0, 0))
    )
    return blocks.reshape(16 * (win_rows + 1), 16 * (win_cols + 1))


LANES = 128
UPDATE_ROWS = 32
TILE_GROUP = 17
WINDOWS_PER_TILE = LANES // 16
HALF = WINDOWS_PER_TILE * 32


def numpy_tables():
    positions = np.arange(32, dtype=np.float32)
    window = np.exp(np.float32(-0.5) * ((positions - np.float32(15.5)) / np.float32(8.0)) ** 2)
    phases = np.float32(2.0 * np.pi) * np.outer(positions, positions) / np.float32(32.0)
    scale = np.sqrt(np.float32(32.0))
    cos_part = np.cos(phases) * window[None, :] / scale
    sin_part = -np.sin(phases) * window[None, :] / scale
    return cos_part.astype(np.float32), sin_part.astype(np.float32)


def transform_tables(win_rows):
    cos_part, sin_part = numpy_tables()
    column_table = np.stack([cos_part.T, sin_part.T], axis=1)
    columns = np.zeros((2 * WINDOWS_PER_TILE, 16, 2, WINDOWS_PER_TILE, 32), np.float32)
    for k in range(WINDOWS_PER_TILE):
        columns[k, :, :, k] = column_table[:16]
        columns[k + 1, :, :, k] = column_table[16:]
    columns = columns.reshape(2 * LANES, 2 * HALF)
    blocks = win_rows + 1
    real = np.zeros((win_rows, 32, blocks * 16), np.float32)
    imag = np.zeros((win_rows, 32, blocks * 16), np.float32)
    for a in range(win_rows):
        real[a, :, 16 * a : 16 * a + 32] = cos_part
        imag[a, :, 16 * a : 16 * a + 32] = sin_part
    real = real.reshape(win_rows * 32, blocks * 16)
    imag = imag.reshape(win_rows * 32, blocks * 16)
    forward = np.concatenate([real, imag], axis=1)
    backward = np.concatenate([real.T, imag.T], axis=1)
    return [columns, forward, backward]


def split_constant(table):
    high = table.astype(jnp.bfloat16)
    low = (table - high.astype(np.float32)).astype(jnp.bfloat16)
    return [jnp.asarray(high), jnp.asarray(low)]


def split_value(value):
    high = value.astype(jnp.bfloat16)
    return high, (value - high.astype(jnp.float32)).astype(jnp.bfloat16)


def three_pass_dot(a, b):
    total = jnp.dot(a[0], b[1], preferred_element_type=jnp.float32)
    total += jnp.dot(a[1], b[0], preferred_element_type=jnp.float32)
    return total + jnp.dot(a[0], b[0], preferred_element_type=jnp.float32)


def transposed_dot(a, b):
    def one(x, y):
        return lax.dot_general(
            x, y, (((1,), (1,)), ((), ())), preferred_element_type=jnp.float32
        )
    return one(a[0], b[1]) + one(a[1], b[0]) + one(a[0], b[0])


def constant_first_dot(a, b):
    rows = a[0].shape[0]
    both = jnp.dot(
        jnp.concatenate([a[0], a[1]], axis=0), b[0], preferred_element_type=jnp.float32
    )
    total = jnp.dot(a[0], b[1], preferred_element_type=jnp.float32)
    total += both[rows:]
    return total + both[:rows]


def transform_kernel(
    above_ref, middle_ref, below_ref, mh_ref, ml_ref, fh_ref, fl_ref, gh_ref, gl_ref, fw_ref,
    ww_ref, out_ref, y_ref, e_ref,
):
    x = jnp.concatenate([above_ref[:16], middle_ref[...], below_ref[...]], axis=0)
    rows = x.shape[0]
    win_rows = rows // 16 - 1
    tiles = (x.shape[1] - LANES) // LANES
    stacked_x = jnp.concatenate(
        [x[:, t * LANES : (t + 2) * LANES] for t in range(tiles)], axis=0
    )
    y_ref[...] = three_pass_dot(split_value(stacked_x), (mh_ref[...], ml_ref[...]))
    forward = (fh_ref[...], fl_ref[...])
    backward = (gh_ref[...], gl_ref[...])
    freq = fw_ref[...]

    def turn(value, sign):
        blocks = []
        for g in range(value.shape[1] // (2 * HALF)):
            re = value[:, 2 * HALF * g : 2 * HALF * g + HALF]
            im = value[:, 2 * HALF * g + HALF : 2 * HALF * (g + 1)]
            blocks += [-im, re] if sign else [im, -re]
        return jnp.concatenate(blocks, axis=1)

    for first in range(0, tiles, TILE_GROUP):
        group = range(first, min(first + TILE_GROUP, tiles))
        y = jnp.concatenate([y_ref[t * rows : (t + 1) * rows, :] for t in group], axis=1)
        weights = ww_ref[:, first * 2 * HALF : (group[-1] + 1) * 2 * HALF]
        z = constant_first_dot(forward, split_value(jnp.concatenate([y, turn(y, True)], axis=0)))
        spread = jnp.concatenate(
            [jnp.broadcast_to(weights[a : a + 1], (32, weights.shape[1])) for a in range(win_rows)],
            axis=0,
        )
        z = z * jnp.concatenate([freq] * len(group), axis=1) * spread
        e = constant_first_dot(backward, split_value(jnp.concatenate([z, turn(z, False)], axis=0)))
        for g, t in enumerate(group):
            e_ref[t * rows : (t + 1) * rows, :] = e[:, 2 * HALF * g : 2 * HALF * (g + 1)]
    pieces = transposed_dot(split_value(e_ref[...]), (mh_ref[...], ml_ref[...]))
    kept = out_ref.shape[0]
    out_ref[...] = jnp.zeros_like(out_ref)
    for t in range(tiles):
        out_ref[:, t * LANES : (t + 2) * LANES] += pieces[t * rows + 16 : t * rows + 16 + kept]


def padded_width(cols):
    windows = (cols - 16) // 16
    return (-(-windows // WINDOWS_PER_TILE) + 1) * LANES


def analyze_weigh_synthesize(above, middle, below, window_weight, freq_weight, cols):
    rows = middle.shape[0] + 32
    windows = (cols - 16) // 16
    tiles = -(-windows // WINDOWS_PER_TILE)
    wide = (tiles + 1) * LANES
    window_weight = jnp.pad(window_weight, ((0, 0), (0, tiles * WINDOWS_PER_TILE - windows)))
    win_rows = rows // 16 - 1
    constants = []
    for table in transform_tables(win_rows):
        constants += split_constant(table)
    freq = jnp.broadcast_to(
        freq_weight.reshape(1, 32, 1, 1, 32), (win_rows, 32, 2, WINDOWS_PER_TILE, 32)
    ).reshape(win_rows * 32, 2 * HALF)
    weights = jnp.broadcast_to(
        window_weight.reshape(win_rows, tiles, 1, WINDOWS_PER_TILE, 1),
        (win_rows, tiles, 2, WINDOWS_PER_TILE, 32),
    ).reshape(win_rows, tiles * 2 * HALF)
    vmem = pl.BlockSpec(memory_space=pltpu.VMEM)
    out = pl.pallas_call(
        transform_kernel,
        out_shape=jax.ShapeDtypeStruct((rows - 32, wide), jnp.float32),
        in_specs=[vmem] * 11,
        out_specs=vmem,
        scratch_shapes=[
            pltpu.VMEM((tiles * rows, 2 * HALF), jnp.float32),
            pltpu.VMEM((tiles * rows, 2 * HALF), jnp.float32),
        ],
    )(above, middle, below, *constants, freq, weights)
    return out[:, :cols]


def update_kernel(sums_ref, iterate_ref, residual_ref, direction_ref, applied_ref,
                  iterate_out, residual_out, direction_out):
    sums = sums_ref[...]
    norm_now, curvature, cross_term, image_norm = (sums[:, i : i + 1] for i in range(4))
    step_length = norm_now / curvature
    norm_next = norm_now - 2.0 * step_length * cross_term + step_length * step_length * image_norm
    ratio = norm_next / norm_now
    direction = direction_ref[...]
    iterate_out[...] = iterate_ref[...] + step_length * direction
    new_residual = residual_ref[...] - step_length * applied_ref[...]
    residual_out[...] = new_residual
    direction_out[...] = new_residual + ratio * direction


def updated(sums, iterate, residual, direction, applied):
    height, breadth = iterate.shape
    rows = UPDATE_ROWS
    block = pl.BlockSpec((rows, breadth), lambda i: (i, 0))
    shape = jax.ShapeDtypeStruct(iterate.shape, jnp.float32)
    return pl.pallas_call(
        update_kernel,
        grid=(height // rows,),
        out_shape=(shape, shape, shape),
        in_specs=[pl.BlockSpec((1, 4), lambda i: (0, 0))] + [block] * 4,
        out_specs=(block, block, block),
    )(sums, iterate, residual, direction, applied)


def per_device(iterate, residual, direction, window_weight, freq_weight):
    height, breadth = direction.shape
    rim_weight = jnp.pad(window_weight[:, -1:], ((0, 0), (0, 15)))
    from_left = passed_along(
        jnp.concatenate([direction[:, -16:], rim_weight], axis=0), COL, 1
    )
    from_right = passed_along(direction[:, :16], COL, -1)
    cols = breadth + 32
    wide = padded_width(cols)
    widened = jnp.concatenate(
        [from_left[:height], direction, from_right, jnp.zeros((height, wide - cols), jnp.float32)],
        axis=1,
    )
    weights_wide = jnp.concatenate([from_left[height:, :1], window_weight], axis=1)
    top_weight = jnp.pad(weights_wide[-1:], ((0, 0), (0, widened.shape[1] - weights_wide.shape[1])))
    from_above = passed_along(
        jnp.concatenate([widened[-16:], top_weight], axis=0), "row", 1
    )
    from_below = passed_along(widened[:16], "row", -1)
    weights_all = jnp.concatenate(
        [from_above[16:, : weights_wide.shape[1]], weights_wide], axis=0
    )
    spread = analyze_weigh_synthesize(
        from_above, widened, from_below, weights_all, freq_weight, cols
    )
    synthesized = spread[:, 16 : 16 + breadth]
    applied = synthesized + damping * direction
    products = jnp.stack(
        [residual * residual, direction * applied, residual * applied, applied * applied]
    )
    sums = summed_everywhere(jnp.sum(products, axis=(1, 2)), DOUBLING)
    return updated(sums.reshape(1, 4), iterate, residual, direction, applied)


def solution(mesh):
    finer = Mesh(
        mesh.devices.reshape(mesh.shape["row"], 4, 4, 2, 2),
        ("row", "col_0", "col_1", "col_2", "col_3"),
    )
    return jax.shard_map(
        per_device,
        mesh=finer,
        in_specs=(P("row", COL), P("row", COL), P("row", COL), P("row", COL), P()),
        out_specs=(P("row", COL), P("row", COL), P("row", COL)),
        check_vma=False,
    )
```

```python
import jax
import numpy as np
import jax.numpy as jnp
from jax import lax
from jax.sharding import Mesh
from jax.sharding import PartitionSpec as P
from jax.experimental import pallas as pl
from jax.experimental.pallas import tpu as pltpu

COL = ("col_0", "col_1", "col_2", "col_3")
DOUBLING = (
    ("col_3", 1),
    ("row", 1),
    ("row", 2),
    ("col_0", 1),
    ("col_0", 2),
    ("col_1", 1),
    ("col_1", 2),
    ("col_2", 1),
)


precise = lax.Precision.HIGHEST
damping = 0.5


def passed_along(value, axis, steps):
    count = lax.axis_size(axis)
    leading, last = (max(0, -steps), min(count, count - steps))
    return lax.ppermute(value, axis, [(source, source + steps) for source in range(leading, last)])


def passed_diagonally(value, steps):
    rows, cols = lax.axis_size("row"), lax.axis_size(COL)
    pairs = [
        (r * cols + c, (r + steps) * cols + (c + steps))
        for r in range(max(0, -steps), min(rows, rows - steps))
        for c in range(max(0, -steps), min(cols, cols - steps))
    ]
    return lax.ppermute(value, ("row",) + COL, pairs)


def summed_everywhere(x, steps):
    for axis, mask in steps:
        count = lax.axis_size(axis)
        x = x + lax.ppermute(x, axis, [(i, i ^ mask) for i in range(count)])
    return x


def tables():
    positions = jnp.arange(32, dtype=jnp.float32)
    window = jnp.exp(-0.5 * ((positions - 15.5) / 8.0) ** 2)
    phases = 2.0 * jnp.pi * jnp.outer(positions, positions) / 32.0
    cos_part = jnp.cos(phases) * window[None, :] / jnp.sqrt(32.0)
    sin_part = -jnp.sin(phases) * window[None, :] / jnp.sqrt(32.0)
    column_table = jnp.concatenate([cos_part.T, sin_part.T], axis=1)
    cos_split = cos_part.reshape(32, 2, 16)
    sin_split = sin_part.reshape(32, 2, 16)
    upper = jnp.stack([cos_split, -sin_split], axis=-1)
    lower = jnp.stack([sin_split, cos_split], axis=-1)
    row_table = jnp.concatenate([upper, lower], axis=0).reshape(64, 64)
    return (column_table, row_table)


def analyze(region, column_table, row_table):
    win_rows = region.shape[0] // 16 - 1
    win_cols = region.shape[1] // 16 - 1
    blocks = region.reshape(win_rows + 1, 16, win_cols + 1, 16)
    section_one = jnp.einsum(
        "akbl,lp->akpb", blocks[:, :, :win_cols], column_table[:16], precision=precise
    )
    section_one = section_one + jnp.einsum(
        "akbl,lp->akpb", blocks[:, :, 1:], column_table[16:], precision=precise
    )
    section_one = section_one.reshape(win_rows + 1, 16, 2, 32, win_cols)
    paired = jnp.stack([section_one[:-1], section_one[1:]], axis=1).reshape(
        win_rows, 64, 32, win_cols
    )
    return jnp.einsum("tm,amvb->atvb", row_table, paired, precision=precise)


def weigh(coefficients, window_weight, freq_weight):
    doubled = jnp.concatenate([freq_weight, freq_weight], axis=0)
    return coefficients * doubled[None, :, :, None] * window_weight[:, None, None, :]


def synthesize(coefficients, column_table, row_table):
    win_rows = coefficients.shape[0]
    win_cols = coefficients.shape[3]
    spread = jnp.einsum("tm,atvb->amvb", row_table, coefficients, precision=precise)
    spread = spread.reshape(win_rows, 2, 16, 64, win_cols)
    stacked = jnp.pad(spread[:, 0], ((0, 1), (0, 0), (0, 0), (0, 0))) + jnp.pad(
        spread[:, 1], ((1, 0), (0, 0), (0, 0), (0, 0))
    )
    lower_piece = jnp.einsum("akpb,lp->akbl", stacked, column_table[:16], precision=precise)
    upper_piece = jnp.einsum("akpb,lp->akbl", stacked, column_table[16:], precision=precise)
    blocks = jnp.pad(lower_piece, ((0, 0), (0, 0), (0, 1), (0, 0))) + jnp.pad(
        upper_piece, ((0, 0), (0, 0), (1, 0), (0, 0))
    )
    return blocks.reshape(16 * (win_rows + 1), 16 * (win_cols + 1))


LANES = 128
UPDATE_ROWS = 32
TILE_GROUP = 17
WINDOWS_PER_TILE = LANES // 16
HALF = WINDOWS_PER_TILE * 32


def numpy_tables():
    positions = np.arange(32, dtype=np.float32)
    window = np.exp(np.float32(-0.5) * ((positions - np.float32(15.5)) / np.float32(8.0)) ** 2)
    phases = np.float32(2.0 * np.pi) * np.outer(positions, positions) / np.float32(32.0)
    scale = np.sqrt(np.float32(32.0))
    cos_part = np.cos(phases) * window[None, :] / scale
    sin_part = -np.sin(phases) * window[None, :] / scale
    return cos_part.astype(np.float32), sin_part.astype(np.float32)


def transform_tables(win_rows):
    cos_part, sin_part = numpy_tables()
    column_table = np.stack([cos_part.T, sin_part.T], axis=1)
    columns = np.zeros((2 * WINDOWS_PER_TILE, 16, 2, WINDOWS_PER_TILE, 32), np.float32)
    for k in range(WINDOWS_PER_TILE):
        columns[k, :, :, k] = column_table[:16]
        columns[k + 1, :, :, k] = column_table[16:]
    columns = columns.reshape(2 * LANES, 2 * HALF)
    blocks = win_rows + 1
    real = np.zeros((win_rows, 32, blocks * 16), np.float32)
    imag = np.zeros((win_rows, 32, blocks * 16), np.float32)
    for a in range(win_rows):
        real[a, :, 16 * a : 16 * a + 32] = cos_part
        imag[a, :, 16 * a : 16 * a + 32] = sin_part
    real = real.reshape(win_rows * 32, blocks * 16)
    imag = imag.reshape(win_rows * 32, blocks * 16)
    forward = np.concatenate([real, imag], axis=1)
    backward = np.concatenate([real.T, imag.T], axis=1)
    return [columns, forward, backward]


def split_constant(table):
    high = table.astype(jnp.bfloat16)
    low = (table - high.astype(np.float32)).astype(jnp.bfloat16)
    return [jnp.asarray(high), jnp.asarray(low)]


def split_value(value):
    high = value.astype(jnp.bfloat16)
    return high, (value - high.astype(jnp.float32)).astype(jnp.bfloat16)


def three_pass_dot(a, b):
    total = jnp.dot(a[0], b[1], preferred_element_type=jnp.float32)
    total += jnp.dot(a[1], b[0], preferred_element_type=jnp.float32)
    return total + jnp.dot(a[0], b[0], preferred_element_type=jnp.float32)


def transposed_dot(a, b):
    def one(x, y):
        return lax.dot_general(
            x, y, (((1,), (1,)), ((), ())), preferred_element_type=jnp.float32
        )
    return one(a[0], b[1]) + one(a[1], b[0]) + one(a[0], b[0])


def constant_first_dot(a, b):
    rows = a[0].shape[0]
    both = jnp.dot(
        jnp.concatenate([a[0], a[1]], axis=0), b[0], preferred_element_type=jnp.float32
    )
    total = jnp.dot(a[0], b[1], preferred_element_type=jnp.float32)
    total += both[rows:]
    return total + both[:rows]


def transform_kernel(
    above_ref, middle_ref, below_ref, mh_ref, ml_ref, fh_ref, fl_ref, gh_ref, gl_ref, fw_ref,
    ww_ref, out_ref, y_ref, e_ref,
):
    x = jnp.concatenate([above_ref[:16], middle_ref[...], below_ref[...]], axis=0)
    rows = x.shape[0]
    win_rows = rows // 16 - 1
    tiles = (x.shape[1] - LANES) // LANES
    stacked_x = jnp.concatenate(
        [x[:, t * LANES : (t + 2) * LANES] for t in range(tiles)], axis=0
    )
    y_ref[...] = three_pass_dot(split_value(stacked_x), (mh_ref[...], ml_ref[...]))
    forward = (fh_ref[...], fl_ref[...])
    backward = (gh_ref[...], gl_ref[...])
    freq = fw_ref[...]

    def turn(value, sign):
        blocks = []
        for g in range(value.shape[1] // (2 * HALF)):
            re = value[:, 2 * HALF * g : 2 * HALF * g + HALF]
            im = value[:, 2 * HALF * g + HALF : 2 * HALF * (g + 1)]
            blocks += [-im, re] if sign else [im, -re]
        return jnp.concatenate(blocks, axis=1)

    for first in range(0, tiles, TILE_GROUP):
        group = range(first, min(first + TILE_GROUP, tiles))
        y = jnp.concatenate([y_ref[t * rows : (t + 1) * rows, :] for t in group], axis=1)
        weights = ww_ref[:, first * 2 * HALF : (group[-1] + 1) * 2 * HALF]
        z = constant_first_dot(forward, split_value(jnp.concatenate([y, turn(y, True)], axis=0)))
        spread = jnp.concatenate(
            [jnp.broadcast_to(weights[a : a + 1], (32, weights.shape[1])) for a in range(win_rows)],
            axis=0,
        )
        z = z * jnp.concatenate([freq] * len(group), axis=1) * spread
        e = constant_first_dot(backward, split_value(jnp.concatenate([z, turn(z, False)], axis=0)))
        for g, t in enumerate(group):
            e_ref[t * rows : (t + 1) * rows, :] = e[:, 2 * HALF * g : 2 * HALF * (g + 1)]
    pieces = transposed_dot(split_value(e_ref[...]), (mh_ref[...], ml_ref[...]))
    kept = out_ref.shape[0]
    out_ref[...] = jnp.zeros_like(out_ref)
    for t in range(tiles):
        out_ref[:, t * LANES : (t + 2) * LANES] += pieces[t * rows + 16 : t * rows + 16 + kept]


def padded_width(cols):
    windows = (cols - 16) // 16
    return (-(-windows // WINDOWS_PER_TILE) + 1) * LANES


def analyze_weigh_synthesize(above, middle, below, window_weight, freq_weight, cols):
    rows = middle.shape[0] + 32
    windows = (cols - 16) // 16
    tiles = -(-windows // WINDOWS_PER_TILE)
    wide = (tiles + 1) * LANES
    window_weight = jnp.pad(window_weight, ((0, 0), (0, tiles * WINDOWS_PER_TILE - windows)))
    win_rows = rows // 16 - 1
    constants = []
    for table in transform_tables(win_rows):
        constants += split_constant(table)
    freq = jnp.broadcast_to(
        freq_weight.reshape(1, 32, 1, 1, 32), (win_rows, 32, 2, WINDOWS_PER_TILE, 32)
    ).reshape(win_rows * 32, 2 * HALF)
    weights = jnp.broadcast_to(
        window_weight.reshape(win_rows, tiles, 1, WINDOWS_PER_TILE, 1),
        (win_rows, tiles, 2, WINDOWS_PER_TILE, 32),
    ).reshape(win_rows, tiles * 2 * HALF)
    vmem = pl.BlockSpec(memory_space=pltpu.VMEM)
    out = pl.pallas_call(
        transform_kernel,
        out_shape=jax.ShapeDtypeStruct((rows - 32, wide), jnp.float32),
        in_specs=[vmem] * 11,
        out_specs=vmem,
        scratch_shapes=[
            pltpu.VMEM((tiles * rows, 2 * HALF), jnp.float32),
            pltpu.VMEM((tiles * rows, 2 * HALF), jnp.float32),
        ],
    )(above, middle, below, *constants, freq, weights)
    return out[:, :cols]


def update_kernel(sums_ref, iterate_ref, residual_ref, direction_ref, applied_ref,
                  iterate_out, residual_out, direction_out):
    sums = sums_ref[...]
    norm_now, curvature, cross_term, image_norm = (sums[:, i : i + 1] for i in range(4))
    step_length = norm_now / curvature
    norm_next = norm_now - 2.0 * step_length * cross_term + step_length * step_length * image_norm
    ratio = norm_next / norm_now
    direction = direction_ref[...]
    iterate_out[...] = iterate_ref[...] + step_length * direction
    new_residual = residual_ref[...] - step_length * applied_ref[...]
    residual_out[...] = new_residual
    direction_out[...] = new_residual + ratio * direction


def updated(sums, iterate, residual, direction, applied):
    height, breadth = iterate.shape
    rows = UPDATE_ROWS
    block = pl.BlockSpec((rows, breadth), lambda i: (i, 0))
    shape = jax.ShapeDtypeStruct(iterate.shape, jnp.float32)
    return pl.pallas_call(
        update_kernel,
        grid=(height // rows,),
        out_shape=(shape, shape, shape),
        in_specs=[pl.BlockSpec((1, 4), lambda i: (0, 0))] + [block] * 4,
        out_specs=(block, block, block),
    )(sums, iterate, residual, direction, applied)


def per_device(iterate, residual, direction, window_weight, freq_weight):
    height, breadth = direction.shape
    rim_weight = jnp.pad(window_weight[:, -1:], ((0, 0), (0, 15)))
    from_left = passed_along(
        jnp.concatenate([direction[:, -16:], rim_weight], axis=0), COL, 1
    )
    from_right = passed_along(direction[:, :16], COL, -1)
    cols = breadth + 32
    wide = padded_width(cols)
    widened = jnp.concatenate(
        [from_left[:height], direction, from_right, jnp.zeros((height, wide - cols), jnp.float32)],
        axis=1,
    )
    weights_wide = jnp.concatenate([from_left[height:, :1], window_weight], axis=1)
    top_weight = jnp.pad(weights_wide[-1:], ((0, 0), (0, widened.shape[1] - weights_wide.shape[1])))
    from_above = passed_along(
        jnp.concatenate([widened[-16:], top_weight], axis=0), "row", 1
    )
    from_below = passed_along(widened[:16], "row", -1)
    weights_all = jnp.concatenate(
        [from_above[16:, : weights_wide.shape[1]], weights_wide], axis=0
    )
    spread = analyze_weigh_synthesize(
        from_above, widened, from_below, weights_all, freq_weight, cols
    )
    synthesized = spread[:, 16 : 16 + breadth]
    applied = synthesized + damping * direction
    products = jnp.stack(
        [residual * residual, direction * applied, residual * applied, applied * applied]
    )
    partial = lax.optimization_barrier(jnp.sum(products, axis=1))
    sums = summed_everywhere(jnp.sum(partial, axis=1), DOUBLING)
    return updated(sums.reshape(1, 4), iterate, residual, direction, applied)


def solution(mesh):
    finer = Mesh(
        mesh.devices.reshape(mesh.shape["row"], 4, 4, 2, 2),
        ("row", "col_0", "col_1", "col_2", "col_3"),
    )
    return jax.shard_map(
        per_device,
        mesh=finer,
        in_specs=(P("row", COL), P("row", COL), P("row", COL), P("row", COL), P()),
        out_specs=(P("row", COL), P("row", COL), P("row", COL)),
        check_vma=False,
    )
```

```python
import jax
import numpy as np
import jax.numpy as jnp
from jax import lax
from jax.sharding import Mesh
from jax.sharding import PartitionSpec as P
from jax.experimental import pallas as pl
from jax.experimental.pallas import tpu as pltpu

COL = ("col_0", "col_1", "col_2", "col_3")
DOUBLING = (
    ("col_3", 1),
    ("col_2", 1),
    ("row", 1),
    ("row", 2),
    ("col_0", 1),
    ("col_0", 2),
    ("col_1", 1),
    ("col_1", 2),
)


precise = lax.Precision.HIGHEST
damping = 0.5


def passed_along(value, axis, steps):
    count = lax.axis_size(axis)
    leading, last = (max(0, -steps), min(count, count - steps))
    return lax.ppermute(value, axis, [(source, source + steps) for source in range(leading, last)])


def passed_diagonally(value, steps):
    rows, cols = lax.axis_size("row"), lax.axis_size(COL)
    pairs = [
        (r * cols + c, (r + steps) * cols + (c + steps))
        for r in range(max(0, -steps), min(rows, rows - steps))
        for c in range(max(0, -steps), min(cols, cols - steps))
    ]
    return lax.ppermute(value, ("row",) + COL, pairs)


def summed_everywhere(x, steps):
    for axis, mask in steps:
        count = lax.axis_size(axis)
        x = x + lax.ppermute(x, axis, [(i, i ^ mask) for i in range(count)])
    return x


def tables():
    positions = jnp.arange(32, dtype=jnp.float32)
    window = jnp.exp(-0.5 * ((positions - 15.5) / 8.0) ** 2)
    phases = 2.0 * jnp.pi * jnp.outer(positions, positions) / 32.0
    cos_part = jnp.cos(phases) * window[None, :] / jnp.sqrt(32.0)
    sin_part = -jnp.sin(phases) * window[None, :] / jnp.sqrt(32.0)
    column_table = jnp.concatenate([cos_part.T, sin_part.T], axis=1)
    cos_split = cos_part.reshape(32, 2, 16)
    sin_split = sin_part.reshape(32, 2, 16)
    upper = jnp.stack([cos_split, -sin_split], axis=-1)
    lower = jnp.stack([sin_split, cos_split], axis=-1)
    row_table = jnp.concatenate([upper, lower], axis=0).reshape(64, 64)
    return (column_table, row_table)


def analyze(region, column_table, row_table):
    win_rows = region.shape[0] // 16 - 1
    win_cols = region.shape[1] // 16 - 1
    blocks = region.reshape(win_rows + 1, 16, win_cols + 1, 16)
    section_one = jnp.einsum(
        "akbl,lp->akpb", blocks[:, :, :win_cols], column_table[:16], precision=precise
    )
    section_one = section_one + jnp.einsum(
        "akbl,lp->akpb", blocks[:, :, 1:], column_table[16:], precision=precise
    )
    section_one = section_one.reshape(win_rows + 1, 16, 2, 32, win_cols)
    paired = jnp.stack([section_one[:-1], section_one[1:]], axis=1).reshape(
        win_rows, 64, 32, win_cols
    )
    return jnp.einsum("tm,amvb->atvb", row_table, paired, precision=precise)


def weigh(coefficients, window_weight, freq_weight):
    doubled = jnp.concatenate([freq_weight, freq_weight], axis=0)
    return coefficients * doubled[None, :, :, None] * window_weight[:, None, None, :]


def synthesize(coefficients, column_table, row_table):
    win_rows = coefficients.shape[0]
    win_cols = coefficients.shape[3]
    spread = jnp.einsum("tm,atvb->amvb", row_table, coefficients, precision=precise)
    spread = spread.reshape(win_rows, 2, 16, 64, win_cols)
    stacked = jnp.pad(spread[:, 0], ((0, 1), (0, 0), (0, 0), (0, 0))) + jnp.pad(
        spread[:, 1], ((1, 0), (0, 0), (0, 0), (0, 0))
    )
    lower_piece = jnp.einsum("akpb,lp->akbl", stacked, column_table[:16], precision=precise)
    upper_piece = jnp.einsum("akpb,lp->akbl", stacked, column_table[16:], precision=precise)
    blocks = jnp.pad(lower_piece, ((0, 0), (0, 0), (0, 1), (0, 0))) + jnp.pad(
        upper_piece, ((0, 0), (0, 0), (1, 0), (0, 0))
    )
    return blocks.reshape(16 * (win_rows + 1), 16 * (win_cols + 1))


LANES = 128
UPDATE_ROWS = 32
TILE_GROUP = 17
WINDOWS_PER_TILE = LANES // 16
HALF = WINDOWS_PER_TILE * 32


def numpy_tables():
    positions = np.arange(32, dtype=np.float32)
    window = np.exp(np.float32(-0.5) * ((positions - np.float32(15.5)) / np.float32(8.0)) ** 2)
    phases = np.float32(2.0 * np.pi) * np.outer(positions, positions) / np.float32(32.0)
    scale = np.sqrt(np.float32(32.0))
    cos_part = np.cos(phases) * window[None, :] / scale
    sin_part = -np.sin(phases) * window[None, :] / scale
    return cos_part.astype(np.float32), sin_part.astype(np.float32)


def transform_tables(win_rows):
    cos_part, sin_part = numpy_tables()
    column_table = np.stack([cos_part.T, sin_part.T], axis=1)
    columns = np.zeros((2 * WINDOWS_PER_TILE, 16, 2, WINDOWS_PER_TILE, 32), np.float32)
    for k in range(WINDOWS_PER_TILE):
        columns[k, :, :, k] = column_table[:16]
        columns[k + 1, :, :, k] = column_table[16:]
    columns = columns.reshape(2 * LANES, 2 * HALF)
    blocks = win_rows + 1
    real = np.zeros((win_rows, 32, blocks * 16), np.float32)
    imag = np.zeros((win_rows, 32, blocks * 16), np.float32)
    for a in range(win_rows):
        real[a, :, 16 * a : 16 * a + 32] = cos_part
        imag[a, :, 16 * a : 16 * a + 32] = sin_part
    real = real.reshape(win_rows * 32, blocks * 16)
    imag = imag.reshape(win_rows * 32, blocks * 16)
    forward = np.concatenate([real, imag], axis=1)
    backward = np.concatenate([real.T, imag.T], axis=1)
    return [columns, forward, backward]


def split_constant(table):
    high = table.astype(jnp.bfloat16)
    low = (table - high.astype(np.float32)).astype(jnp.bfloat16)
    return [jnp.asarray(high), jnp.asarray(low)]


def split_value(value):
    high = value.astype(jnp.bfloat16)
    return high, (value - high.astype(jnp.float32)).astype(jnp.bfloat16)


def three_pass_dot(a, b):
    total = jnp.dot(a[0], b[1], preferred_element_type=jnp.float32)
    total += jnp.dot(a[1], b[0], preferred_element_type=jnp.float32)
    return total + jnp.dot(a[0], b[0], preferred_element_type=jnp.float32)


def transposed_dot(a, b):
    def one(x, y):
        return lax.dot_general(
            x, y, (((1,), (1,)), ((), ())), preferred_element_type=jnp.float32
        )
    return one(a[0], b[1]) + one(a[1], b[0]) + one(a[0], b[0])


def constant_first_dot(a, b):
    rows = a[0].shape[0]
    both = jnp.dot(
        jnp.concatenate([a[0], a[1]], axis=0), b[0], preferred_element_type=jnp.float32
    )
    total = jnp.dot(a[0], b[1], preferred_element_type=jnp.float32)
    total += both[rows:]
    return total + both[:rows]


def transform_kernel(
    above_ref, middle_ref, below_ref, mh_ref, ml_ref, fh_ref, fl_ref, gh_ref, gl_ref, fw_ref,
    ww_ref, out_ref, y_ref, e_ref,
):
    x = jnp.concatenate([above_ref[:16], middle_ref[...], below_ref[...]], axis=0)
    rows = x.shape[0]
    win_rows = rows // 16 - 1
    tiles = (x.shape[1] - LANES) // LANES
    stacked_x = jnp.concatenate(
        [x[:, t * LANES : (t + 2) * LANES] for t in range(tiles)], axis=0
    )
    y_ref[...] = three_pass_dot(split_value(stacked_x), (mh_ref[...], ml_ref[...]))
    forward = (fh_ref[...], fl_ref[...])
    backward = (gh_ref[...], gl_ref[...])
    freq = fw_ref[...]

    def turn(value, sign):
        blocks = []
        for g in range(value.shape[1] // (2 * HALF)):
            re = value[:, 2 * HALF * g : 2 * HALF * g + HALF]
            im = value[:, 2 * HALF * g + HALF : 2 * HALF * (g + 1)]
            blocks += [-im, re] if sign else [im, -re]
        return jnp.concatenate(blocks, axis=1)

    for first in range(0, tiles, TILE_GROUP):
        group = range(first, min(first + TILE_GROUP, tiles))
        y = jnp.concatenate([y_ref[t * rows : (t + 1) * rows, :] for t in group], axis=1)
        weights = ww_ref[:, first * 2 * HALF : (group[-1] + 1) * 2 * HALF]
        z = constant_first_dot(forward, split_value(jnp.concatenate([y, turn(y, True)], axis=0)))
        spread = jnp.concatenate(
            [jnp.broadcast_to(weights[a : a + 1], (32, weights.shape[1])) for a in range(win_rows)],
            axis=0,
        )
        z = z * jnp.concatenate([freq] * len(group), axis=1) * spread
        e = constant_first_dot(backward, split_value(jnp.concatenate([z, turn(z, False)], axis=0)))
        for g, t in enumerate(group):
            e_ref[t * rows : (t + 1) * rows, :] = e[:, 2 * HALF * g : 2 * HALF * (g + 1)]
    pieces = transposed_dot(split_value(e_ref[...]), (mh_ref[...], ml_ref[...]))
    kept = out_ref.shape[0]
    out_ref[...] = jnp.zeros_like(out_ref)
    for t in range(tiles):
        out_ref[:, t * LANES : (t + 2) * LANES] += pieces[t * rows + 16 : t * rows + 16 + kept]


def padded_width(cols):
    windows = (cols - 16) // 16
    return (-(-windows // WINDOWS_PER_TILE) + 1) * LANES


def analyze_weigh_synthesize(above, middle, below, window_weight, freq_weight, cols):
    rows = middle.shape[0] + 32
    windows = (cols - 16) // 16
    tiles = -(-windows // WINDOWS_PER_TILE)
    wide = (tiles + 1) * LANES
    window_weight = jnp.pad(window_weight, ((0, 0), (0, tiles * WINDOWS_PER_TILE - windows)))
    win_rows = rows // 16 - 1
    constants = []
    for table in transform_tables(win_rows):
        constants += split_constant(table)
    freq = jnp.broadcast_to(
        freq_weight.reshape(1, 32, 1, 1, 32), (win_rows, 32, 2, WINDOWS_PER_TILE, 32)
    ).reshape(win_rows * 32, 2 * HALF)
    weights = jnp.broadcast_to(
        window_weight.reshape(win_rows, tiles, 1, WINDOWS_PER_TILE, 1),
        (win_rows, tiles, 2, WINDOWS_PER_TILE, 32),
    ).reshape(win_rows, tiles * 2 * HALF)
    vmem = pl.BlockSpec(memory_space=pltpu.VMEM)
    out = pl.pallas_call(
        transform_kernel,
        out_shape=jax.ShapeDtypeStruct((rows - 32, wide), jnp.float32),
        in_specs=[vmem] * 11,
        out_specs=vmem,
        scratch_shapes=[
            pltpu.VMEM((tiles * rows, 2 * HALF), jnp.float32),
            pltpu.VMEM((tiles * rows, 2 * HALF), jnp.float32),
        ],
    )(above, middle, below, *constants, freq, weights)
    return out[:, :cols]


def update_kernel(sums_ref, iterate_ref, residual_ref, direction_ref, applied_ref,
                  iterate_out, residual_out, direction_out):
    sums = sums_ref[...]
    norm_now, curvature, cross_term, image_norm = (sums[:, i : i + 1] for i in range(4))
    step_length = norm_now / curvature
    norm_next = norm_now - 2.0 * step_length * cross_term + step_length * step_length * image_norm
    ratio = norm_next / norm_now
    direction = direction_ref[...]
    iterate_out[...] = iterate_ref[...] + step_length * direction
    new_residual = residual_ref[...] - step_length * applied_ref[...]
    residual_out[...] = new_residual
    direction_out[...] = new_residual + ratio * direction


def updated(sums, iterate, residual, direction, applied):
    height, breadth = iterate.shape
    rows = UPDATE_ROWS
    block = pl.BlockSpec((rows, breadth), lambda i: (i, 0))
    shape = jax.ShapeDtypeStruct(iterate.shape, jnp.float32)
    return pl.pallas_call(
        update_kernel,
        grid=(height // rows,),
        out_shape=(shape, shape, shape),
        in_specs=[pl.BlockSpec((1, 4), lambda i: (0, 0))] + [block] * 4,
        out_specs=(block, block, block),
    )(sums, iterate, residual, direction, applied)


def per_device(iterate, residual, direction, window_weight, freq_weight):
    height, breadth = direction.shape
    rim_weight = jnp.pad(window_weight[:, -1:], ((0, 0), (0, 15)))
    from_left = passed_along(
        jnp.concatenate([direction[:, -16:], rim_weight], axis=0), COL, 1
    )
    from_right = passed_along(direction[:, :16], COL, -1)
    cols = breadth + 32
    wide = padded_width(cols)
    widened = jnp.concatenate(
        [from_left[:height], direction, from_right, jnp.zeros((height, wide - cols), jnp.float32)],
        axis=1,
    )
    weights_wide = jnp.concatenate([from_left[height:, :1], window_weight], axis=1)
    top_weight = jnp.pad(weights_wide[-1:], ((0, 0), (0, widened.shape[1] - weights_wide.shape[1])))
    from_above = passed_along(
        jnp.concatenate([widened[-16:], top_weight], axis=0), "row", 1
    )
    from_below = passed_along(widened[:16], "row", -1)
    weights_all = jnp.concatenate(
        [from_above[16:, : weights_wide.shape[1]], weights_wide], axis=0
    )
    spread = analyze_weigh_synthesize(
        from_above, widened, from_below, weights_all, freq_weight, cols
    )
    synthesized = spread[:, 16 : 16 + breadth]
    applied = synthesized + damping * direction
    products = jnp.stack(
        [residual * residual, direction * applied, residual * applied, applied * applied]
    )
    sums = summed_everywhere(jnp.sum(products, axis=(1, 2)), DOUBLING)
    return updated(sums.reshape(1, 4), iterate, residual, direction, applied)


def solution(mesh):
    finer = Mesh(
        mesh.devices.reshape(mesh.shape["row"], 4, 4, 2, 2),
        ("row", "col_0", "col_1", "col_2", "col_3"),
    )
    return jax.shard_map(
        per_device,
        mesh=finer,
        in_specs=(P("row", COL), P("row", COL), P("row", COL), P("row", COL), P()),
        out_specs=(P("row", COL), P("row", COL), P("row", COL)),
        check_vma=False,
    )
```

```python
import jax
import numpy as np
import jax.numpy as jnp
from jax import lax
from jax.sharding import Mesh
from jax.sharding import PartitionSpec as P
from jax.experimental import pallas as pl
from jax.experimental.pallas import tpu as pltpu

COL = ("col_0", "col_1", "col_2", "col_3")
DOUBLING = (
    ("col_2", 1),
    ("col_3", 1),
    ("row", 1),
    ("row", 2),
    ("col_0", 1),
    ("col_0", 2),
    ("col_1", 1),
    ("col_1", 2),
)


precise = lax.Precision.HIGHEST
damping = 0.5


def passed_along(value, axis, steps):
    count = lax.axis_size(axis)
    leading, last = (max(0, -steps), min(count, count - steps))
    return lax.ppermute(value, axis, [(source, source + steps) for source in range(leading, last)])


def passed_diagonally(value, steps):
    rows, cols = lax.axis_size("row"), lax.axis_size(COL)
    pairs = [
        (r * cols + c, (r + steps) * cols + (c + steps))
        for r in range(max(0, -steps), min(rows, rows - steps))
        for c in range(max(0, -steps), min(cols, cols - steps))
    ]
    return lax.ppermute(value, ("row",) + COL, pairs)


def summed_everywhere(x, steps):
    for axis, mask in steps:
        count = lax.axis_size(axis)
        x = x + lax.ppermute(x, axis, [(i, i ^ mask) for i in range(count)])
    return x


def tables():
    positions = jnp.arange(32, dtype=jnp.float32)
    window = jnp.exp(-0.5 * ((positions - 15.5) / 8.0) ** 2)
    phases = 2.0 * jnp.pi * jnp.outer(positions, positions) / 32.0
    cos_part = jnp.cos(phases) * window[None, :] / jnp.sqrt(32.0)
    sin_part = -jnp.sin(phases) * window[None, :] / jnp.sqrt(32.0)
    column_table = jnp.concatenate([cos_part.T, sin_part.T], axis=1)
    cos_split = cos_part.reshape(32, 2, 16)
    sin_split = sin_part.reshape(32, 2, 16)
    upper = jnp.stack([cos_split, -sin_split], axis=-1)
    lower = jnp.stack([sin_split, cos_split], axis=-1)
    row_table = jnp.concatenate([upper, lower], axis=0).reshape(64, 64)
    return (column_table, row_table)


def analyze(region, column_table, row_table):
    win_rows = region.shape[0] // 16 - 1
    win_cols = region.shape[1] // 16 - 1
    blocks = region.reshape(win_rows + 1, 16, win_cols + 1, 16)
    section_one = jnp.einsum(
        "akbl,lp->akpb", blocks[:, :, :win_cols], column_table[:16], precision=precise
    )
    section_one = section_one + jnp.einsum(
        "akbl,lp->akpb", blocks[:, :, 1:], column_table[16:], precision=precise
    )
    section_one = section_one.reshape(win_rows + 1, 16, 2, 32, win_cols)
    paired = jnp.stack([section_one[:-1], section_one[1:]], axis=1).reshape(
        win_rows, 64, 32, win_cols
    )
    return jnp.einsum("tm,amvb->atvb", row_table, paired, precision=precise)


def weigh(coefficients, window_weight, freq_weight):
    doubled = jnp.concatenate([freq_weight, freq_weight], axis=0)
    return coefficients * doubled[None, :, :, None] * window_weight[:, None, None, :]


def synthesize(coefficients, column_table, row_table):
    win_rows = coefficients.shape[0]
    win_cols = coefficients.shape[3]
    spread = jnp.einsum("tm,atvb->amvb", row_table, coefficients, precision=precise)
    spread = spread.reshape(win_rows, 2, 16, 64, win_cols)
    stacked = jnp.pad(spread[:, 0], ((0, 1), (0, 0), (0, 0), (0, 0))) + jnp.pad(
        spread[:, 1], ((1, 0), (0, 0), (0, 0), (0, 0))
    )
    lower_piece = jnp.einsum("akpb,lp->akbl", stacked, column_table[:16], precision=precise)
    upper_piece = jnp.einsum("akpb,lp->akbl", stacked, column_table[16:], precision=precise)
    blocks = jnp.pad(lower_piece, ((0, 0), (0, 0), (0, 1), (0, 0))) + jnp.pad(
        upper_piece, ((0, 0), (0, 0), (1, 0), (0, 0))
    )
    return blocks.reshape(16 * (win_rows + 1), 16 * (win_cols + 1))


LANES = 128
UPDATE_ROWS = 32
TILE_GROUP = 17
WINDOWS_PER_TILE = LANES // 16
HALF = WINDOWS_PER_TILE * 32


def numpy_tables():
    positions = np.arange(32, dtype=np.float32)
    window = np.exp(np.float32(-0.5) * ((positions - np.float32(15.5)) / np.float32(8.0)) ** 2)
    phases = np.float32(2.0 * np.pi) * np.outer(positions, positions) / np.float32(32.0)
    scale = np.sqrt(np.float32(32.0))
    cos_part = np.cos(phases) * window[None, :] / scale
    sin_part = -np.sin(phases) * window[None, :] / scale
    return cos_part.astype(np.float32), sin_part.astype(np.float32)


def transform_tables(win_rows):
    cos_part, sin_part = numpy_tables()
    column_table = np.stack([cos_part.T, sin_part.T], axis=1)
    columns = np.zeros((2 * WINDOWS_PER_TILE, 16, 2, WINDOWS_PER_TILE, 32), np.float32)
    for k in range(WINDOWS_PER_TILE):
        columns[k, :, :, k] = column_table[:16]
        columns[k + 1, :, :, k] = column_table[16:]
    columns = columns.reshape(2 * LANES, 2 * HALF)
    blocks = win_rows + 1
    real = np.zeros((win_rows, 32, blocks * 16), np.float32)
    imag = np.zeros((win_rows, 32, blocks * 16), np.float32)
    for a in range(win_rows):
        real[a, :, 16 * a : 16 * a + 32] = cos_part
        imag[a, :, 16 * a : 16 * a + 32] = sin_part
    real = real.reshape(win_rows * 32, blocks * 16)
    imag = imag.reshape(win_rows * 32, blocks * 16)
    forward = np.concatenate([real, imag], axis=1)
    backward = np.concatenate([real.T, imag.T], axis=1)
    return [columns, forward, backward]


def split_constant(table):
    high = table.astype(jnp.bfloat16)
    low = (table - high.astype(np.float32)).astype(jnp.bfloat16)
    return [jnp.asarray(high), jnp.asarray(low)]


def split_value(value):
    high = value.astype(jnp.bfloat16)
    return high, (value - high.astype(jnp.float32)).astype(jnp.bfloat16)


def three_pass_dot(a, b):
    total = jnp.dot(a[0], b[1], preferred_element_type=jnp.float32)
    total += jnp.dot(a[1], b[0], preferred_element_type=jnp.float32)
    return total + jnp.dot(a[0], b[0], preferred_element_type=jnp.float32)


def transposed_dot(a, b):
    def one(x, y):
        return lax.dot_general(
            x, y, (((1,), (1,)), ((), ())), preferred_element_type=jnp.float32
        )
    return one(a[0], b[1]) + one(a[1], b[0]) + one(a[0], b[0])


def constant_first_dot(a, b):
    rows = a[0].shape[0]
    both = jnp.dot(
        jnp.concatenate([a[0], a[1]], axis=0), b[0], preferred_element_type=jnp.float32
    )
    total = jnp.dot(a[0], b[1], preferred_element_type=jnp.float32)
    total += both[rows:]
    return total + both[:rows]


def transform_kernel(
    above_ref, middle_ref, below_ref, mh_ref, ml_ref, fh_ref, fl_ref, gh_ref, gl_ref, fw_ref,
    ww_ref, out_ref, y_ref, e_ref,
):
    x = jnp.concatenate([above_ref[:16], middle_ref[...], below_ref[...]], axis=0)
    rows = x.shape[0]
    win_rows = rows // 16 - 1
    tiles = (x.shape[1] - LANES) // LANES
    stacked_x = jnp.concatenate(
        [x[:, t * LANES : (t + 2) * LANES] for t in range(tiles)], axis=0
    )
    y_ref[...] = three_pass_dot(split_value(stacked_x), (mh_ref[...], ml_ref[...]))
    forward = (fh_ref[...], fl_ref[...])
    backward = (gh_ref[...], gl_ref[...])
    freq = fw_ref[...]

    def turn(value, sign):
        blocks = []
        for g in range(value.shape[1] // (2 * HALF)):
            re = value[:, 2 * HALF * g : 2 * HALF * g + HALF]
            im = value[:, 2 * HALF * g + HALF : 2 * HALF * (g + 1)]
            blocks += [-im, re] if sign else [im, -re]
        return jnp.concatenate(blocks, axis=1)

    for first in range(0, tiles, TILE_GROUP):
        group = range(first, min(first + TILE_GROUP, tiles))
        y = jnp.concatenate([y_ref[t * rows : (t + 1) * rows, :] for t in group], axis=1)
        weights = ww_ref[:, first * 2 * HALF : (group[-1] + 1) * 2 * HALF]
        z = constant_first_dot(forward, split_value(jnp.concatenate([y, turn(y, True)], axis=0)))
        spread = jnp.concatenate(
            [jnp.broadcast_to(weights[a : a + 1], (32, weights.shape[1])) for a in range(win_rows)],
            axis=0,
        )
        z = z * jnp.concatenate([freq] * len(group), axis=1) * spread
        e = constant_first_dot(backward, split_value(jnp.concatenate([z, turn(z, False)], axis=0)))
        for g, t in enumerate(group):
            e_ref[t * rows : (t + 1) * rows, :] = e[:, 2 * HALF * g : 2 * HALF * (g + 1)]
    pieces = transposed_dot(split_value(e_ref[...]), (mh_ref[...], ml_ref[...]))
    kept = out_ref.shape[0]
    out_ref[...] = jnp.zeros_like(out_ref)
    for t in range(tiles):
        out_ref[:, t * LANES : (t + 2) * LANES] += pieces[t * rows + 16 : t * rows + 16 + kept]


def padded_width(cols):
    windows = (cols - 16) // 16
    return (-(-windows // WINDOWS_PER_TILE) + 1) * LANES


def analyze_weigh_synthesize(above, middle, below, window_weight, freq_weight, cols):
    rows = middle.shape[0] + 32
    windows = (cols - 16) // 16
    tiles = -(-windows // WINDOWS_PER_TILE)
    wide = (tiles + 1) * LANES
    window_weight = jnp.pad(window_weight, ((0, 0), (0, tiles * WINDOWS_PER_TILE - windows)))
    win_rows = rows // 16 - 1
    constants = []
    for table in transform_tables(win_rows):
        constants += split_constant(table)
    freq = jnp.broadcast_to(
        freq_weight.reshape(1, 32, 1, 1, 32), (win_rows, 32, 2, WINDOWS_PER_TILE, 32)
    ).reshape(win_rows * 32, 2 * HALF)
    weights = jnp.broadcast_to(
        window_weight.reshape(win_rows, tiles, 1, WINDOWS_PER_TILE, 1),
        (win_rows, tiles, 2, WINDOWS_PER_TILE, 32),
    ).reshape(win_rows, tiles * 2 * HALF)
    vmem = pl.BlockSpec(memory_space=pltpu.VMEM)
    out = pl.pallas_call(
        transform_kernel,
        out_shape=jax.ShapeDtypeStruct((rows - 32, wide), jnp.float32),
        in_specs=[vmem] * 11,
        out_specs=vmem,
        scratch_shapes=[
            pltpu.VMEM((tiles * rows, 2 * HALF), jnp.float32),
            pltpu.VMEM((tiles * rows, 2 * HALF), jnp.float32),
        ],
    )(above, middle, below, *constants, freq, weights)
    return out[:, :cols]


def update_kernel(sums_ref, iterate_ref, residual_ref, direction_ref, applied_ref,
                  iterate_out, residual_out, direction_out):
    sums = sums_ref[...]
    norm_now, curvature, cross_term, image_norm = (sums[:, i : i + 1] for i in range(4))
    step_length = norm_now / curvature
    norm_next = norm_now - 2.0 * step_length * cross_term + step_length * step_length * image_norm
    ratio = norm_next / norm_now
    direction = direction_ref[...]
    iterate_out[...] = iterate_ref[...] + step_length * direction
    new_residual = residual_ref[...] - step_length * applied_ref[...]
    residual_out[...] = new_residual
    direction_out[...] = new_residual + ratio * direction


def updated(sums, iterate, residual, direction, applied):
    height, breadth = iterate.shape
    rows = UPDATE_ROWS
    block = pl.BlockSpec((rows, breadth), lambda i: (i, 0))
    shape = jax.ShapeDtypeStruct(iterate.shape, jnp.float32)
    return pl.pallas_call(
        update_kernel,
        grid=(height // rows,),
        out_shape=(shape, shape, shape),
        in_specs=[pl.BlockSpec((1, 4), lambda i: (0, 0))] + [block] * 4,
        out_specs=(block, block, block),
    )(sums, iterate, residual, direction, applied)


def per_device(iterate, residual, direction, window_weight, freq_weight):
    height, breadth = direction.shape
    rim_weight = jnp.pad(window_weight[:, -1:], ((0, 0), (0, 15)))
    from_left = passed_along(
        jnp.concatenate([direction[:, -16:], rim_weight], axis=0), COL, 1
    )
    from_right = passed_along(direction[:, :16], COL, -1)
    cols = breadth + 32
    wide = padded_width(cols)
    widened = jnp.concatenate(
        [from_left[:height], direction, from_right, jnp.zeros((height, wide - cols), jnp.float32)],
        axis=1,
    )
    weights_wide = jnp.concatenate([from_left[height:, :1], window_weight], axis=1)
    top_weight = jnp.pad(weights_wide[-1:], ((0, 0), (0, widened.shape[1] - weights_wide.shape[1])))
    from_above = passed_along(
        jnp.concatenate([widened[-16:], top_weight], axis=0), "row", 1
    )
    from_below = passed_along(widened[:16], "row", -1)
    weights_all = jnp.concatenate(
        [from_above[16:, : weights_wide.shape[1]], weights_wide], axis=0
    )
    spread = analyze_weigh_synthesize(
        from_above, widened, from_below, weights_all, freq_weight, cols
    )
    synthesized = spread[:, 16 : 16 + breadth]
    applied = synthesized + damping * direction
    products = jnp.stack(
        [residual * residual, direction * applied, residual * applied, applied * applied]
    )
    sums = summed_everywhere(jnp.sum(products, axis=(1, 2)), DOUBLING)
    return updated(sums.reshape(1, 4), iterate, residual, direction, applied)


def solution(mesh):
    finer = Mesh(
        mesh.devices.reshape(mesh.shape["row"], 4, 4, 2, 2),
        ("row", "col_0", "col_1", "col_2", "col_3"),
    )
    return jax.shard_map(
        per_device,
        mesh=finer,
        in_specs=(P("row", COL), P("row", COL), P("row", COL), P("row", COL), P()),
        out_specs=(P("row", COL), P("row", COL), P("row", COL)),
        check_vma=False,
    )
```

```python
import jax
import numpy as np
import jax.numpy as jnp
from jax import lax
from jax.sharding import Mesh
from jax.sharding import PartitionSpec as P
from jax.experimental import pallas as pl
from jax.experimental.pallas import tpu as pltpu

COL = ("col_0", "col_1", "col_2", "col_3")
DOUBLING = (
    ("col_3", 1),
    ("col_2", 1),
    ("row", 1),
    ("row", 2),
    ("col_0", 1),
    ("col_0", 2),
    ("col_1", 1),
    ("col_1", 2),
)


precise = lax.Precision.HIGHEST
damping = 0.5


def passed_along(value, axis, steps):
    count = lax.axis_size(axis)
    leading, last = (max(0, -steps), min(count, count - steps))
    return lax.ppermute(value, axis, [(source, source + steps) for source in range(leading, last)])


def passed_diagonally(value, steps):
    rows, cols = lax.axis_size("row"), lax.axis_size(COL)
    pairs = [
        (r * cols + c, (r + steps) * cols + (c + steps))
        for r in range(max(0, -steps), min(rows, rows - steps))
        for c in range(max(0, -steps), min(cols, cols - steps))
    ]
    return lax.ppermute(value, ("row",) + COL, pairs)


def summed_everywhere(x, steps):
    for axis, mask in steps:
        count = lax.axis_size(axis)
        x = x + lax.ppermute(x, axis, [(i, i ^ mask) for i in range(count)])
    return x


def tables():
    positions = jnp.arange(32, dtype=jnp.float32)
    window = jnp.exp(-0.5 * ((positions - 15.5) / 8.0) ** 2)
    phases = 2.0 * jnp.pi * jnp.outer(positions, positions) / 32.0
    cos_part = jnp.cos(phases) * window[None, :] / jnp.sqrt(32.0)
    sin_part = -jnp.sin(phases) * window[None, :] / jnp.sqrt(32.0)
    column_table = jnp.concatenate([cos_part.T, sin_part.T], axis=1)
    cos_split = cos_part.reshape(32, 2, 16)
    sin_split = sin_part.reshape(32, 2, 16)
    upper = jnp.stack([cos_split, -sin_split], axis=-1)
    lower = jnp.stack([sin_split, cos_split], axis=-1)
    row_table = jnp.concatenate([upper, lower], axis=0).reshape(64, 64)
    return (column_table, row_table)


def analyze(region, column_table, row_table):
    win_rows = region.shape[0] // 16 - 1
    win_cols = region.shape[1] // 16 - 1
    blocks = region.reshape(win_rows + 1, 16, win_cols + 1, 16)
    section_one = jnp.einsum(
        "akbl,lp->akpb", blocks[:, :, :win_cols], column_table[:16], precision=precise
    )
    section_one = section_one + jnp.einsum(
        "akbl,lp->akpb", blocks[:, :, 1:], column_table[16:], precision=precise
    )
    section_one = section_one.reshape(win_rows + 1, 16, 2, 32, win_cols)
    paired = jnp.stack([section_one[:-1], section_one[1:]], axis=1).reshape(
        win_rows, 64, 32, win_cols
    )
    return jnp.einsum("tm,amvb->atvb", row_table, paired, precision=precise)


def weigh(coefficients, window_weight, freq_weight):
    doubled = jnp.concatenate([freq_weight, freq_weight], axis=0)
    return coefficients * doubled[None, :, :, None] * window_weight[:, None, None, :]


def synthesize(coefficients, column_table, row_table):
    win_rows = coefficients.shape[0]
    win_cols = coefficients.shape[3]
    spread = jnp.einsum("tm,atvb->amvb", row_table, coefficients, precision=precise)
    spread = spread.reshape(win_rows, 2, 16, 64, win_cols)
    stacked = jnp.pad(spread[:, 0], ((0, 1), (0, 0), (0, 0), (0, 0))) + jnp.pad(
        spread[:, 1], ((1, 0), (0, 0), (0, 0), (0, 0))
    )
    lower_piece = jnp.einsum("akpb,lp->akbl", stacked, column_table[:16], precision=precise)
    upper_piece = jnp.einsum("akpb,lp->akbl", stacked, column_table[16:], precision=precise)
    blocks = jnp.pad(lower_piece, ((0, 0), (0, 0), (0, 1), (0, 0))) + jnp.pad(
        upper_piece, ((0, 0), (0, 0), (1, 0), (0, 0))
    )
    return blocks.reshape(16 * (win_rows + 1), 16 * (win_cols + 1))


LANES = 128
UPDATE_ROWS = 32
TILE_GROUP = 17
WINDOWS_PER_TILE = LANES // 16
HALF = WINDOWS_PER_TILE * 32


def numpy_tables():
    positions = np.arange(32, dtype=np.float32)
    window = np.exp(np.float32(-0.5) * ((positions - np.float32(15.5)) / np.float32(8.0)) ** 2)
    phases = np.float32(2.0 * np.pi) * np.outer(positions, positions) / np.float32(32.0)
    scale = np.sqrt(np.float32(32.0))
    cos_part = np.cos(phases) * window[None, :] / scale
    sin_part = -np.sin(phases) * window[None, :] / scale
    return cos_part.astype(np.float32), sin_part.astype(np.float32)


def transform_tables(win_rows):
    cos_part, sin_part = numpy_tables()
    column_table = np.stack([cos_part.T, sin_part.T], axis=1)
    columns = np.zeros((2 * WINDOWS_PER_TILE, 16, 2, WINDOWS_PER_TILE, 32), np.float32)
    for k in range(WINDOWS_PER_TILE):
        columns[k, :, :, k] = column_table[:16]
        columns[k + 1, :, :, k] = column_table[16:]
    columns = columns.reshape(2 * LANES, 2 * HALF)
    blocks = win_rows + 1
    real = np.zeros((win_rows, 32, blocks * 16), np.float32)
    imag = np.zeros((win_rows, 32, blocks * 16), np.float32)
    for a in range(win_rows):
        real[a, :, 16 * a : 16 * a + 32] = cos_part
        imag[a, :, 16 * a : 16 * a + 32] = sin_part
    real = real.reshape(win_rows * 32, blocks * 16)
    imag = imag.reshape(win_rows * 32, blocks * 16)
    forward = np.concatenate([real, imag], axis=1)
    backward = np.concatenate([real.T, imag.T], axis=1)
    return [columns, forward, backward]


def split_constant(table, stacked=False):
    high = table.astype(jnp.bfloat16)
    low = (table - high.astype(np.float32)).astype(jnp.bfloat16)
    parts = [high, low] + ([np.concatenate([high, low], axis=0)] if stacked else [])
    return [jnp.asarray(part) for part in parts]


def split_value(value):
    high = value.astype(jnp.bfloat16)
    return high, (value - high.astype(jnp.float32)).astype(jnp.bfloat16)


def three_pass_dot(a, b):
    total = jnp.dot(a[0], b[1], preferred_element_type=jnp.float32)
    total += jnp.dot(a[1], b[0], preferred_element_type=jnp.float32)
    return total + jnp.dot(a[0], b[0], preferred_element_type=jnp.float32)


def transposed_dot(a, b):
    def one(x, y):
        return lax.dot_general(
            x, y, (((1,), (1,)), ((), ())), preferred_element_type=jnp.float32
        )
    return one(a[0], b[1]) + one(a[1], b[0]) + one(a[0], b[0])


def constant_first_dot(a, b):
    rows = a[0].shape[0]
    both = jnp.dot(a[2], b[0], preferred_element_type=jnp.float32)
    total = jnp.dot(a[0], b[1], preferred_element_type=jnp.float32)
    total += both[rows:]
    return total + both[:rows]


def transform_kernel(
    above_ref, middle_ref, below_ref, mh_ref, ml_ref, fh_ref, fl_ref, fs_ref, gh_ref, gl_ref, gs_ref, fw_ref,
    ww_ref, out_ref, y_ref, e_ref,
):
    x = jnp.concatenate([above_ref[:16], middle_ref[...], below_ref[...]], axis=0)
    rows = x.shape[0]
    win_rows = rows // 16 - 1
    tiles = (x.shape[1] - LANES) // LANES
    stacked_x = jnp.concatenate(
        [x[:, t * LANES : (t + 2) * LANES] for t in range(tiles)], axis=0
    )
    y_ref[...] = three_pass_dot(split_value(stacked_x), (mh_ref[...], ml_ref[...]))
    forward = (fh_ref[...], fl_ref[...], fs_ref[...])
    backward = (gh_ref[...], gl_ref[...], gs_ref[...])
    freq = fw_ref[...]

    def turn(value, sign):
        blocks = []
        for g in range(value.shape[1] // (2 * HALF)):
            re = value[:, 2 * HALF * g : 2 * HALF * g + HALF]
            im = value[:, 2 * HALF * g + HALF : 2 * HALF * (g + 1)]
            blocks += [-im, re] if sign else [im, -re]
        return jnp.concatenate(blocks, axis=1)

    for first in range(0, tiles, TILE_GROUP):
        group = range(first, min(first + TILE_GROUP, tiles))
        y = jnp.concatenate([y_ref[t * rows : (t + 1) * rows, :] for t in group], axis=1)
        weights = ww_ref[:, first * 2 * HALF : (group[-1] + 1) * 2 * HALF]
        z = constant_first_dot(forward, split_value(jnp.concatenate([y, turn(y, True)], axis=0)))
        spread = jnp.concatenate(
            [jnp.broadcast_to(weights[a : a + 1], (32, weights.shape[1])) for a in range(win_rows)],
            axis=0,
        )
        z = z * jnp.concatenate([freq] * len(group), axis=1) * spread
        e = constant_first_dot(backward, split_value(jnp.concatenate([z, turn(z, False)], axis=0)))
        for g, t in enumerate(group):
            e_ref[t * rows : (t + 1) * rows, :] = e[:, 2 * HALF * g : 2 * HALF * (g + 1)]
    pieces = transposed_dot(split_value(e_ref[...]), (mh_ref[...], ml_ref[...]))
    kept = out_ref.shape[0]
    out_ref[...] = jnp.zeros_like(out_ref)
    for t in range(tiles):
        out_ref[:, t * LANES : (t + 2) * LANES] += pieces[t * rows + 16 : t * rows + 16 + kept]


def padded_width(cols):
    windows = (cols - 16) // 16
    return (-(-windows // WINDOWS_PER_TILE) + 1) * LANES


def analyze_weigh_synthesize(above, middle, below, window_weight, freq_weight, cols):
    rows = middle.shape[0] + 32
    windows = (cols - 16) // 16
    tiles = -(-windows // WINDOWS_PER_TILE)
    wide = (tiles + 1) * LANES
    window_weight = jnp.pad(window_weight, ((0, 0), (0, tiles * WINDOWS_PER_TILE - windows)))
    win_rows = rows // 16 - 1
    constants = []
    for i, table in enumerate(transform_tables(win_rows)):
        constants += split_constant(table, stacked=i > 0)
    freq = jnp.broadcast_to(
        freq_weight.reshape(1, 32, 1, 1, 32), (win_rows, 32, 2, WINDOWS_PER_TILE, 32)
    ).reshape(win_rows * 32, 2 * HALF)
    weights = jnp.broadcast_to(
        window_weight.reshape(win_rows, tiles, 1, WINDOWS_PER_TILE, 1),
        (win_rows, tiles, 2, WINDOWS_PER_TILE, 32),
    ).reshape(win_rows, tiles * 2 * HALF)
    vmem = pl.BlockSpec(memory_space=pltpu.VMEM)
    out = pl.pallas_call(
        transform_kernel,
        out_shape=jax.ShapeDtypeStruct((rows - 32, wide), jnp.float32),
        in_specs=[vmem] * 13,
        out_specs=vmem,
        scratch_shapes=[
            pltpu.VMEM((tiles * rows, 2 * HALF), jnp.float32),
            pltpu.VMEM((tiles * rows, 2 * HALF), jnp.float32),
        ],
    )(above, middle, below, *constants, freq, weights)
    return out[:, :cols]


def update_kernel(sums_ref, iterate_ref, residual_ref, direction_ref, applied_ref,
                  iterate_out, residual_out, direction_out):
    sums = sums_ref[...]
    norm_now, curvature, cross_term, image_norm = (sums[:, i : i + 1] for i in range(4))
    step_length = norm_now / curvature
    norm_next = norm_now - 2.0 * step_length * cross_term + step_length * step_length * image_norm
    ratio = norm_next / norm_now
    direction = direction_ref[...]
    iterate_out[...] = iterate_ref[...] + step_length * direction
    new_residual = residual_ref[...] - step_length * applied_ref[...]
    residual_out[...] = new_residual
    direction_out[...] = new_residual + ratio * direction


def updated(sums, iterate, residual, direction, applied):
    height, breadth = iterate.shape
    rows = UPDATE_ROWS
    block = pl.BlockSpec((rows, breadth), lambda i: (i, 0))
    shape = jax.ShapeDtypeStruct(iterate.shape, jnp.float32)
    return pl.pallas_call(
        update_kernel,
        grid=(height // rows,),
        out_shape=(shape, shape, shape),
        in_specs=[pl.BlockSpec((1, 4), lambda i: (0, 0))] + [block] * 4,
        out_specs=(block, block, block),
    )(sums, iterate, residual, direction, applied)


def per_device(iterate, residual, direction, window_weight, freq_weight):
    height, breadth = direction.shape
    rim_weight = jnp.pad(window_weight[:, -1:], ((0, 0), (0, 15)))
    from_left = passed_along(
        jnp.concatenate([direction[:, -16:], rim_weight], axis=0), COL, 1
    )
    from_right = passed_along(direction[:, :16], COL, -1)
    cols = breadth + 32
    wide = padded_width(cols)
    widened = jnp.concatenate(
        [from_left[:height], direction, from_right, jnp.zeros((height, wide - cols), jnp.float32)],
        axis=1,
    )
    weights_wide = jnp.concatenate([from_left[height:, :1], window_weight], axis=1)
    top_weight = jnp.pad(weights_wide[-1:], ((0, 0), (0, widened.shape[1] - weights_wide.shape[1])))
    from_above = passed_along(
        jnp.concatenate([widened[-16:], top_weight], axis=0), "row", 1
    )
    from_below = passed_along(widened[:16], "row", -1)
    weights_all = jnp.concatenate(
        [from_above[16:, : weights_wide.shape[1]], weights_wide], axis=0
    )
    spread = analyze_weigh_synthesize(
        from_above, widened, from_below, weights_all, freq_weight, cols
    )
    synthesized = spread[:, 16 : 16 + breadth]
    applied = synthesized + damping * direction
    products = jnp.stack(
        [residual * residual, direction * applied, residual * applied, applied * applied]
    )
    sums = summed_everywhere(jnp.sum(products, axis=(1, 2)), DOUBLING)
    return updated(sums.reshape(1, 4), iterate, residual, direction, applied)


def solution(mesh):
    finer = Mesh(
        mesh.devices.reshape(mesh.shape["row"], 4, 4, 2, 2),
        ("row", "col_0", "col_1", "col_2", "col_3"),
    )
    return jax.shard_map(
        per_device,
        mesh=finer,
        in_specs=(P("row", COL), P("row", COL), P("row", COL), P("row", COL), P()),
        out_specs=(P("row", COL), P("row", COL), P("row", COL)),
        check_vma=False,
    )
```
